32 devices in a mesh: req: 8 (over y, x, core), exp: 4 (over z).
Axes of the slice: x: 2, y: 2, z: 4, core: 2. Of those that a mesh axis runs over, the one named last changes fastest.
Arguments:
- tokens: bfloat16 [4096, 1024], P(('req', 'exp'))
- norm_attn: bfloat16 [1024], replicated, may hold values from 0.099609375 to 1.8984375
- w_query: bfloat16 [1024, 1024], replicated
- w_key: bfloat16 [1024, 512], replicated
- w_value: bfloat16 [1024, 512], replicated, may hold values from -0.1875 to 0.1875
- w_out: bfloat16 [1024, 1024], P('exp'), may hold values from -0.1875 to 0.1875
- norm_moe: bfloat16 [1024], replicated, may hold values from 0.099609375 to 1.8984375
- w_router: bfloat16 [1024, 32], replicated
- w_gate: bfloat16 [32, 1024, 512], P('exp'), may hold values from -0.1875 to 0.1875
- w_up: bfloat16 [32, 1024, 512], P('exp'), may hold values from -0.1875 to 0.1875
- w_down: bfloat16 [32, 512, 1024], P('exp')
- segment_ids: int32 [8, 512], P('req'), may hold values from 0 to 3, never falling along the last dimension, each value on 1 to 256 neighbouring positions
- page_order: int32 [8, 512], P('req'), may hold values from 0 to 511, each once within a row
- expert_ids: int32 [4096, 8], P(('req', 'exp')), may hold values from 0 to 31, all different within a row; in each aligned block of 128 rows (0 to 127, 128 to 255, ...) at most 64 rows name the same one
Outputs:
- mixed: bfloat16 [4096, 1024], P(('req', 'exp'))
- kv_cache: bfloat16 [4096, 8, 128], P('req', 'exp')
The draws below stay inside these ranges and needn't reach their ends.
Inputs may be any that keep to these rules, and one draw needn't show every extreme that they name: `segment_ids`: along each row, request numbers never fall; every pack holds 4 requests of 1 to 256 positions, one of exactly 256. `page_order`: each row is a permutation of the pack's 512 positions. `expert_ids`: A token's 8 experts differ. Within the rows of one device no expert is named by more than 64 rows, and in some device's rows an expert is named by exactly 64.
All inputs are finite; a program needn't handle non-finite values.
Results may differ from the reference program's by a relative error of at most 0.0055.
Values may be sent and summed in bfloat16 or wider, within the bound.
No kernel may reach another device: no remote copies, remote signals or barrier semaphores. Data moves between devices by JAX's collectives and lax.ppermute only.
A program may use at most 128 MiB of HBM per device.

```python
import math
import jax
import jax.numpy as jnp
import numpy as np
from jax import lax

D = 1024
HEADS = 16
KV = 8
HD = 64
EXPERTS = 32
FF_E = 512
TOP = 8
TOK_DEV = 128
REQS = 4
CAP = 64
PACK = 512
MOST = 256
TOKENS = 4096
N_REQ = 8


def draw_tokens(key, part):
    values = jnp.clip(jax.random.normal(key, (TOKENS, D), jnp.float32), -6.0, 6.0)
    return values.astype(jnp.bfloat16)


def attention_maps(key):
    base_key = jax.random.fold_in(key, 11)
    first, second = jax.random.split(base_key, 2)
    query = jnp.clip(jax.random.normal(first, (D, KV, 2, HD), jnp.float32), -6.0, 6.0) / math.sqrt(D)
    keys = jnp.clip(jax.random.normal(second, (D, KV, HD), jnp.float32), -6.0, 6.0) / math.sqrt(D)
    return (query.reshape(D, HEADS * HD), keys.reshape(D, KV * HD))


def draw_w_query(key, part):
    return attention_maps(key)[0].astype(jnp.bfloat16)


def draw_w_key(key, part):
    return attention_maps(key)[1].astype(jnp.bfloat16)


def draw_w_router(key, part):
    second = jax.random.fold_in(key, 1)
    values = 0.4 * jnp.clip(jax.random.normal(second, (D, EXPERTS), jnp.float32), -6.0, 6.0) / math.sqrt(D)
    return values.astype(jnp.bfloat16)


def draw_w_down(key, part):
    values = 2.8 * jnp.clip(jax.random.normal(key, (EXPERTS, FF_E, D), jnp.float32), -6.0, 6.0) / math.sqrt(FF_E)
    return values.astype(jnp.bfloat16)


def block_levels(key, dims, pieces, smallest, largest):
    level, own = 1.0, jax.random.fold_in(key, 6)
    for position, parts in pieces:
        heights = jnp.exp(jax.random.uniform(jax.random.fold_in(own, position), (parts,), jnp.float32, smallest / len(pieces), largest / len(pieces)))
        level = level * jnp.repeat(heights, dims[position] // parts).reshape([-1 if axis == position else 1 for axis in range(len(dims))])
    return level


def length_profile(count, total, reach, lean):
    loads = [(1 << 20) // math.isqrt(standing ** lean) + 1 for standing in range(2, count + 1)]
    surplus, holding = total - reach - (count - 1), [1] * (count - 1)
    while surplus > 0:
        candidates = [i for i in range(count - 1) if holding[i] < reach]
        whole, left = sum([loads[i] for i in candidates]), surplus
        for i in candidates:
            extra = min(reach - holding[i], max(1, left * loads[i] // whole), surplus)
            holding[i] = holding[i] + extra
            surplus = surplus - extra
    return np.array([reach] + holding)


def uneven(stream_key, number_of, total, limit, skew):
    if number_of == 2:
        one = jax.random.randint(stream_key, (), max(1, total - limit), min(limit, total - 1) + 1)
        return jnp.stack([one, total - one])
    lengths = jnp.asarray(length_profile(number_of, total, limit, skew), jnp.int32)
    pairs = (number_of - 1) // 2
    giver, taker = lengths[1:1 + 2 * pairs:2], lengths[2:2 + 2 * pairs:2]
    room = jnp.minimum(giver - 1, limit - taker)
    shifted = jax.random.randint(jax.random.fold_in(stream_key, 1), (pairs,), 0, 1 << 20) % (room + 1)
    lengths = lengths.at[1:1 + 2 * pairs:2].set(giver - shifted).at[2:2 + 2 * pairs:2].set(taker + shifted)
    return lengths[jax.random.permutation(jax.random.fold_in(stream_key, 2), number_of)]


def routed_block(key, own, number, rows, number_of, top, most, slope):
    ranking = jax.random.permutation(key, number_of)
    packed, usual = shares(number_of, rows * top, most, slope, True), shares(number_of, rows * top, most, slope, False)
    places = jnp.arange(number_of)

    def named(tallies, turn):
        used = int((tallies > 0).sum())
        fixed = max(1, used // 4)
        shifted = fixed + (places - fixed + turn * (used - fixed)) % max(1, number_of - fixed)
        return jnp.zeros((number_of,), jnp.int32).at[ranking[jnp.where(places < fixed, places, shifted)]].set(jnp.asarray(tallies, jnp.int32))

    tallies = jnp.where(number % 4 == 0, named(packed, number // 4), named(usual, number - number // 4 - 1))
    mixed = jax.random.permutation(jax.random.fold_in(own, 3), number_of)
    giver, sink = mixed[0:number_of // 2 * 2:2], mixed[1:number_of // 2 * 2:2]
    room = jnp.minimum(tallies[giver] - 1, most - tallies[sink]) // 2
    room = jnp.where((giver == ranking[0]) | (sink == ranking[0]) | (tallies[sink] == 0), 0, jnp.maximum(room, 0))
    shifted = jax.random.randint(jax.random.fold_in(own, 4), (number_of // 2,), 0, 1 << 20) % (room + 1)
    tallies = tallies.at[giver].add(-shifted).at[sink].add(shifted)
    items = jnp.searchsorted(jnp.cumsum(tallies), jnp.arange(rows * top), side="right").astype(jnp.int32)
    grid = items.reshape(top, rows).T
    grid = grid[jax.random.permutation(jax.random.fold_in(own, 1), rows)]
    turn = jax.random.randint(jax.random.fold_in(own, 2), (rows, 1), 0, top)
    return jnp.take_along_axis(grid, (jnp.arange(top)[None, :] + turn) % top, axis=1)


def shares(number_of, total, bound, lean, full):
    loads = [(1 << 20) // math.isqrt(rank ** lean) + 1 for rank in range(1, number_of + 1)]
    largest = bound if full else min(bound, max(-(-total // number_of), total * loads[0] // sum(loads)))
    least = 1 if total - largest >= number_of - 1 else 0
    given, rest = [largest] + [least] * (number_of - 1), total - largest - least * (number_of - 1)
    while rest > 0:
        candidates = [i for i in range(1, number_of) if given[i] < largest] or [i for i in range(1, number_of) if given[i] < bound]
        pool, budget = sum([loads[i] for i in candidates]), rest
        for i in candidates:
            more = min(bound - given[i], max(1, budget * loads[i] // pool), rest)
            given[i] = given[i] + more
            rest = rest - more
    return np.array(given)


def noise(own_key, shape, deviation, most, shards=(), kind=jnp.bfloat16):
    entries = deviation * jax.random.normal(own_key, shape, jnp.float32)
    if shards:
        entries = entries * block_levels(own_key, shape, shards, -0.22, 0.18)
    return jnp.clip(entries, -most, most).astype(kind)


def setup_inputs(seed: int = 0) -> dict:
    key_of = jax.random.split(jax.random.key(seed), 15)
    tokens = draw_tokens(jax.random.fold_in(key_of[14], 71), 0)
    norm_attn = jnp.clip(1.0 + 0.18 * jax.random.normal(key_of[1], (D,), jnp.float32), 0.099609375, 1.8984375).astype(jnp.bfloat16)
    w_query = draw_w_query(jax.random.fold_in(key_of[14], 71), 0)
    w_key = draw_w_key(jax.random.fold_in(key_of[14], 71), 0)
    w_value = noise(key_of[4], (D, KV * HD), D ** -0.5, 0.1875)
    w_out = noise(key_of[5], (HEADS * HD, D), (HEADS * HD) ** -0.5, 0.1875, ((0, 4),))
    norm_moe = jnp.clip(1.0 + 0.18 * jax.random.normal(key_of[6], (D,), jnp.float32), 0.099609375, 1.8984375).astype(jnp.bfloat16)
    w_router = draw_w_router(jax.random.fold_in(key_of[14], 71), 0)
    w_gate = noise(key_of[8], (EXPERTS, D, FF_E), D ** -0.5, 0.1875, ((0, 4),))
    w_up = noise(key_of[9], (EXPERTS, D, FF_E), D ** -0.5, 0.1875, ((0, 4),))
    w_down = draw_w_down(jax.random.fold_in(key_of[14], 71), 0)
    segment_ids = jax.vmap(lambda own: jnp.searchsorted(jnp.cumsum(uneven(own, REQS, PACK, MOST, 2)), jnp.arange(PACK), side="right"))(jax.random.split(key_of[11], N_REQ)).reshape((N_REQ, PACK)).astype(jnp.int32)
    page_order = jax.vmap(lambda own: jax.random.permutation(own, PACK))(jax.random.split(key_of[12], N_REQ)).reshape((N_REQ, PACK)).astype(jnp.int32)
    expert_ids_keys = jax.random.split(jax.random.fold_in(key_of[13], 1), TOKENS // TOK_DEV)
    expert_ids_turns = jax.random.permutation(jax.random.fold_in(key_of[13], 3), TOKENS // TOK_DEV)
    expert_ids = jax.vmap(lambda own, number: routed_block(jax.random.fold_in(key_of[13], 2), own, number, TOK_DEV, EXPERTS, TOP, CAP, 1))(expert_ids_keys, expert_ids_turns).reshape((TOKENS, TOP))
    return {"tokens": tokens, "norm_attn": norm_attn, "w_query": w_query, "w_key": w_key, "w_value": w_value, "w_out": w_out, "norm_moe": norm_moe, "w_router": w_router, "w_gate": w_gate, "w_up": w_up, "w_down": w_down, "segment_ids": segment_ids, "page_order": page_order, "expert_ids": expert_ids}


def rms_scale(rows, gain):
    rows = rows.astype(jnp.float32)
    inverse = lax.rsqrt(lax.optimization_barrier(jnp.mean(rows * rows, axis=-1, keepdims=True)) + 1e-06)
    return (rows * inverse * gain.astype(jnp.float32)).astype(jnp.bfloat16)

def positions(seg):
    index = jnp.arange(seg.shape[0], dtype=jnp.int32)
    starts = jnp.concatenate([jnp.ones((1,), dtype=bool), seg[1:] != seg[:-1]])
    first = lax.cummax(jnp.where(starts, index, 0).astype(jnp.int32), axis=0)
    return (index - first).astype(jnp.int32)

def rotate(values, pos):
    half = values.shape[-1] // 2
    freq = 10000.0 ** (-jnp.arange(half, dtype=jnp.float32) / half)
    angle = pos.astype(jnp.float32)[:, None] * freq[None, :]
    cosine = jnp.cos(angle)[:, None, :]
    sine = jnp.sin(angle)[:, None, :]
    front = values[..., :half]
    back = values[..., half:]
    return jnp.concatenate([front * cosine - back * sine, back * cosine + front * sine], axis=-1)

def attend(query, keyval, seg):
    plen, groups, width = query.shape
    half = width // 2
    block = min(512, plen)
    blocks = plen // block
    queries = query.astype(jnp.float32).reshape(blocks, block, groups, 2, half)
    keys = keyval[..., :half].astype(jnp.float32)
    values = keyval[..., half:].astype(jnp.float32)
    key_pos = jnp.arange(plen, dtype=jnp.int32)
    query_pos = key_pos.reshape(blocks, block)
    query_seg = seg.reshape(blocks, block)

    def one_block(args):
        qblock, qpos, qseg = args
        score = jnp.einsum('qkgd,tkd->kgqt', qblock, keys) * 0.125
        allowed = (qseg[:, None] == seg[None, :]) & (key_pos[None, :] <= qpos[:, None])
        score = jnp.where(allowed[None, None], score, -1e+30)
        top = lax.optimization_barrier(jnp.max(score, axis=-1, keepdims=True))
        expo = jnp.exp(score - top)
        probs = lax.optimization_barrier((expo / lax.optimization_barrier(jnp.sum(expo, axis=-1, keepdims=True))).astype(jnp.bfloat16))
        out = jnp.einsum('kgqt,tkd->qkgd', probs.astype(jnp.float32), values)
        return out.astype(jnp.bfloat16)
    outs = lax.map(one_block, (queries, query_pos, query_seg))
    return outs.reshape(plen, groups * width)

def reference(tokens, norm_attn, w_query, w_key, w_value, w_out, norm_moe, w_router, w_gate, w_up, w_down, segment_ids, page_order, expert_ids):
    total = tokens.shape[0]
    normed = rms_scale(tokens, norm_attn)
    pos = jax.vmap(positions)(segment_ids).reshape(total)
    query = jnp.dot(normed, w_query, preferred_element_type=jnp.float32).reshape(total, HEADS, HD)
    query = rotate(query, pos).astype(jnp.bfloat16).reshape(total, KV, 2 * HD)
    keys = jnp.dot(normed, w_key, preferred_element_type=jnp.float32).reshape(total, KV, HD)
    keys = rotate(keys, pos).astype(jnp.bfloat16)
    values = jnp.dot(normed, w_value, preferred_element_type=jnp.float32).astype(jnp.bfloat16).reshape(total, KV, HD)
    keyval = jnp.concatenate([keys, values], axis=-1)
    query = lax.optimization_barrier(query)
    keyval = lax.optimization_barrier(keyval)
    packs_q = query.reshape(N_REQ, PACK, KV, 2 * HD)
    packs_kv = keyval.reshape(N_REQ, PACK, KV, 2 * HD)
    heads_out = lax.map(lambda args: attend(args[0], args[1], args[2]), (packs_q, packs_kv, segment_ids))
    heads_out = heads_out.reshape(total, HEADS * HD)
    resid = tokens.astype(jnp.float32) + jnp.dot(heads_out, w_out, preferred_element_type=jnp.float32)
    cache = jax.vmap(lambda rows, order: jnp.zeros_like(rows).at[order].set(rows))(packs_kv, page_order)
    kv_cache = cache.reshape(total, KV, 2 * HD)
    normed2 = rms_scale(resid, norm_moe)
    logits = jnp.dot(normed2, w_router, preferred_element_type=jnp.float32)
    weights = jax.nn.softmax(jnp.take_along_axis(logits, expert_ids, axis=1), axis=-1)
    flat = expert_ids.reshape(-1)
    order = jnp.argsort(flat, stable=True).astype(jnp.int32)
    sizes = lax.optimization_barrier(jnp.sum((flat[:, None] == jnp.arange(EXPERTS, dtype=jnp.int32)[None, :]).astype(jnp.int32), axis=0)).astype(jnp.int32)
    rows = normed2[order // TOP].astype(jnp.float32)
    gate = lax.ragged_dot(rows, w_gate.astype(jnp.float32), sizes)
    up = lax.ragged_dot(rows, w_up.astype(jnp.float32), sizes)
    hidden = lax.optimization_barrier((jax.nn.silu(gate) * up).astype(jnp.bfloat16))
    expert_out = lax.ragged_dot(hidden.astype(jnp.float32), w_down.astype(jnp.float32), sizes)
    expert_out = lax.optimization_barrier(expert_out.astype(jnp.bfloat16))
    placed = jnp.zeros_like(expert_out).at[order].set(expert_out).reshape(total, TOP, D)
    moe = lax.optimization_barrier(jnp.sum(weights[:, :, None] * placed.astype(jnp.float32), axis=1))
    mixed = (resid + moe).astype(jnp.bfloat16)
    return (mixed, kv_cache)
```

```python
import jax
import jax.numpy as jnp
from jax import lax
from jax.sharding import PartitionSpec as P

HD = 64
CAP = 64


def rms_scale(rows, gain):
    rows = rows.astype(jnp.float32)
    inverse = lax.rsqrt(jnp.mean(rows * rows, axis=-1, keepdims=True) + 1e-06)
    return (rows * inverse * gain.astype(jnp.float32)).astype(jnp.bfloat16)


def positions(seg):
    index = jnp.arange(seg.shape[0], dtype=jnp.int32)
    starts = jnp.concatenate([jnp.ones((1,), dtype=bool), seg[1:] != seg[:-1]])
    first = lax.cummax(jnp.where(starts, index, 0), axis=0)
    return index - first


def rotate(values, pos):
    half = values.shape[-1] // 2
    freq = 10000.0 ** (-jnp.arange(half, dtype=jnp.float32) / half)
    angle = pos.astype(jnp.float32)[:, None] * freq[None, :]
    cosine = jnp.cos(angle)[:, None, :]
    sine = jnp.sin(angle)[:, None, :]
    front = values[..., :half]
    back = values[..., half:]
    return jnp.concatenate([front * cosine - back * sine, back * cosine + front * sine], axis=-1)


def attend(query, keyval, seg):
    plen, groups, width = query.shape
    half = width // 2
    block = min(512, plen)
    blocks = plen // block
    queries = query.reshape(blocks, block, groups, 2, half)
    keys = keyval[..., :half]
    values = keyval[..., half:]
    key_pos = jnp.arange(plen, dtype=jnp.int32)
    query_pos = key_pos.reshape(blocks, block)
    query_seg = seg.reshape(blocks, block)

    def one_block(args):
        qblock, qpos, qseg = args
        score = (
            jnp.einsum("qkgd,tkd->kgqt", qblock, keys, preferred_element_type=jnp.float32) * 0.125
        )
        allowed = (qseg[:, None] == seg[None, :]) & (key_pos[None, :] <= qpos[:, None])
        score = jnp.where(allowed[None, None], score, -1e30)
        top = jnp.max(score, axis=-1, keepdims=True)
        expo = jnp.exp(score - top)
        probs = (expo / jnp.sum(expo, axis=-1, keepdims=True)).astype(jnp.bfloat16)
        out = jnp.einsum("kgqt,tkd->qkgd", probs, values, preferred_element_type=jnp.float32)
        return out.astype(jnp.bfloat16)

    outs = lax.map(one_block, (queries, query_pos, query_seg))
    return outs.reshape(plen, groups * width)


def expert_mix(rows_all, ids_all, w_router, w_gate, w_up, w_down):
    tokens_all = rows_all.shape[0]
    local = w_gate.shape[0]
    cap = CAP * lax.axis_size("exp")
    here = lax.axis_index("exp")
    logits = jnp.dot(rows_all, w_router, preferred_element_type=jnp.float32)
    weights = jax.nn.softmax(jnp.take_along_axis(logits, ids_all, axis=1), axis=-1)
    match = (ids_all - here * local)[:, :, None] == jnp.arange(local, dtype=jnp.int32)
    hits = jnp.any(match, axis=1)
    mine = jnp.sum(jnp.where(match, weights[:, :, None], 0.0), axis=1)
    order = jnp.arange(tokens_all, dtype=jnp.int32)
    before = (order[None, :] < order[:, None]).astype(jnp.bfloat16)
    slot = jnp.dot(before, hits.astype(jnp.bfloat16), preferred_element_type=jnp.float32)
    slot = slot.astype(jnp.int32)
    picks = hits.T[:, None, :] & (
        slot.T[:, None, :] == jnp.arange(cap, dtype=jnp.int32)[None, :, None]
    )
    received = jnp.einsum(
        "est,td->esd", picks.astype(jnp.bfloat16), rows_all, preferred_element_type=jnp.float32
    ).astype(jnp.bfloat16)
    gate = jnp.einsum("esd,edf->esf", received, w_gate, preferred_element_type=jnp.float32)
    upward = jnp.einsum("esd,edf->esf", received, w_up, preferred_element_type=jnp.float32)
    hidden = (jax.nn.silu(gate) * upward).astype(jnp.bfloat16)
    result = jnp.einsum("esf,efd->esd", hidden, w_down, preferred_element_type=jnp.float32)
    result = result.astype(jnp.bfloat16)
    combine = jnp.where(picks, mine.T[:, None, :], 0.0)
    high = combine.astype(jnp.bfloat16)
    low = (combine - high.astype(jnp.float32)).astype(jnp.bfloat16)
    partial = jnp.einsum("est,esd->td", high, result, preferred_element_type=jnp.float32)
    partial = partial + jnp.einsum("est,esd->td", low, result, preferred_element_type=jnp.float32)
    return partial


def shards(
    tokens,
    norm_attn,
    w_query,
    w_key,
    w_value,
    w_out,
    norm_moe,
    w_router,
    w_gate,
    w_up,
    w_down,
    segment_ids,
    page_order,
    expert_ids,
):
    rows, width = tokens.shape
    seg = segment_ids[0]
    groups = w_key.shape[1] // HD
    here = lax.axis_index("exp")
    ids_all = lax.all_gather(expert_ids, "exp", axis=0, tiled=True)
    pos = lax.dynamic_slice_in_dim(positions(seg), here * rows, rows)
    normed = rms_scale(tokens, norm_attn)
    query = jnp.dot(normed, w_query, preferred_element_type=jnp.float32).reshape(
        rows, 2 * groups, HD
    )
    query = rotate(query, pos).astype(jnp.bfloat16).reshape(rows, groups, 2 * HD)
    keys = jnp.dot(normed, w_key, preferred_element_type=jnp.float32).reshape(rows, groups, HD)
    keys = rotate(keys, pos).astype(jnp.bfloat16)
    values = (
        jnp.dot(normed, w_value, preferred_element_type=jnp.float32)
        .astype(jnp.bfloat16)
        .reshape(rows, groups, HD)
    )
    keyval = jnp.concatenate([keys, values], axis=-1)
    query_heads, keyval_heads = (
        lax.all_to_all(query, "exp", split_axis=1, concat_axis=0, tiled=True),
        lax.all_to_all(keyval, "exp", split_axis=1, concat_axis=0, tiled=True),
    )
    kv_cache = jnp.zeros_like(keyval_heads).at[page_order[0]].set(keyval_heads)
    heads_out = attend(query_heads, keyval_heads, seg)
    attention = lax.psum_scatter(
        jnp.dot(heads_out, w_out, preferred_element_type=jnp.float32),
        "exp",
        scatter_dimension=0,
        tiled=True,
    )
    resid = tokens.astype(jnp.float32) + attention
    normed2 = rms_scale(resid, norm_moe)
    rows_all = lax.all_gather(normed2, "exp", axis=0, tiled=True)
    partial = expert_mix(rows_all, ids_all, w_router, w_gate, w_up, w_down)
    moe = lax.psum_scatter(partial, "exp", scatter_dimension=0, tiled=True)
    mixed = (resid + moe).astype(jnp.bfloat16)
    return (mixed, kv_cache)


def solution(mesh):
    placed = (
        P(("req", "exp"), None),
        P(),
        P(),
        P(),
        P(),
        P("exp", None),
        P(),
        P(),
        P("exp", None, None),
        P("exp", None, None),
        P("exp", None, None),
        P("req", None),
        P("req", None),
        P(("req", "exp"), None),
    )
    return jax.shard_map(
        shards,
        mesh=mesh,
        in_specs=placed,
        out_specs=(P(("req", "exp"), None), P("req", "exp", None)),
        check_vma=False,
    )
```

```python
import jax
import jax.numpy as jnp
from jax import lax
from jax.sharding import PartitionSpec as P

HD = 64
CAP = 64


def rms_scale(rows, gain):
    rows = rows.astype(jnp.float32)
    inverse = lax.rsqrt(jnp.mean(rows * rows, axis=-1, keepdims=True) + 1e-06)
    return (rows * inverse * gain.astype(jnp.float32)).astype(jnp.bfloat16)


def positions(seg):
    index = jnp.arange(seg.shape[0], dtype=jnp.int32)
    starts = jnp.concatenate([jnp.ones((1,), dtype=bool), seg[1:] != seg[:-1]])
    first = lax.cummax(jnp.where(starts, index, 0), axis=0)
    return index - first


def rotate(values, pos):
    half = values.shape[-1] // 2
    freq = 10000.0 ** (-jnp.arange(half, dtype=jnp.float32) / half)
    angle = pos.astype(jnp.float32)[:, None] * freq[None, :]
    cosine = jnp.cos(angle)[:, None, :]
    sine = jnp.sin(angle)[:, None, :]
    front = values[..., :half]
    back = values[..., half:]
    return jnp.concatenate([front * cosine - back * sine, back * cosine + front * sine], axis=-1)


def attend(query, keyval, seg):
    plen, groups, width = query.shape
    half = width // 2
    block = min(512, plen)
    blocks = plen // block
    queries = query.reshape(blocks, block, groups, 2, half)
    keys = keyval[..., :half]
    values = keyval[..., half:]
    key_pos = jnp.arange(plen, dtype=jnp.int32)
    query_pos = key_pos.reshape(blocks, block)
    query_seg = seg.reshape(blocks, block)

    def one_block(args):
        qblock, qpos, qseg = args
        score = (
            jnp.einsum("qkgd,tkd->kgqt", qblock, keys, preferred_element_type=jnp.float32) * 0.125
        )
        allowed = (qseg[:, None] == seg[None, :]) & (key_pos[None, :] <= qpos[:, None])
        score = jnp.where(allowed[None, None], score, -1e30)
        top = jnp.max(score, axis=-1, keepdims=True)
        expo = jnp.exp(score - top)
        probs = (expo / jnp.sum(expo, axis=-1, keepdims=True)).astype(jnp.bfloat16)
        out = jnp.einsum("kgqt,tkd->qkgd", probs, values, preferred_element_type=jnp.float32)
        return out.astype(jnp.bfloat16)

    outs = lax.map(one_block, (queries, query_pos, query_seg))
    return outs.reshape(plen, groups * width)


def routing(normed2, ids, w_router):
    experts = w_router.shape[1]
    logits = jnp.dot(normed2, w_router, preferred_element_type=jnp.float32)
    match = ids[:, :, None] == jnp.arange(experts, dtype=jnp.int32)
    chosen = jnp.sum(jnp.where(match, logits[:, None, :], 0.0), axis=2)
    weights = jax.nn.softmax(chosen, axis=-1)
    dense = jnp.sum(jnp.where(match, weights[:, :, None], 0.0), axis=1)
    high = dense.astype(jnp.bfloat16)
    low = (dense - high.astype(jnp.float32)).astype(jnp.bfloat16)
    named = jnp.any(match, axis=1).astype(jnp.bfloat16)
    pad = (-3 * experts) % 128
    fill = jnp.zeros((normed2.shape[0], pad), jnp.bfloat16)
    return jnp.concatenate([normed2, high, low, named, fill], axis=1)


def expert_mix(packed, width, experts, w_gate, w_up, w_down):
    tokens_all = packed.shape[0]
    local = w_gate.shape[0]
    cap = CAP * lax.axis_size("exp")
    here = lax.axis_index("exp")
    rows_all = packed[:, :width]

    def columns(block):
        return lax.dynamic_slice_in_dim(packed, width + block * experts + here * local, local, 1)

    high, low, named = columns(0), columns(1), columns(2)
    hits = named > 0
    order = jnp.arange(tokens_all, dtype=jnp.int32)
    before = (order[None, :] < order[:, None]).astype(jnp.bfloat16)
    slot = jnp.dot(before, named, preferred_element_type=jnp.float32).astype(jnp.int32)
    picks = hits.T[:, None, :] & (
        slot.T[:, None, :] == jnp.arange(cap, dtype=jnp.int32)[None, :, None]
    )
    received = jnp.einsum(
        "est,td->esd", picks.astype(jnp.bfloat16), rows_all, preferred_element_type=jnp.float32
    ).astype(jnp.bfloat16)
    gate = jnp.einsum("esd,edf->esf", received, w_gate, preferred_element_type=jnp.float32)
    upward = jnp.einsum("esd,edf->esf", received, w_up, preferred_element_type=jnp.float32)
    hidden = (jax.nn.silu(gate) * upward).astype(jnp.bfloat16)
    result = jnp.einsum("esf,efd->esd", hidden, w_down, preferred_element_type=jnp.float32)
    result = result.astype(jnp.bfloat16)
    zero = jnp.zeros((), jnp.bfloat16)
    high = jnp.where(picks, high.T[:, None, :], zero)
    low = jnp.where(picks, low.T[:, None, :], zero)
    partial = jnp.einsum("est,esd->td", high, result, preferred_element_type=jnp.float32)
    partial = partial + jnp.einsum("est,esd->td", low, result, preferred_element_type=jnp.float32)
    return partial


def shards(
    tokens,
    norm_attn,
    w_query,
    w_key,
    w_value,
    w_out,
    norm_moe,
    w_router,
    w_gate,
    w_up,
    w_down,
    segment_ids,
    page_order,
    expert_ids,
):
    rows, width = tokens.shape
    seg = segment_ids[0]
    groups = w_key.shape[1] // HD
    here = lax.axis_index("exp")
    pos = lax.dynamic_slice_in_dim(positions(seg), here * rows, rows)
    normed = rms_scale(tokens, norm_attn)
    query = jnp.dot(normed, w_query, preferred_element_type=jnp.float32).reshape(
        rows, 2 * groups, HD
    )
    query = rotate(query, pos).astype(jnp.bfloat16).reshape(rows, groups, 2 * HD)
    keys = jnp.dot(normed, w_key, preferred_element_type=jnp.float32).reshape(rows, groups, HD)
    keys = rotate(keys, pos).astype(jnp.bfloat16)
    values = (
        jnp.dot(normed, w_value, preferred_element_type=jnp.float32)
        .astype(jnp.bfloat16)
        .reshape(rows, groups, HD)
    )
    keyval = jnp.concatenate([keys, values], axis=-1)
    query_heads, keyval_heads = (
        lax.all_to_all(query, "exp", split_axis=1, concat_axis=0, tiled=True),
        lax.all_to_all(keyval, "exp", split_axis=1, concat_axis=0, tiled=True),
    )
    plen = keyval_heads.shape[0]
    placing = page_order[0][None, :] == jnp.arange(plen, dtype=jnp.int32)[:, None]
    kv_cache = jnp.einsum(
        "rs,skd->rkd", placing.astype(jnp.bfloat16), keyval_heads, preferred_element_type=jnp.float32
    ).astype(jnp.bfloat16)
    heads_out = attend(query_heads, keyval_heads, seg)
    attention = lax.psum_scatter(
        jnp.dot(heads_out, w_out, preferred_element_type=jnp.float32),
        "exp",
        scatter_dimension=0,
        tiled=True,
    )
    resid = tokens.astype(jnp.float32) + attention
    normed2 = rms_scale(resid, norm_moe)
    packed = lax.all_gather(routing(normed2, expert_ids, w_router), "exp", axis=0, tiled=True)
    partial = expert_mix(packed, width, w_router.shape[1], w_gate, w_up, w_down)
    moe = lax.psum_scatter(partial, "exp", scatter_dimension=0, tiled=True)
    mixed = (resid + moe).astype(jnp.bfloat16)
    return (mixed, kv_cache)


def solution(mesh):
    placed = (
        P(("req", "exp"), None),
        P(),
        P(),
        P(),
        P(),
        P("exp", None),
        P(),
        P(),
        P("exp", None, None),
        P("exp", None, None),
        P("exp", None, None),
        P("req", None),
        P("req", None),
        P(("req", "exp"), None),
    )
    return jax.shard_map(
        shards,
        mesh=mesh,
        in_specs=placed,
        out_specs=(P(("req", "exp"), None), P("req", "exp", None)),
        check_vma=False,
    )
```

```python
import jax
import jax.numpy as jnp
from jax import lax
from jax.sharding import PartitionSpec as P

HD = 64
CAP = 64


def rms_scale(rows, gain):
    rows = rows.astype(jnp.float32)
    inverse = lax.rsqrt(jnp.mean(rows * rows, axis=-1, keepdims=True) + 1e-06)
    return (rows * inverse * gain.astype(jnp.float32)).astype(jnp.bfloat16)


def positions(seg):
    index = jnp.arange(seg.shape[0], dtype=jnp.int32)
    starts = jnp.concatenate([jnp.ones((1,), dtype=bool), seg[1:] != seg[:-1]])
    first = lax.cummax(jnp.where(starts, index, 0), axis=0)
    return index - first


def rotate(values, pos):
    half = values.shape[-1] // 2
    freq = 10000.0 ** (-jnp.arange(half, dtype=jnp.float32) / half)
    angle = pos.astype(jnp.float32)[:, None] * freq[None, :]
    cosine = jnp.cos(angle)[:, None, :]
    sine = jnp.sin(angle)[:, None, :]
    front = values[..., :half]
    back = values[..., half:]
    return jnp.concatenate([front * cosine - back * sine, back * cosine + front * sine], axis=-1)


def attend(query, keyval, seg):
    plen, groups, width = query.shape
    half = width // 2
    block = min(512, plen)
    blocks = plen // block
    queries = query.reshape(blocks, block, groups, 2, half)
    keys = keyval[..., :half]
    values = keyval[..., half:]
    key_pos = jnp.arange(plen, dtype=jnp.int32)
    query_pos = key_pos.reshape(blocks, block)
    query_seg = seg.reshape(blocks, block)

    def one_block(args):
        qblock, qpos, qseg = args
        score = (
            jnp.einsum("qkgd,tkd->kgqt", qblock, keys, preferred_element_type=jnp.float32) * 0.125
        )
        allowed = (qseg[:, None] == seg[None, :]) & (key_pos[None, :] <= qpos[:, None])
        score = jnp.where(allowed[None, None], score, -1e30)
        top = jnp.max(score, axis=-1, keepdims=True)
        expo = jnp.exp(score - top)
        probs = (expo / jnp.sum(expo, axis=-1, keepdims=True)).astype(jnp.bfloat16)
        out = jnp.einsum("kgqt,tkd->qkgd", probs, values, preferred_element_type=jnp.float32)
        return out.astype(jnp.bfloat16)

    outs = lax.map(one_block, (queries, query_pos, query_seg))
    return outs.reshape(plen, groups * width)


def routing(normed2, ids, w_router):
    experts = w_router.shape[1]
    logits = jnp.dot(normed2, w_router, preferred_element_type=jnp.float32)
    match = ids[:, :, None] == jnp.arange(experts, dtype=jnp.int32)
    chosen = jnp.sum(jnp.where(match, logits[:, None, :], 0.0), axis=2)
    weights = jax.nn.softmax(chosen, axis=-1)
    dense = jnp.sum(jnp.where(match, weights[:, :, None], 0.0), axis=1)
    high = dense.astype(jnp.bfloat16)
    low = (dense - high.astype(jnp.float32)).astype(jnp.bfloat16)
    named = jnp.any(match, axis=1).astype(jnp.bfloat16)
    pad = (-3 * experts) % 128
    fill = jnp.zeros((normed2.shape[0], pad), jnp.bfloat16)
    return jnp.concatenate([normed2, high, low, named, fill], axis=1)


def expert_mix(packed, width, experts, w_gate, w_up, w_down):
    tokens_all = packed.shape[0]
    local = w_gate.shape[0]
    cap = CAP * lax.axis_size("exp")
    here = lax.axis_index("exp")
    rows_all = packed[:, :width]

    def columns(block):
        return lax.dynamic_slice_in_dim(packed, width + block * experts + here * local, local, 1)

    high, low, named = columns(0), columns(1), columns(2)
    hits = named > 0
    order = jnp.arange(tokens_all, dtype=jnp.int32)
    before = (order[None, :] < order[:, None]).astype(jnp.bfloat16)
    slot = jnp.dot(before, named, preferred_element_type=jnp.float32).astype(jnp.int32)
    picks = hits.T[:, None, :] & (
        slot.T[:, None, :] == jnp.arange(cap, dtype=jnp.int32)[None, :, None]
    )
    received = jnp.einsum(
        "est,td->esd", picks.astype(jnp.bfloat16), rows_all, preferred_element_type=jnp.float32
    ).astype(jnp.bfloat16)
    gate = jnp.einsum("esd,edf->esf", received, w_gate, preferred_element_type=jnp.float32)
    upward = jnp.einsum("esd,edf->esf", received, w_up, preferred_element_type=jnp.float32)
    hidden = (jax.nn.silu(gate) * upward).astype(jnp.bfloat16)
    result = jnp.einsum("esf,efd->esd", hidden, w_down, preferred_element_type=jnp.float32)
    result = result.astype(jnp.bfloat16)
    zero = jnp.zeros((), jnp.bfloat16)
    high = jnp.where(picks, high.T[:, None, :], zero)
    low = jnp.where(picks, low.T[:, None, :], zero)
    partial = jnp.einsum("est,esd->td", high, result, preferred_element_type=jnp.float32)
    partial = partial + jnp.einsum("est,esd->td", low, result, preferred_element_type=jnp.float32)
    return partial


def shards(
    tokens,
    norm_attn,
    w_query,
    w_key,
    w_value,
    w_out,
    norm_moe,
    w_router,
    w_gate,
    w_up,
    w_down,
    segment_ids,
    page_order,
    expert_ids,
):
    rows, width = tokens.shape
    seg = segment_ids[0]
    groups = w_key.shape[1] // HD
    here = lax.axis_index("exp")
    pos = lax.dynamic_slice_in_dim(positions(seg), here * rows, rows)
    normed = rms_scale(tokens, norm_attn)
    query = jnp.dot(normed, w_query, preferred_element_type=jnp.float32).reshape(
        rows, 2 * groups, HD
    )
    query = rotate(query, pos).astype(jnp.bfloat16).reshape(rows, groups, 2 * HD)
    keys = jnp.dot(normed, w_key, preferred_element_type=jnp.float32).reshape(rows, groups, HD)
    keys = rotate(keys, pos).astype(jnp.bfloat16)
    values = (
        jnp.dot(normed, w_value, preferred_element_type=jnp.float32)
        .astype(jnp.bfloat16)
        .reshape(rows, groups, HD)
    )
    keyval = jnp.concatenate([keys, values], axis=-1)
    both = lax.all_to_all(
        jnp.concatenate([query, keyval], axis=-1), "exp", split_axis=1, concat_axis=0, tiled=True
    )
    query_heads, keyval_heads = both[..., : 2 * HD], both[..., 2 * HD :]
    plen = keyval_heads.shape[0]
    placing = page_order[0][None, :] == jnp.arange(plen, dtype=jnp.int32)[:, None]
    kv_cache = jnp.einsum(
        "rs,skd->rkd", placing.astype(jnp.bfloat16), keyval_heads, preferred_element_type=jnp.float32
    ).astype(jnp.bfloat16)
    heads_out = attend(query_heads, keyval_heads, seg)
    attention = lax.psum_scatter(
        jnp.dot(heads_out, w_out, preferred_element_type=jnp.float32).astype(jnp.bfloat16),
        "exp",
        scatter_dimension=0,
        tiled=True,
    )
    resid = tokens.astype(jnp.float32) + attention.astype(jnp.float32)
    normed2 = rms_scale(resid, norm_moe)
    packed = lax.all_gather(routing(normed2, expert_ids, w_router), "exp", axis=0, tiled=True)
    partial = expert_mix(packed, width, w_router.shape[1], w_gate, w_up, w_down)
    moe = lax.psum_scatter(partial.astype(jnp.bfloat16), "exp", scatter_dimension=0, tiled=True)
    moe = moe.astype(jnp.float32)
    mixed = (resid + moe).astype(jnp.bfloat16)
    return (mixed, kv_cache)


def solution(mesh):
    placed = (
        P(("req", "exp"), None),
        P(),
        P(),
        P(),
        P(),
        P("exp", None),
        P(),
        P(),
        P("exp", None, None),
        P("exp", None, None),
        P("exp", None, None),
        P("req", None),
        P("req", None),
        P(("req", "exp"), None),
    )
    return jax.shard_map(
        shards,
        mesh=mesh,
        in_specs=placed,
        out_specs=(P(("req", "exp"), None), P("req", "exp", None)),
        check_vma=False,
    )
```

```python
import jax
import jax.numpy as jnp
from jax import lax
from jax.sharding import PartitionSpec as P

HD = 64
CAP = 64


def rms_scale(rows, gain):
    rows = rows.astype(jnp.float32)
    inverse = lax.rsqrt(jnp.mean(rows * rows, axis=-1, keepdims=True) + 1e-06)
    return (rows * inverse * gain.astype(jnp.float32)).astype(jnp.bfloat16)


def positions(seg):
    index = jnp.arange(seg.shape[0], dtype=jnp.int32)
    starts = jnp.concatenate([jnp.ones((1,), dtype=bool), seg[1:] != seg[:-1]])
    first = lax.cummax(jnp.where(starts, index, 0), axis=0)
    return index - first


def rotate(values, pos):
    half = values.shape[-1] // 2
    freq = 10000.0 ** (-jnp.arange(half, dtype=jnp.float32) / half)
    angle = pos.astype(jnp.float32)[:, None] * freq[None, :]
    cosine = jnp.cos(angle)[:, None, :]
    sine = jnp.sin(angle)[:, None, :]
    front = values[..., :half]
    back = values[..., half:]
    return jnp.concatenate([front * cosine - back * sine, back * cosine + front * sine], axis=-1)


def attend(query, keyval, seg):
    plen, groups, width = query.shape
    half = width // 2
    block = min(512, plen)
    blocks = plen // block
    queries = query.reshape(blocks, block, groups, 2, half)
    keys = keyval[..., :half]
    values = keyval[..., half:]
    key_pos = jnp.arange(plen, dtype=jnp.int32)
    query_pos = key_pos.reshape(blocks, block)
    query_seg = seg.reshape(blocks, block)

    def one_block(args):
        qblock, qpos, qseg = args
        score = (
            jnp.einsum("qkgd,tkd->kgqt", qblock, keys, preferred_element_type=jnp.float32) * 0.125
        )
        allowed = (qseg[:, None] == seg[None, :]) & (key_pos[None, :] <= qpos[:, None])
        score = jnp.where(allowed[None, None], score, -1e30)
        top = jnp.max(score, axis=-1, keepdims=True)
        expo = jnp.exp(score - top)
        probs = (expo / jnp.sum(expo, axis=-1, keepdims=True)).astype(jnp.bfloat16)
        out = jnp.einsum("kgqt,tkd->qkgd", probs, values, preferred_element_type=jnp.float32)
        return out.astype(jnp.bfloat16)

    outs = lax.map(one_block, (queries, query_pos, query_seg))
    return outs.reshape(plen, groups * width)


def routing(normed2, ids, w_router):
    experts = w_router.shape[1]
    logits = jnp.dot(normed2, w_router, preferred_element_type=jnp.float32)
    match = ids[:, :, None] == jnp.arange(experts, dtype=jnp.int32)
    chosen = jnp.sum(jnp.where(match, logits[:, None, :], 0.0), axis=2)
    weights = jax.nn.softmax(chosen, axis=-1)
    dense = jnp.sum(jnp.where(match, weights[:, :, None], 0.0), axis=1)
    high = dense.astype(jnp.bfloat16)
    low = (dense - high.astype(jnp.float32)).astype(jnp.bfloat16)
    named = jnp.any(match, axis=1).astype(jnp.bfloat16)
    pad = (-3 * experts) % 128
    fill = jnp.zeros((normed2.shape[0], pad), jnp.bfloat16)
    return jnp.concatenate([normed2, high, low, named, fill], axis=1)


def expert_mix(packed, width, experts, w_gate, w_up, w_down):
    tokens_all = packed.shape[0]
    local = w_gate.shape[0]
    cap = CAP
    here = lax.axis_index("exp")
    rows_all = packed[:, :width]

    def columns(block):
        return lax.dynamic_slice_in_dim(packed, width + block * experts + here * local, local, 1)

    high, low, named = columns(0), columns(1), columns(2)
    hits = named > 0
    order = jnp.arange(tokens_all, dtype=jnp.int32)
    before = (order[None, :] < order[:, None]).astype(jnp.bfloat16)
    slot = jnp.dot(before, named, preferred_element_type=jnp.float32).astype(jnp.int32)
    picks = hits.T[:, None, :] & (
        slot.T[:, None, :] == jnp.arange(cap, dtype=jnp.int32)[None, :, None]
    )
    received = jnp.einsum(
        "est,td->esd", picks.astype(jnp.bfloat16), rows_all, preferred_element_type=jnp.float32
    ).astype(jnp.bfloat16)
    gate = jnp.einsum("esd,edf->esf", received, w_gate, preferred_element_type=jnp.float32)
    upward = jnp.einsum("esd,edf->esf", received, w_up, preferred_element_type=jnp.float32)
    hidden = (jax.nn.silu(gate) * upward).astype(jnp.bfloat16)
    result = jnp.einsum("esf,efd->esd", hidden, w_down, preferred_element_type=jnp.float32)
    result = result.astype(jnp.bfloat16)
    zero = jnp.zeros((), jnp.bfloat16)
    high = jnp.where(picks, high.T[:, None, :], zero)
    low = jnp.where(picks, low.T[:, None, :], zero)
    partial = jnp.einsum("est,esd->td", high, result, preferred_element_type=jnp.float32)
    partial = partial + jnp.einsum("est,esd->td", low, result, preferred_element_type=jnp.float32)
    return partial


def shifted(x, step):
    count = lax.axis_size("exp")
    return lax.ppermute(x, "exp", [(j, (j + step) % count) for j in range(count)])


def exchange_sum(blocks):
    count = blocks.shape[0]
    here = lax.axis_index("exp")
    total = lax.dynamic_index_in_dim(blocks, here, 0, keepdims=False).astype(jnp.float32)
    for step in range(1, count):
        send = lax.dynamic_index_in_dim(blocks, (here + step) % count, 0, keepdims=False)
        total = total + shifted(send, step).astype(jnp.float32)
    return total


def shards(
    tokens,
    norm_attn,
    w_query,
    w_key,
    w_value,
    w_out,
    norm_moe,
    w_router,
    w_gate,
    w_up,
    w_down,
    segment_ids,
    page_order,
    expert_ids,
):
    rows, width = tokens.shape
    seg = segment_ids[0]
    groups = w_key.shape[1] // HD
    here = lax.axis_index("exp")
    pos = lax.dynamic_slice_in_dim(positions(seg), here * rows, rows)
    normed = rms_scale(tokens, norm_attn)
    query = jnp.dot(normed, w_query, preferred_element_type=jnp.float32).reshape(
        rows, 2 * groups, HD
    )
    query = rotate(query, pos).astype(jnp.bfloat16).reshape(rows, groups, 2 * HD)
    keys = jnp.dot(normed, w_key, preferred_element_type=jnp.float32).reshape(rows, groups, HD)
    keys = rotate(keys, pos).astype(jnp.bfloat16)
    values = (
        jnp.dot(normed, w_value, preferred_element_type=jnp.float32)
        .astype(jnp.bfloat16)
        .reshape(rows, groups, HD)
    )
    keyval = jnp.concatenate([keys, values], axis=-1)
    both = lax.all_to_all(
        jnp.concatenate([query, keyval], axis=-1), "exp", split_axis=1, concat_axis=0, tiled=True
    )
    query_heads, keyval_heads = both[..., : 2 * HD], both[..., 2 * HD :]
    plen = keyval_heads.shape[0]
    placing = page_order[0][None, :] == jnp.arange(plen, dtype=jnp.int32)[:, None]
    kv_cache = jnp.einsum(
        "rs,skd->rkd", placing.astype(jnp.bfloat16), keyval_heads, preferred_element_type=jnp.float32
    ).astype(jnp.bfloat16)
    heads_out = attend(query_heads, keyval_heads, seg)
    owners = lax.axis_size("exp")
    attention = jnp.dot(heads_out, w_out, preferred_element_type=jnp.float32).astype(jnp.bfloat16)
    attention = exchange_sum(attention.reshape(owners, rows, width))
    resid = tokens.astype(jnp.float32) + attention
    normed2 = rms_scale(resid, norm_moe)
    packed = routing(normed2, expert_ids, w_router)
    experts = w_router.shape[1]
    moe = expert_mix(packed, width, experts, w_gate, w_up, w_down)
    for step in range(1, owners):
        partial = expert_mix(shifted(packed, step), width, experts, w_gate, w_up, w_down)
        moe = moe + shifted(partial.astype(jnp.bfloat16), -step).astype(jnp.float32)
    mixed = (resid + moe).astype(jnp.bfloat16)
    return (mixed, kv_cache)


def solution(mesh):
    placed = (
        P(("req", "exp"), None),
        P(),
        P(),
        P(),
        P(),
        P("exp", None),
        P(),
        P(),
        P("exp", None, None),
        P("exp", None, None),
        P("exp", None, None),
        P("req", None),
        P("req", None),
        P(("req", "exp"), None),
    )
    return jax.shard_map(
        shards,
        mesh=mesh,
        in_specs=placed,
        out_specs=(P(("req", "exp"), None), P("req", "exp", None)),
        check_vma=False,
    )
```

```python
import jax
import jax.numpy as jnp
from jax import lax
from jax.sharding import PartitionSpec as P

HD = 64
CAP = 64


def rms_scale(rows, gain):
    rows = rows.astype(jnp.float32)
    inverse = lax.rsqrt(jnp.mean(rows * rows, axis=-1, keepdims=True) + 1e-06)
    return (rows * inverse * gain.astype(jnp.float32)).astype(jnp.bfloat16)


def positions(seg):
    index = jnp.arange(seg.shape[0], dtype=jnp.int32)
    starts = jnp.concatenate([jnp.ones((1,), dtype=bool), seg[1:] != seg[:-1]])
    first = lax.cummax(jnp.where(starts, index, 0), axis=0)
    return index - first


def rotate(values, pos):
    half = values.shape[-1] // 2
    freq = 10000.0 ** (-jnp.arange(half, dtype=jnp.float32) / half)
    angle = pos.astype(jnp.float32)[:, None] * freq[None, :]
    cosine = jnp.cos(angle)[:, None, :]
    sine = jnp.sin(angle)[:, None, :]
    front = values[..., :half]
    back = values[..., half:]
    return jnp.concatenate([front * cosine - back * sine, back * cosine + front * sine], axis=-1)


def attend(query, keyval, seg, where_at):
    plen, groups, width = query.shape
    half = width // 2
    queries = query.reshape(plen, groups, 2, half)
    keys = keyval[..., :half]
    values = keyval[..., half:]
    score = jnp.einsum("qkgd,tkd->kgqt", queries, keys, preferred_element_type=jnp.float32) * 0.125
    allowed = (seg[:, None] == seg[None, :]) & (where_at[None, :] <= where_at[:, None])
    score = jnp.where(allowed[None, None], score, -1e30)
    top = jnp.max(score, axis=-1, keepdims=True)
    expo = jnp.exp(score - top)
    probs = (expo / jnp.sum(expo, axis=-1, keepdims=True)).astype(jnp.bfloat16)
    out = jnp.einsum("kgqt,tkd->qkgd", probs, values, preferred_element_type=jnp.float32)
    return out.astype(jnp.bfloat16).reshape(plen, groups * width)


def routing(normed2, ids, w_router):
    experts = w_router.shape[1]
    logits = jnp.dot(normed2, w_router, preferred_element_type=jnp.float32)
    match = ids[:, :, None] == jnp.arange(experts, dtype=jnp.int32)
    chosen = jnp.sum(jnp.where(match, logits[:, None, :], 0.0), axis=2)
    weights = jax.nn.softmax(chosen, axis=-1)
    dense = jnp.sum(jnp.where(match, weights[:, :, None], 0.0), axis=1)
    high = dense.astype(jnp.bfloat16)
    low = (dense - high.astype(jnp.float32)).astype(jnp.bfloat16)
    named = jnp.any(match, axis=1).astype(jnp.bfloat16)
    pad = (-3 * experts) % 128
    fill = jnp.zeros((normed2.shape[0], pad), jnp.bfloat16)
    return jnp.concatenate([normed2, high, low, named, fill], axis=1)


def expert_mix(packed, sources, width, experts, w_gate, w_up, w_down):
    tokens_all = packed.shape[0]
    local = w_gate.shape[0]
    rows = tokens_all // sources
    cap = CAP * sources
    here = lax.axis_index("exp")
    rows_all = packed[:, :width]

    def columns(block):
        return lax.dynamic_slice_in_dim(packed, width + block * experts + here * local, local, 1)

    high, low, named = columns(0), columns(1), columns(2)
    hits = named > 0
    order = jnp.arange(tokens_all, dtype=jnp.int32)
    block = order // rows
    before = (order[None, :] < order[:, None]) & (block[None, :] == block[:, None])
    slot = jnp.dot(before.astype(jnp.bfloat16), named, preferred_element_type=jnp.float32)
    slot = slot.astype(jnp.int32) + (block * CAP)[:, None]
    picks = hits.T[:, None, :] & (
        slot.T[:, None, :] == jnp.arange(cap, dtype=jnp.int32)[None, :, None]
    )
    received = jnp.einsum(
        "est,td->esd", picks.astype(jnp.bfloat16), rows_all, preferred_element_type=jnp.float32
    ).astype(jnp.bfloat16)
    gate = jnp.einsum("esd,edf->esf", received, w_gate, preferred_element_type=jnp.float32)
    upward = jnp.einsum("esd,edf->esf", received, w_up, preferred_element_type=jnp.float32)
    hidden = (jax.nn.silu(gate) * upward).astype(jnp.bfloat16)
    result = jnp.einsum("esf,efd->esd", hidden, w_down, preferred_element_type=jnp.float32)
    result = result.astype(jnp.bfloat16)
    zero = jnp.zeros((), jnp.bfloat16)
    high = jnp.where(picks, high.T[:, None, :], zero)
    low = jnp.where(picks, low.T[:, None, :], zero)
    partial = jnp.einsum("est,esd->td", high, result, preferred_element_type=jnp.float32)
    partial = partial + jnp.einsum("est,esd->td", low, result, preferred_element_type=jnp.float32)
    return partial


def shifted(x, step):
    count = lax.axis_size("exp")
    return lax.ppermute(x, "exp", [(j, (j + step) % count) for j in range(count)])


def exchange_sum(blocks):
    total = blocks[0].astype(jnp.float32)
    for step in range(1, blocks.shape[0]):
        total = total + shifted(blocks[step], -step).astype(jnp.float32)
    return total


def step_rows(x, rows):
    count = lax.axis_size("exp")
    here = lax.axis_index("exp")
    parts = [
        lax.dynamic_slice_in_dim(x, (here - step) % count * rows, rows) for step in range(count)
    ]
    return jnp.concatenate(parts)


def shards(
    tokens,
    norm_attn,
    w_query,
    w_key,
    w_value,
    w_out,
    norm_moe,
    w_router,
    w_gate,
    w_up,
    w_down,
    segment_ids,
    page_order,
    expert_ids,
):
    rows, width = tokens.shape
    seg = segment_ids[0]
    groups = w_key.shape[1] // HD
    here = lax.axis_index("exp")
    pos = lax.dynamic_slice_in_dim(positions(seg), here * rows, rows)
    normed = rms_scale(tokens, norm_attn)
    query = jnp.dot(normed, w_query, preferred_element_type=jnp.float32).reshape(
        rows, 2 * groups, HD
    )
    query = rotate(query, pos).astype(jnp.bfloat16).reshape(rows, groups, 2 * HD)
    keys = jnp.dot(normed, w_key, preferred_element_type=jnp.float32).reshape(rows, groups, HD)
    keys = rotate(keys, pos).astype(jnp.bfloat16)
    values = (
        jnp.dot(normed, w_value, preferred_element_type=jnp.float32)
        .astype(jnp.bfloat16)
        .reshape(rows, groups, HD)
    )
    keyval = jnp.concatenate([keys, values], axis=-1)
    owners = lax.axis_size("exp")
    share = groups // owners
    both = jnp.concatenate([query, keyval], axis=-1)
    parts = [lax.dynamic_slice_in_dim(both, here * share, share, 1)]
    for step in range(1, owners):
        send = lax.dynamic_slice_in_dim(both, (here + step) % owners * share, share, 1)
        parts.append(shifted(send, step))
    both = jnp.concatenate(parts)
    query_heads, keyval_heads = both[..., : 2 * HD], both[..., 2 * HD :]
    plen = keyval_heads.shape[0]
    where_at = step_rows(jnp.arange(plen, dtype=jnp.int32), rows)
    placing = step_rows(page_order[0], rows)[None, :] == jnp.arange(plen, dtype=jnp.int32)[:, None]
    kv_cache = jnp.einsum(
        "rs,skd->rkd", placing.astype(jnp.bfloat16), keyval_heads, preferred_element_type=jnp.float32
    ).astype(jnp.bfloat16)
    heads_out = attend(query_heads, keyval_heads, step_rows(seg, rows), where_at)
    attention = jnp.dot(heads_out, w_out, preferred_element_type=jnp.float32).astype(jnp.bfloat16)
    attention = exchange_sum(attention.reshape(owners, rows, width))
    resid = tokens.astype(jnp.float32) + attention
    normed2 = rms_scale(resid, norm_moe)
    packed = routing(normed2, expert_ids, w_router)
    experts = w_router.shape[1]
    moe = expert_mix(packed, 1, width, experts, w_gate, w_up, w_down)
    received = jnp.concatenate([shifted(packed, step) for step in range(1, owners)])
    others = expert_mix(received, owners - 1, width, experts, w_gate, w_up, w_down)
    others = others.astype(jnp.bfloat16).reshape(owners - 1, rows, width)
    for step in range(1, owners):
        moe = moe + shifted(others[step - 1], -step).astype(jnp.float32)
    mixed = (resid + moe).astype(jnp.bfloat16)
    return (mixed, kv_cache)


def solution(mesh):
    placed = (
        P(("req", "exp"), None),
        P(),
        P(),
        P(),
        P(),
        P("exp", None),
        P(),
        P(),
        P("exp", None, None),
        P("exp", None, None),
        P("exp", None, None),
        P("req", None),
        P("req", None),
        P(("req", "exp"), None),
    )
    return jax.shard_map(
        shards,
        mesh=mesh,
        in_specs=placed,
        out_specs=(P(("req", "exp"), None), P("req", "exp", None)),
        check_vma=False,
    )
```

```python
import jax
import jax.numpy as jnp
from jax import lax
from jax.sharding import PartitionSpec as P

HD = 64
CAP = 64


def rms_scale(rows, gain):
    rows = rows.astype(jnp.float32)
    inverse = lax.rsqrt(jnp.mean(rows * rows, axis=-1, keepdims=True) + 1e-06)
    return (rows * inverse * gain.astype(jnp.float32)).astype(jnp.bfloat16)


def positions(seg):
    index = jnp.arange(seg.shape[0], dtype=jnp.int32)
    starts = jnp.concatenate([jnp.ones((1,), dtype=bool), seg[1:] != seg[:-1]])
    first = lax.cummax(jnp.where(starts, index, 0), axis=0)
    return index - first


def rotate(values, pos):
    half = values.shape[-1] // 2
    freq = 10000.0 ** (-jnp.arange(half, dtype=jnp.float32) / half)
    angle = pos.astype(jnp.float32)[:, None] * freq[None, :]
    cosine = jnp.cos(angle)[:, None, :]
    sine = jnp.sin(angle)[:, None, :]
    front = values[..., :half]
    back = values[..., half:]
    return jnp.concatenate([front * cosine - back * sine, back * cosine + front * sine], axis=-1)


def attend(query, keyval, query_seg, seg, query_at, where_at):
    plen, groups, width = query.shape
    half = width // 2
    queries = query.reshape(plen, groups, 2, half)
    keys = keyval[..., :half]
    values = keyval[..., half:]
    score = jnp.einsum("qkgd,tkd->kgqt", queries, keys, preferred_element_type=jnp.float32) * 0.125
    allowed = (query_seg[:, None] == seg[None, :]) & (where_at[None, :] <= query_at[:, None])
    score = jnp.where(allowed[None, None], score, -1e30)
    top = jnp.max(score, axis=-1, keepdims=True)
    expo = jnp.exp(score - top)
    probs = (expo / jnp.sum(expo, axis=-1, keepdims=True)).astype(jnp.bfloat16)
    out = jnp.einsum("kgqt,tkd->qkgd", probs, values, preferred_element_type=jnp.float32)
    return out.astype(jnp.bfloat16).reshape(plen, groups * width)


def routing(normed2, ids, w_router):
    experts = w_router.shape[1]
    logits = jnp.dot(normed2, w_router, preferred_element_type=jnp.float32)
    match = ids[:, :, None] == jnp.arange(experts, dtype=jnp.int32)
    chosen = jnp.sum(jnp.where(match, logits[:, None, :], 0.0), axis=2)
    weights = jax.nn.softmax(chosen, axis=-1)
    dense = jnp.sum(jnp.where(match, weights[:, :, None], 0.0), axis=1)
    high = dense.astype(jnp.bfloat16)
    low = (dense - high.astype(jnp.float32)).astype(jnp.bfloat16)
    named = jnp.any(match, axis=1).astype(jnp.bfloat16)
    pad = (-3 * experts) % 128
    fill = jnp.zeros((normed2.shape[0], pad), jnp.bfloat16)
    return jnp.concatenate([normed2, high, low, named, fill], axis=1)


def expert_mix(packed, sources, width, experts, w_gate, w_up, w_down, pieces):
    tokens_all = packed.shape[0]
    local = w_gate.shape[0]
    rows = tokens_all // sources
    cap = CAP * sources
    here = lax.axis_index("exp")
    rows_all = packed[:, :width]

    def columns(block):
        return lax.dynamic_slice_in_dim(packed, width + block * experts + here * local, local, 1)

    high, low, named = columns(0), columns(1), columns(2)
    hits = named > 0
    order = jnp.arange(tokens_all, dtype=jnp.int32)
    block = order // rows
    before = (order[None, :] < order[:, None]) & (block[None, :] == block[:, None])
    slot = jnp.dot(before.astype(jnp.bfloat16), named, preferred_element_type=jnp.float32)
    slot = slot.astype(jnp.int32) + (block * CAP)[:, None]
    picks = hits.T[:, None, :] & (
        slot.T[:, None, :] == jnp.arange(cap, dtype=jnp.int32)[None, :, None]
    )
    received = jnp.einsum(
        "est,td->esd", picks.astype(jnp.bfloat16), rows_all, preferred_element_type=jnp.float32
    ).astype(jnp.bfloat16)
    gate = jnp.einsum("esd,edf->esf", received, w_gate, preferred_element_type=jnp.float32)
    upward = jnp.einsum("esd,edf->esf", received, w_up, preferred_element_type=jnp.float32)
    hidden = (jax.nn.silu(gate) * upward).astype(jnp.bfloat16)
    zero = jnp.zeros((), jnp.bfloat16)
    high = jnp.where(picks, high.T[:, None, :], zero)
    low = jnp.where(picks, low.T[:, None, :], zero)
    cut = w_down.shape[2] // pieces
    outs = []
    for piece in range(pieces):
        down = lax.slice_in_dim(w_down, piece * cut, (piece + 1) * cut, axis=2)
        result = jnp.einsum("esf,efd->esd", hidden, down, preferred_element_type=jnp.float32)
        result = result.astype(jnp.bfloat16)
        partial = jnp.einsum("est,esd->td", high, result, preferred_element_type=jnp.float32)
        partial = partial + jnp.einsum(
            "est,esd->td", low, result, preferred_element_type=jnp.float32
        )
        outs.append(partial)
    return outs


def shifted(x, step):
    count = lax.axis_size("exp")
    return lax.ppermute(x, "exp", [(j, (j + step) % count) for j in range(count)])


def exchange_sum(blocks):
    total = blocks[0].astype(jnp.float32)
    for step in range(1, blocks.shape[0]):
        total = total + shifted(blocks[step], -step).astype(jnp.float32)
    return total


def step_rows(x, rows):
    count = lax.axis_size("exp")
    here = lax.axis_index("exp")
    parts = [
        lax.dynamic_slice_in_dim(x, (here - step) % count * rows, rows) for step in range(count)
    ]
    return jnp.concatenate(parts)


def shards(
    tokens,
    norm_attn,
    w_query,
    w_key,
    w_value,
    w_out,
    norm_moe,
    w_router,
    w_gate,
    w_up,
    w_down,
    segment_ids,
    page_order,
    expert_ids,
):
    rows, width = tokens.shape
    seg = segment_ids[0]
    groups = w_key.shape[1] // HD
    here = lax.axis_index("exp")
    pos = lax.dynamic_slice_in_dim(positions(seg), here * rows, rows)
    normed = rms_scale(tokens, norm_attn)
    query = jnp.dot(normed, w_query, preferred_element_type=jnp.float32).reshape(
        rows, 2 * groups, HD
    )
    query = rotate(query, pos).astype(jnp.bfloat16).reshape(rows, groups, 2 * HD)
    keys = jnp.dot(normed, w_key, preferred_element_type=jnp.float32).reshape(rows, groups, HD)
    keys = rotate(keys, pos).astype(jnp.bfloat16)
    values = (
        jnp.dot(normed, w_value, preferred_element_type=jnp.float32)
        .astype(jnp.bfloat16)
        .reshape(rows, groups, HD)
    )
    keyval = jnp.concatenate([keys, values], axis=-1)
    owners = lax.axis_size("exp")
    share = groups // owners
    both = jnp.concatenate([query, keyval], axis=-1)
    parts = [lax.dynamic_slice_in_dim(both, here * share, share, 1)]
    for step in range(1, owners):
        send = lax.dynamic_slice_in_dim(both, (here + step) % owners * share, share, 1)
        parts.append(shifted(send, step))
    both = jnp.concatenate(parts)
    query_heads, keyval_heads = both[..., : 2 * HD], both[..., 2 * HD :]
    plen = keyval_heads.shape[0]
    where_at = step_rows(jnp.arange(plen, dtype=jnp.int32), rows)
    placing = step_rows(page_order[0], rows)[None, :] == jnp.arange(plen, dtype=jnp.int32)[:, None]
    kv_cache = jnp.einsum(
        "rs,skd->rkd", placing.astype(jnp.bfloat16), keyval_heads, preferred_element_type=jnp.float32
    ).astype(jnp.bfloat16)
    seg_rows = step_rows(seg, rows)
    attention = None
    for step in list(range(1, owners)) + [0]:
        picked = slice(step * rows, (step + 1) * rows)
        heads_out = attend(
            query_heads[picked], keyval_heads, seg_rows[picked], seg_rows, where_at[picked], where_at
        )
        block = jnp.dot(heads_out, w_out, preferred_element_type=jnp.float32)
        if step:
            block = shifted(block.astype(jnp.bfloat16), -step).astype(jnp.float32)
        attention = block if attention is None else attention + block
    resid = tokens.astype(jnp.float32) + attention
    normed2 = rms_scale(resid, norm_moe)
    packed = routing(normed2, expert_ids, w_router)
    experts = w_router.shape[1]
    moe = expert_mix(packed, 1, width, experts, w_gate, w_up, w_down, 1)[0]
    received = jnp.concatenate([shifted(packed, step) for step in range(1, owners)])
    pieces = expert_mix(received, owners - 1, width, experts, w_gate, w_up, w_down, 2)
    backs = []
    for piece in pieces:
        piece = piece.astype(jnp.bfloat16).reshape(owners - 1, rows, -1)
        back = sum(
            shifted(piece[step - 1], -step).astype(jnp.float32) for step in range(1, owners)
        )
        backs.append(back)
    moe = moe + jnp.concatenate(backs, axis=1)
    mixed = (resid + moe).astype(jnp.bfloat16)
    return (mixed, kv_cache)


def solution(mesh):
    placed = (
        P(("req", "exp"), None),
        P(),
        P(),
        P(),
        P(),
        P("exp", None),
        P(),
        P(),
        P("exp", None, None),
        P("exp", None, None),
        P("exp", None, None),
        P("req", None),
        P("req", None),
        P(("req", "exp"), None),
    )
    return jax.shard_map(
        shards,
        mesh=mesh,
        in_specs=placed,
        out_specs=(P(("req", "exp"), None), P("req", "exp", None)),
        check_vma=False,
    )
```

```python
import jax
import jax.numpy as jnp
from jax import lax
from jax.sharding import PartitionSpec as P

HD = 64
CAP = 64


def rms_scale(rows, gain):
    rows = rows.astype(jnp.float32)
    inverse = lax.rsqrt(jnp.mean(rows * rows, axis=-1, keepdims=True) + 1e-06)
    return (rows * inverse * gain.astype(jnp.float32)).astype(jnp.bfloat16)


def positions(seg):
    index = jnp.arange(seg.shape[0], dtype=jnp.int32)
    starts = jnp.concatenate([jnp.ones((1,), dtype=bool), seg[1:] != seg[:-1]])
    first = lax.cummax(jnp.where(starts, index, 0), axis=0)
    return index - first


def rotate(values, pos):
    half = values.shape[-1] // 2
    freq = 10000.0 ** (-jnp.arange(half, dtype=jnp.float32) / half)
    angle = pos.astype(jnp.float32)[:, None] * freq[None, :]
    cosine = jnp.cos(angle)[:, None, :]
    sine = jnp.sin(angle)[:, None, :]
    front = values[..., :half]
    back = values[..., half:]
    return jnp.concatenate([front * cosine - back * sine, back * cosine + front * sine], axis=-1)


def attend(query, keyval, query_seg, seg, query_at, where_at):
    plen, groups, width = query.shape
    half = width // 2
    queries = query.reshape(plen, groups, 2, half)
    keys = keyval[..., :half]
    values = keyval[..., half:]
    score = jnp.einsum("qkgd,tkd->kgqt", queries, keys, preferred_element_type=jnp.float32) * 0.125
    allowed = (query_seg[:, None] == seg[None, :]) & (where_at[None, :] <= query_at[:, None])
    score = jnp.where(allowed[None, None], score, -1e30)
    top = jnp.max(score, axis=-1, keepdims=True)
    expo = jnp.exp(score - top)
    probs = (expo / jnp.sum(expo, axis=-1, keepdims=True)).astype(jnp.bfloat16)
    out = jnp.einsum("kgqt,tkd->qkgd", probs, values, preferred_element_type=jnp.float32)
    return out.astype(jnp.bfloat16).reshape(plen, groups * width)


def routing(normed2, ids, w_router):
    experts = w_router.shape[1]
    logits = jnp.dot(normed2, w_router, preferred_element_type=jnp.float32)
    match = ids[:, :, None] == jnp.arange(experts, dtype=jnp.int32)
    chosen = jnp.sum(jnp.where(match, logits[:, None, :], 0.0), axis=2)
    weights = jax.nn.softmax(chosen, axis=-1)
    dense = jnp.sum(jnp.where(match, weights[:, :, None], 0.0), axis=1)
    high = dense.astype(jnp.bfloat16)
    low = (dense - high.astype(jnp.float32)).astype(jnp.bfloat16)
    named = jnp.any(match, axis=1).astype(jnp.bfloat16)
    pad = (-3 * experts) % 128
    fill = jnp.zeros((normed2.shape[0], pad), jnp.bfloat16)
    return jnp.concatenate([normed2, high, low, named, fill], axis=1)


def expert_front(packed, sources, width, experts, w_gate, w_up):
    tokens_all = packed.shape[0]
    local = w_gate.shape[0]
    rows = tokens_all // sources
    cap = CAP * sources
    here = lax.axis_index("exp")
    rows_all = packed[:, :width]

    def columns(block):
        return lax.dynamic_slice_in_dim(packed, width + block * experts + here * local, local, 1)

    high, low, named = columns(0), columns(1), columns(2)
    hits = named > 0
    order = jnp.arange(tokens_all, dtype=jnp.int32)
    block = order // rows
    before = (order[None, :] < order[:, None]) & (block[None, :] == block[:, None])
    slot = jnp.dot(before.astype(jnp.bfloat16), named, preferred_element_type=jnp.float32)
    slot = slot.astype(jnp.int32) + (block * CAP)[:, None]
    picks = hits.T[:, None, :] & (
        slot.T[:, None, :] == jnp.arange(cap, dtype=jnp.int32)[None, :, None]
    )
    received = jnp.einsum(
        "est,td->esd", picks.astype(jnp.bfloat16), rows_all, preferred_element_type=jnp.float32
    ).astype(jnp.bfloat16)
    gate = jnp.einsum("esd,edf->esf", received, w_gate, preferred_element_type=jnp.float32)
    upward = jnp.einsum("esd,edf->esf", received, w_up, preferred_element_type=jnp.float32)
    hidden = (jax.nn.silu(gate) * upward).astype(jnp.bfloat16)
    zero = jnp.zeros((), jnp.bfloat16)
    high = jnp.where(picks, high.T[:, None, :], zero)
    low = jnp.where(picks, low.T[:, None, :], zero)
    return hidden, high, low


def expert_back(hidden, high, low, w_down, pieces):
    cut = w_down.shape[2] // pieces
    outs = []
    for piece in range(pieces):
        down = lax.slice_in_dim(w_down, piece * cut, (piece + 1) * cut, axis=2)
        result = jnp.einsum("esf,efd->esd", hidden, down, preferred_element_type=jnp.float32)
        result = result.astype(jnp.bfloat16)
        partial = jnp.einsum("est,esd->td", high, result, preferred_element_type=jnp.float32)
        partial = partial + jnp.einsum(
            "est,esd->td", low, result, preferred_element_type=jnp.float32
        )
        outs.append(partial)
    return outs


def shifted(x, step):
    count = lax.axis_size("exp")
    return lax.ppermute(x, "exp", [(j, (j + step) % count) for j in range(count)])


def exchange_sum(blocks):
    total = blocks[0].astype(jnp.float32)
    for step in range(1, blocks.shape[0]):
        total = total + shifted(blocks[step], -step).astype(jnp.float32)
    return total


def step_rows(x, rows):
    count = lax.axis_size("exp")
    here = lax.axis_index("exp")
    parts = [
        lax.dynamic_slice_in_dim(x, (here - step) % count * rows, rows) for step in range(count)
    ]
    return jnp.concatenate(parts)


def shards(
    tokens,
    norm_attn,
    w_query,
    w_key,
    w_value,
    w_out,
    norm_moe,
    w_router,
    w_gate,
    w_up,
    w_down,
    segment_ids,
    page_order,
    expert_ids,
):
    rows, width = tokens.shape
    seg = segment_ids[0]
    groups = w_key.shape[1] // HD
    here = lax.axis_index("exp")
    pos = lax.dynamic_slice_in_dim(positions(seg), here * rows, rows)
    normed = rms_scale(tokens, norm_attn)
    query = jnp.dot(normed, w_query, preferred_element_type=jnp.float32).reshape(
        rows, 2 * groups, HD
    )
    query = rotate(query, pos).astype(jnp.bfloat16).reshape(rows, groups, 2 * HD)
    keys = jnp.dot(normed, w_key, preferred_element_type=jnp.float32).reshape(rows, groups, HD)
    keys = rotate(keys, pos).astype(jnp.bfloat16)
    values = (
        jnp.dot(normed, w_value, preferred_element_type=jnp.float32)
        .astype(jnp.bfloat16)
        .reshape(rows, groups, HD)
    )
    keyval = jnp.concatenate([keys, values], axis=-1)
    owners = lax.axis_size("exp")
    share = groups // owners
    both = jnp.concatenate([query, keyval], axis=-1)
    parts = [lax.dynamic_slice_in_dim(both, here * share, share, 1)]
    for step in range(1, owners):
        send = lax.dynamic_slice_in_dim(both, (here + step) % owners * share, share, 1)
        parts.append(shifted(send, step))
    both = jnp.concatenate(parts)
    query_heads, keyval_heads = both[..., : 2 * HD], both[..., 2 * HD :]
    plen = keyval_heads.shape[0]
    where_at = step_rows(jnp.arange(plen, dtype=jnp.int32), rows)
    placing = step_rows(page_order[0], rows)[None, :] == jnp.arange(plen, dtype=jnp.int32)[:, None]
    kv_cache = jnp.einsum(
        "rs,skd->rkd", placing.astype(jnp.bfloat16), keyval_heads, preferred_element_type=jnp.float32
    ).astype(jnp.bfloat16)
    seg_rows = step_rows(seg, rows)
    heads_out = attend(query_heads, keyval_heads, seg_rows, seg_rows, where_at, where_at)
    attention = jnp.dot(heads_out, w_out, preferred_element_type=jnp.float32).astype(jnp.bfloat16)
    attention = exchange_sum(attention.reshape(owners, rows, width))
    resid = tokens.astype(jnp.float32) + attention
    normed2 = rms_scale(resid, norm_moe)
    packed = routing(normed2, expert_ids, w_router)
    experts = w_router.shape[1]
    own = expert_front(packed, 1, width, experts, w_gate, w_up)
    received = jnp.concatenate([shifted(packed, step) for step in range(1, owners)])
    others = expert_front(received, owners - 1, width, experts, w_gate, w_up)
    pieces = expert_back(*others, w_down, 2)
    own, pieces = lax.optimization_barrier((own, pieces))
    backs = []
    for piece in pieces:
        piece = piece.astype(jnp.bfloat16).reshape(owners - 1, rows, -1)
        back = sum(
            shifted(piece[step - 1], -step).astype(jnp.float32) for step in range(1, owners)
        )
        backs.append(back)
    moe = expert_back(*own, w_down, 1)[0] + jnp.concatenate(backs, axis=1)
    mixed = (resid + moe).astype(jnp.bfloat16)
    return (mixed, kv_cache)


def solution(mesh):
    placed = (
        P(("req", "exp"), None),
        P(),
        P(),
        P(),
        P(),
        P("exp", None),
        P(),
        P(),
        P("exp", None, None),
        P("exp", None, None),
        P("exp", None, None),
        P("req", None),
        P("req", None),
        P(("req", "exp"), None),
    )
    return jax.shard_map(
        shards,
        mesh=mesh,
        in_specs=placed,
        out_specs=(P(("req", "exp"), None), P("req", "exp", None)),
        check_vma=False,
    )
```

```python
import jax
import jax.numpy as jnp
from jax import lax
from jax.sharding import PartitionSpec as P

HD = 64
CAP = 64


def rms_scale(rows, gain):
    rows = rows.astype(jnp.float32)
    inverse = lax.rsqrt(jnp.mean(rows * rows, axis=-1, keepdims=True) + 1e-06)
    return (rows * inverse * gain.astype(jnp.float32)).astype(jnp.bfloat16)


def positions(seg):
    index = jnp.arange(seg.shape[0], dtype=jnp.int32)
    starts = jnp.concatenate([jnp.ones((1,), dtype=bool), seg[1:] != seg[:-1]])
    first = lax.cummax(jnp.where(starts, index, 0), axis=0)
    return index - first


def rotate(values, pos):
    half = values.shape[-1] // 2
    freq = 10000.0 ** (-jnp.arange(half, dtype=jnp.float32) / half)
    angle = pos.astype(jnp.float32)[:, None] * freq[None, :]
    cosine = jnp.cos(angle)[:, None, :]
    sine = jnp.sin(angle)[:, None, :]
    front = values[..., :half]
    back = values[..., half:]
    return jnp.concatenate([front * cosine - back * sine, back * cosine + front * sine], axis=-1)


def attend(query, keyval, query_seg, seg, query_at, where_at):
    plen, groups, width = query.shape
    half = width // 2
    queries = query.reshape(plen, groups, 2, half)
    keys = keyval[..., :half]
    values = keyval[..., half:]
    score = jnp.einsum("qkgd,tkd->kgqt", queries, keys, preferred_element_type=jnp.float32) * 0.125
    allowed = (query_seg[:, None] == seg[None, :]) & (where_at[None, :] <= query_at[:, None])
    score = jnp.where(allowed[None, None], score, -1e30)
    top = jnp.max(score, axis=-1, keepdims=True)
    expo = jnp.exp(score - top)
    probs = (expo / jnp.sum(expo, axis=-1, keepdims=True)).astype(jnp.bfloat16)
    out = jnp.einsum("kgqt,tkd->qkgd", probs, values, preferred_element_type=jnp.float32)
    return out.astype(jnp.bfloat16).reshape(plen, groups * width)


def routing(normed2, ids, w_router):
    experts = w_router.shape[1]
    logits = jnp.dot(normed2, w_router, preferred_element_type=jnp.float32)
    match = ids[:, :, None] == jnp.arange(experts, dtype=jnp.int32)
    chosen = jnp.sum(jnp.where(match, logits[:, None, :], 0.0), axis=2)
    weights = jax.nn.softmax(chosen, axis=-1)
    dense = jnp.sum(jnp.where(match, weights[:, :, None], 0.0), axis=1)
    high = dense.astype(jnp.bfloat16)
    low = (dense - high.astype(jnp.float32)).astype(jnp.bfloat16)
    named = jnp.any(match, axis=1).astype(jnp.bfloat16)
    pad = (-3 * experts) % 128
    fill = jnp.zeros((normed2.shape[0], pad), jnp.bfloat16)
    return jnp.concatenate([normed2, high, low, named, fill], axis=1)


def expert_mix(packed, sources, width, experts, w_gate, w_up, w_down, pieces):
    tokens_all = packed.shape[0]
    local = w_gate.shape[0]
    rows = tokens_all // sources
    cap = CAP * sources
    here = lax.axis_index("exp")
    rows_all = packed[:, :width]

    def columns(block):
        return lax.dynamic_slice_in_dim(packed, width + block * experts + here * local, local, 1)

    high, low, named = columns(0), columns(1), columns(2)
    hits = named > 0
    order = jnp.arange(tokens_all, dtype=jnp.int32)
    block = order // rows
    before = (order[None, :] < order[:, None]) & (block[None, :] == block[:, None])
    slot = jnp.dot(before.astype(jnp.bfloat16), named, preferred_element_type=jnp.float32)
    slot = slot.astype(jnp.int32) + (block * CAP)[:, None]
    picks = hits.T[:, None, :] & (
        slot.T[:, None, :] == jnp.arange(cap, dtype=jnp.int32)[None, :, None]
    )
    received = jnp.einsum(
        "est,td->esd", picks.astype(jnp.bfloat16), rows_all, preferred_element_type=jnp.float32
    ).astype(jnp.bfloat16)
    gate = jnp.einsum("esd,edf->esf", received, w_gate, preferred_element_type=jnp.float32)
    upward = jnp.einsum("esd,edf->esf", received, w_up, preferred_element_type=jnp.float32)
    hidden = (jax.nn.silu(gate) * upward).astype(jnp.bfloat16)
    zero = jnp.zeros((), jnp.bfloat16)
    high = jnp.where(picks, high.T[:, None, :], zero)
    low = jnp.where(picks, low.T[:, None, :], zero)
    cut = w_down.shape[2] // pieces
    outs = []
    for piece in range(pieces):
        down = lax.slice_in_dim(w_down, piece * cut, (piece + 1) * cut, axis=2)
        result = jnp.einsum("esf,efd->esd", hidden, down, preferred_element_type=jnp.float32)
        result = result.astype(jnp.bfloat16)
        partial = jnp.einsum("est,esd->td", high, result, preferred_element_type=jnp.float32)
        partial = partial + jnp.einsum(
            "est,esd->td", low, result, preferred_element_type=jnp.float32
        )
        outs.append(partial)
    return outs


def shifted(x, step):
    count = lax.axis_size("exp")
    return lax.ppermute(x, "exp", [(j, (j + step) % count) for j in range(count)])


def exchange_sum(blocks):
    total = blocks[0].astype(jnp.float32)
    for step in range(1, blocks.shape[0]):
        total = total + shifted(blocks[step], -step).astype(jnp.float32)
    return total


def step_rows(x, rows):
    count = lax.axis_size("exp")
    here = lax.axis_index("exp")
    parts = [
        lax.dynamic_slice_in_dim(x, (here - step) % count * rows, rows) for step in range(count)
    ]
    return jnp.concatenate(parts)


def gather_w_out(w_out):
    count = lax.axis_size("exp")
    mates = lax.axis_size("req")
    part = lax.axis_index("req") % 2
    cut = w_out.shape[0] // 2
    mine = lax.dynamic_slice_in_dim(w_out, part * cut, cut, 0)
    got = jnp.stack([shifted(mine, step) for step in range(1, count)])
    other = lax.ppermute(got, "req", [(j, j ^ 1) for j in range(mates)])
    lower = jnp.where(part == 0, got, other)
    upper = jnp.where(part == 0, other, got)
    return jnp.concatenate([lower, upper], axis=1)


def shards(
    tokens,
    norm_attn,
    w_query,
    w_key,
    w_value,
    w_out,
    norm_moe,
    w_router,
    w_gate,
    w_up,
    w_down,
    segment_ids,
    page_order,
    expert_ids,
):
    rows, width = tokens.shape
    seg = segment_ids[0]
    groups = w_key.shape[1] // HD
    here = lax.axis_index("exp")
    pos = lax.dynamic_slice_in_dim(positions(seg), here * rows, rows)
    normed = rms_scale(tokens, norm_attn)
    query = jnp.dot(normed, w_query, preferred_element_type=jnp.float32).reshape(
        rows, 2 * groups, HD
    )
    query = rotate(query, pos).astype(jnp.bfloat16).reshape(rows, groups, 2 * HD)
    keys = jnp.dot(normed, w_key, preferred_element_type=jnp.float32).reshape(rows, groups, HD)
    keys = rotate(keys, pos).astype(jnp.bfloat16)
    values = (
        jnp.dot(normed, w_value, preferred_element_type=jnp.float32)
        .astype(jnp.bfloat16)
        .reshape(rows, groups, HD)
    )
    keyval = jnp.concatenate([keys, values], axis=-1)
    owners = lax.axis_size("exp")
    share = groups // owners
    both = jnp.concatenate([query, keyval], axis=-1)
    parts = [lax.dynamic_slice_in_dim(both, here * share, share, 1)]
    for step in range(1, owners):
        send = lax.dynamic_slice_in_dim(both, (here + step) % owners * share, share, 1)
        parts.append(shifted(send, step))
    both = jnp.concatenate(parts)
    query_heads, keyval_heads = both[..., : 2 * HD], both[..., 2 * HD :]
    plen = keyval_heads.shape[0]
    where_at = step_rows(jnp.arange(plen, dtype=jnp.int32), rows)
    placing = step_rows(page_order[0], rows)[None, :] == jnp.arange(plen, dtype=jnp.int32)[:, None]
    kv_cache = jnp.einsum(
        "rs,skd->rkd", placing.astype(jnp.bfloat16), keyval_heads, preferred_element_type=jnp.float32
    ).astype(jnp.bfloat16)
    seg_rows = step_rows(seg, rows)
    heads_out = attend(query_heads, keyval_heads, seg_rows, seg_rows, where_at, where_at)
    blocks = heads_out.reshape(owners, rows, -1)
    remote = gather_w_out(w_out)
    attention = jnp.dot(blocks[0], w_out, preferred_element_type=jnp.float32)
    for step in range(1, owners):
        got = shifted(blocks[step], -step)
        attention = attention + jnp.dot(
            got, remote[owners - step - 1], preferred_element_type=jnp.float32
        )
    resid = tokens.astype(jnp.float32) + attention
    normed2 = rms_scale(resid, norm_moe)
    packed = routing(normed2, expert_ids, w_router)
    experts = w_router.shape[1]
    moe = expert_mix(packed, 1, width, experts, w_gate, w_up, w_down, 1)[0]
    received = jnp.concatenate([shifted(packed, step) for step in range(1, owners)])
    pieces = expert_mix(received, owners - 1, width, experts, w_gate, w_up, w_down, 2)
    backs = []
    for piece in pieces:
        piece = piece.astype(jnp.bfloat16).reshape(owners - 1, rows, -1)
        back = sum(
            shifted(piece[step - 1], -step).astype(jnp.float32) for step in range(1, owners)
        )
        backs.append(back)
    moe = moe + jnp.concatenate(backs, axis=1)
    mixed = (resid + moe).astype(jnp.bfloat16)
    return (mixed, kv_cache)


def solution(mesh):
    placed = (
        P(("req", "exp"), None),
        P(),
        P(),
        P(),
        P(),
        P("exp", None),
        P(),
        P(),
        P("exp", None, None),
        P("exp", None, None),
        P("exp", None, None),
        P("req", None),
        P("req", None),
        P(("req", "exp"), None),
    )
    return jax.shard_map(
        shards,
        mesh=mesh,
        in_specs=placed,
        out_specs=(P(("req", "exp"), None), P("req", "exp", None)),
        check_vma=False,
    )
```

```python
import jax
import jax.numpy as jnp
from jax import lax
from jax.sharding import PartitionSpec as P

HD = 64
CAP = 64


def rms_scale(rows, gain):
    rows = rows.astype(jnp.float32)
    inverse = lax.rsqrt(jnp.mean(rows * rows, axis=-1, keepdims=True) + 1e-06)
    return (rows * inverse * gain.astype(jnp.float32)).astype(jnp.bfloat16)


def positions(seg):
    index = jnp.arange(seg.shape[0], dtype=jnp.int32)
    starts = jnp.concatenate([jnp.ones((1,), dtype=bool), seg[1:] != seg[:-1]])
    first = lax.cummax(jnp.where(starts, index, 0), axis=0)
    return index - first


def rotate(values, pos):
    half = values.shape[-1] // 2
    freq = 10000.0 ** (-jnp.arange(half, dtype=jnp.float32) / half)
    angle = pos.astype(jnp.float32)[:, None] * freq[None, :]
    cosine = jnp.cos(angle)[:, None, :]
    sine = jnp.sin(angle)[:, None, :]
    front = values[..., :half]
    back = values[..., half:]
    return jnp.concatenate([front * cosine - back * sine, back * cosine + front * sine], axis=-1)


def attend(query, keyval, query_seg, seg, query_at, where_at):
    plen, groups, width = query.shape
    half = width // 2
    queries = query.reshape(plen, groups, 2, half)
    keys = keyval[..., :half]
    values = keyval[..., half:]
    score = jnp.einsum("qkgd,tkd->kgqt", queries, keys, preferred_element_type=jnp.float32) * 0.125
    allowed = (query_seg[:, None] == seg[None, :]) & (where_at[None, :] <= query_at[:, None])
    score = jnp.where(allowed[None, None], score, -1e30)
    top = jnp.max(score, axis=-1, keepdims=True)
    expo = jnp.exp(score - top)
    probs = (expo / jnp.sum(expo, axis=-1, keepdims=True)).astype(jnp.bfloat16)
    out = jnp.einsum("kgqt,tkd->qkgd", probs, values, preferred_element_type=jnp.float32)
    return out.astype(jnp.bfloat16).reshape(plen, groups * width)


def routing(normed2, ids, w_router):
    experts = w_router.shape[1]
    logits = jnp.dot(normed2, w_router, preferred_element_type=jnp.float32)
    match = ids[:, :, None] == jnp.arange(experts, dtype=jnp.int32)
    chosen = jnp.sum(jnp.where(match, logits[:, None, :], 0.0), axis=2)
    weights = jax.nn.softmax(chosen, axis=-1)
    dense = jnp.sum(jnp.where(match, weights[:, :, None], 0.0), axis=1)
    high = dense.astype(jnp.bfloat16)
    low = (dense - high.astype(jnp.float32)).astype(jnp.bfloat16)
    named = jnp.any(match, axis=1).astype(jnp.bfloat16)
    pad = (-3 * experts) % 128
    fill = jnp.zeros((normed2.shape[0], pad), jnp.bfloat16)
    return jnp.concatenate([normed2, high, low, named, fill], axis=1)


def expert_mix(packed, sources, width, experts, w_gate, w_up, w_down, pieces):
    tokens_all = packed.shape[0]
    local = w_gate.shape[0]
    rows = tokens_all // sources
    cap = CAP * sources
    here = lax.axis_index("exp")
    rows_all = packed[:, :width]

    def columns(block):
        return lax.dynamic_slice_in_dim(packed, width + block * experts + here * local, local, 1)

    high, low, named = columns(0), columns(1), columns(2)
    hits = named > 0
    order = jnp.arange(tokens_all, dtype=jnp.int32)
    block = order // rows
    before = (order[None, :] < order[:, None]) & (block[None, :] == block[:, None])
    slot = jnp.dot(before.astype(jnp.bfloat16), named, preferred_element_type=jnp.float32)
    slot = slot.astype(jnp.int32) + (block * CAP)[:, None]
    picks = hits.T[:, None, :] & (
        slot.T[:, None, :] == jnp.arange(cap, dtype=jnp.int32)[None, :, None]
    )
    received = jnp.einsum(
        "est,td->esd", picks.astype(jnp.bfloat16), rows_all, preferred_element_type=jnp.float32
    ).astype(jnp.bfloat16)
    gate = jnp.einsum("esd,edf->esf", received, w_gate, preferred_element_type=jnp.float32)
    upward = jnp.einsum("esd,edf->esf", received, w_up, preferred_element_type=jnp.float32)
    hidden = (jax.nn.silu(gate) * upward).astype(jnp.bfloat16)
    zero = jnp.zeros((), jnp.bfloat16)
    high = jnp.where(picks, high.T[:, None, :], zero)
    low = jnp.where(picks, low.T[:, None, :], zero)
    cut = w_down.shape[2] // pieces
    outs = []
    for piece in range(pieces):
        down = lax.slice_in_dim(w_down, piece * cut, (piece + 1) * cut, axis=2)
        result = jnp.einsum("esf,efd->esd", hidden, down, preferred_element_type=jnp.float32)
        result = result.astype(jnp.bfloat16)
        partial = jnp.einsum("est,esd->td", high, result, preferred_element_type=jnp.float32)
        partial = partial + jnp.einsum(
            "est,esd->td", low, result, preferred_element_type=jnp.float32
        )
        outs.append(partial)
    return outs


def shifted(x, step):
    count = lax.axis_size("exp")
    return lax.ppermute(x, "exp", [(j, (j + step) % count) for j in range(count)])


def exchange_sum(blocks):
    total = blocks[0].astype(jnp.float32)
    for step in range(1, blocks.shape[0]):
        total = total + shifted(blocks[step], -step).astype(jnp.float32)
    return total


def step_rows(x, rows):
    count = lax.axis_size("exp")
    here = lax.axis_index("exp")
    parts = [
        lax.dynamic_slice_in_dim(x, (here - step) % count * rows, rows) for step in range(count)
    ]
    return jnp.concatenate(parts)


def gather_w_out(w_out):
    count = lax.axis_size("exp")
    mates = lax.axis_size("req")
    part = lax.axis_index("req") % 2
    cut = w_out.shape[0] // 2
    mine = lax.dynamic_slice_in_dim(w_out, part * cut, cut, 0)
    got = jnp.stack([shifted(mine, step) for step in range(1, count)])
    other = lax.ppermute(got, "req", [(j, j ^ 1) for j in range(mates)])
    lower = jnp.where(part == 0, got, other)
    upper = jnp.where(part == 0, other, got)
    return jnp.concatenate([lower, upper], axis=1)


def shards(
    tokens,
    norm_attn,
    w_query,
    w_key,
    w_value,
    w_out,
    norm_moe,
    w_router,
    w_gate,
    w_up,
    w_down,
    segment_ids,
    page_order,
    expert_ids,
):
    rows, width = tokens.shape
    seg = segment_ids[0]
    groups = w_key.shape[1] // HD
    here = lax.axis_index("exp")
    pos = lax.dynamic_slice_in_dim(positions(seg), here * rows, rows)
    normed = rms_scale(tokens, norm_attn)
    query = jnp.dot(normed, w_query, preferred_element_type=jnp.float32).reshape(
        rows, 2 * groups, HD
    )
    query = rotate(query, pos).astype(jnp.bfloat16).reshape(rows, groups, 2 * HD)
    keys = jnp.dot(normed, w_key, preferred_element_type=jnp.float32).reshape(rows, groups, HD)
    keys = rotate(keys, pos).astype(jnp.bfloat16)
    values = (
        jnp.dot(normed, w_value, preferred_element_type=jnp.float32)
        .astype(jnp.bfloat16)
        .reshape(rows, groups, HD)
    )
    keyval = jnp.concatenate([keys, values], axis=-1)
    owners = lax.axis_size("exp")
    share = groups // owners
    both = jnp.concatenate([query, keyval], axis=-1)
    remote = gather_w_out(lax.optimization_barrier((w_out, both))[0])
    parts = [lax.dynamic_slice_in_dim(both, here * share, share, 1)]
    for step in range(1, owners):
        send = lax.dynamic_slice_in_dim(both, (here + step) % owners * share, share, 1)
        parts.append(shifted(send, step))
    both = jnp.concatenate(parts)
    query_heads, keyval_heads = both[..., : 2 * HD], both[..., 2 * HD :]
    plen = keyval_heads.shape[0]
    where_at = step_rows(jnp.arange(plen, dtype=jnp.int32), rows)
    placing = step_rows(page_order[0], rows)[None, :] == jnp.arange(plen, dtype=jnp.int32)[:, None]
    kv_cache = jnp.einsum(
        "rs,skd->rkd", placing.astype(jnp.bfloat16), keyval_heads, preferred_element_type=jnp.float32
    ).astype(jnp.bfloat16)
    seg_rows = step_rows(seg, rows)
    heads_out = attend(query_heads, keyval_heads, seg_rows, seg_rows, where_at, where_at)
    blocks = heads_out.reshape(owners, rows, -1)
    attention = jnp.dot(blocks[0], w_out, preferred_element_type=jnp.float32)
    for step in range(1, owners):
        got = shifted(blocks[step], -step)
        attention = attention + jnp.dot(
            got, remote[owners - step - 1], preferred_element_type=jnp.float32
        )
    resid = tokens.astype(jnp.float32) + attention
    normed2 = rms_scale(resid, norm_moe)
    packed = routing(normed2, expert_ids, w_router)
    experts = w_router.shape[1]
    moe = expert_mix(packed, 1, width, experts, w_gate, w_up, w_down, 1)[0]
    received = jnp.concatenate([shifted(packed, step) for step in range(1, owners)])
    pieces = expert_mix(received, owners - 1, width, experts, w_gate, w_up, w_down, 2)
    backs = []
    for piece in pieces:
        piece = piece.astype(jnp.bfloat16).reshape(owners - 1, rows, -1)
        back = sum(
            shifted(piece[step - 1], -step).astype(jnp.float32) for step in range(1, owners)
        )
        backs.append(back)
    moe = moe + jnp.concatenate(backs, axis=1)
    mixed = (resid + moe).astype(jnp.bfloat16)
    return (mixed, kv_cache)


def solution(mesh):
    placed = (
        P(("req", "exp"), None),
        P(),
        P(),
        P(),
        P(),
        P("exp", None),
        P(),
        P(),
        P("exp", None, None),
        P("exp", None, None),
        P("exp", None, None),
        P("req", None),
        P("req", None),
        P(("req", "exp"), None),
    )
    return jax.shard_map(
        shards,
        mesh=mesh,
        in_specs=placed,
        out_specs=(P(("req", "exp"), None), P("req", "exp", None)),
        check_vma=False,
    )
```

```python
import jax
import jax.numpy as jnp
from jax import lax
from jax.sharding import PartitionSpec as P

HD = 64
CAP = 64


def rms_scale(rows, gain):
    rows = rows.astype(jnp.float32)
    inverse = lax.rsqrt(jnp.mean(rows * rows, axis=-1, keepdims=True) + 1e-06)
    return (rows * inverse * gain.astype(jnp.float32)).astype(jnp.bfloat16)


def positions(seg):
    index = jnp.arange(seg.shape[0], dtype=jnp.int32)
    starts = jnp.concatenate([jnp.ones((1,), dtype=bool), seg[1:] != seg[:-1]])
    first = lax.cummax(jnp.where(starts, index, 0), axis=0)
    return index - first


def rotate(values, pos):
    half = values.shape[-1] // 2
    freq = 10000.0 ** (-jnp.arange(half, dtype=jnp.float32) / half)
    angle = pos.astype(jnp.float32)[:, None] * freq[None, :]
    cosine = jnp.cos(angle)[:, None, :]
    sine = jnp.sin(angle)[:, None, :]
    front = values[..., :half]
    back = values[..., half:]
    return jnp.concatenate([front * cosine - back * sine, back * cosine + front * sine], axis=-1)


def attend(query, keyval, query_seg, seg, query_at, where_at):
    plen, groups, width = query.shape
    half = width // 2
    queries = query.reshape(plen, groups, 2, half)
    keys = keyval[..., :half]
    values = keyval[..., half:]
    score = jnp.einsum("qkgd,tkd->kgqt", queries, keys, preferred_element_type=jnp.float32) * 0.125
    allowed = (query_seg[:, None] == seg[None, :]) & (where_at[None, :] <= query_at[:, None])
    score = jnp.where(allowed[None, None], score, -1e30)
    top = jnp.max(score, axis=-1, keepdims=True)
    expo = jnp.exp(score - top)
    probs = (expo / jnp.sum(expo, axis=-1, keepdims=True)).astype(jnp.bfloat16)
    out = jnp.einsum("kgqt,tkd->qkgd", probs, values, preferred_element_type=jnp.float32)
    return out.astype(jnp.bfloat16).reshape(plen, groups * width)


def routing(normed2, ids, w_router):
    experts = w_router.shape[1]
    logits = jnp.dot(normed2, w_router, preferred_element_type=jnp.float32)
    match = ids[:, :, None] == jnp.arange(experts, dtype=jnp.int32)
    chosen = jnp.sum(jnp.where(match, logits[:, None, :], 0.0), axis=2)
    weights = jax.nn.softmax(chosen, axis=-1)
    dense = jnp.sum(jnp.where(match, weights[:, :, None], 0.0), axis=1)
    high = dense.astype(jnp.bfloat16)
    low = (dense - high.astype(jnp.float32)).astype(jnp.bfloat16)
    named = jnp.any(match, axis=1).astype(jnp.bfloat16)
    pad = (-3 * experts) % 128
    fill = jnp.zeros((normed2.shape[0], pad), jnp.bfloat16)
    return jnp.concatenate([normed2, high, low, named, fill], axis=1)


def expert_mix(packed, sources, width, experts, w_gate, w_up, w_down, pieces):
    tokens_all = packed.shape[0]
    local = w_gate.shape[0]
    rows = tokens_all // sources
    cap = CAP * sources
    here = lax.axis_index("exp")
    rows_all = packed[:, :width]

    def columns(block):
        return lax.dynamic_slice_in_dim(packed, width + block * experts + here * local, local, 1)

    high, low, named = columns(0), columns(1), columns(2)
    hits = named > 0
    order = jnp.arange(tokens_all, dtype=jnp.int32)
    block = order // rows
    before = (order[None, :] < order[:, None]) & (block[None, :] == block[:, None])
    slot = jnp.dot(before.astype(jnp.bfloat16), named, preferred_element_type=jnp.float32)
    slot = slot.astype(jnp.int32) + (block * CAP)[:, None]
    picks = hits.T[:, None, :] & (
        slot.T[:, None, :] == jnp.arange(cap, dtype=jnp.int32)[None, :, None]
    )
    received = jnp.einsum(
        "est,td->esd", picks.astype(jnp.bfloat16), rows_all, preferred_element_type=jnp.float32
    ).astype(jnp.bfloat16)
    gate = jnp.einsum("esd,edf->esf", received, w_gate, preferred_element_type=jnp.float32)
    upward = jnp.einsum("esd,edf->esf", received, w_up, preferred_element_type=jnp.float32)
    hidden = (jax.nn.silu(gate) * upward).astype(jnp.bfloat16)
    zero = jnp.zeros((), jnp.bfloat16)
    high = jnp.where(picks, high.T[:, None, :], zero)
    low = jnp.where(picks, low.T[:, None, :], zero)
    cut = w_down.shape[2] // pieces
    results = []
    for piece in range(pieces):
        down = lax.slice_in_dim(w_down, piece * cut, (piece + 1) * cut, axis=2)
        result = jnp.einsum("esf,efd->esd", hidden, down, preferred_element_type=jnp.float32)
        results.append(result.astype(jnp.bfloat16))
    result = jnp.concatenate(results, axis=2)
    partial = jnp.einsum("est,esd->td", high, result, preferred_element_type=jnp.float32)
    partial = partial + jnp.einsum("est,esd->td", low, result, preferred_element_type=jnp.float32)
    return [partial]


def shifted(x, step):
    count = lax.axis_size("exp")
    return lax.ppermute(x, "exp", [(j, (j + step) % count) for j in range(count)])


def exchange_sum(blocks):
    total = blocks[0].astype(jnp.float32)
    for step in range(1, blocks.shape[0]):
        total = total + shifted(blocks[step], -step).astype(jnp.float32)
    return total


def step_rows(x, rows):
    count = lax.axis_size("exp")
    here = lax.axis_index("exp")
    parts = [
        lax.dynamic_slice_in_dim(x, (here - step) % count * rows, rows) for step in range(count)
    ]
    return jnp.concatenate(parts)


def gather_w_out(w_out):
    count = lax.axis_size("exp")
    mates = lax.axis_size("req")
    part = lax.axis_index("req") % 2
    cut = w_out.shape[0] // 2
    mine = lax.dynamic_slice_in_dim(w_out, part * cut, cut, 0)
    got = jnp.stack([shifted(mine, step) for step in range(1, count)])
    other = lax.ppermute(got, "req", [(j, j ^ 1) for j in range(mates)])
    lower = jnp.where(part == 0, got, other)
    upper = jnp.where(part == 0, other, got)
    return jnp.concatenate([lower, upper], axis=1)


def shards(
    tokens,
    norm_attn,
    w_query,
    w_key,
    w_value,
    w_out,
    norm_moe,
    w_router,
    w_gate,
    w_up,
    w_down,
    segment_ids,
    page_order,
    expert_ids,
):
    rows, width = tokens.shape
    seg = segment_ids[0]
    groups = w_key.shape[1] // HD
    here = lax.axis_index("exp")
    pos = lax.dynamic_slice_in_dim(positions(seg), here * rows, rows)
    normed = rms_scale(tokens, norm_attn)
    query = jnp.dot(normed, w_query, preferred_element_type=jnp.float32).reshape(
        rows, 2 * groups, HD
    )
    query = rotate(query, pos).astype(jnp.bfloat16).reshape(rows, groups, 2 * HD)
    keys = jnp.dot(normed, w_key, preferred_element_type=jnp.float32).reshape(rows, groups, HD)
    keys = rotate(keys, pos).astype(jnp.bfloat16)
    values = (
        jnp.dot(normed, w_value, preferred_element_type=jnp.float32)
        .astype(jnp.bfloat16)
        .reshape(rows, groups, HD)
    )
    keyval = jnp.concatenate([keys, values], axis=-1)
    owners = lax.axis_size("exp")
    share = groups // owners
    both = jnp.concatenate([query, keyval], axis=-1)
    parts = [lax.dynamic_slice_in_dim(both, here * share, share, 1)]
    for step in range(1, owners):
        send = lax.dynamic_slice_in_dim(both, (here + step) % owners * share, share, 1)
        parts.append(shifted(send, step))
    both = jnp.concatenate(parts)
    query_heads, keyval_heads = both[..., : 2 * HD], both[..., 2 * HD :]
    plen = keyval_heads.shape[0]
    where_at = step_rows(jnp.arange(plen, dtype=jnp.int32), rows)
    placing = step_rows(page_order[0], rows)[None, :] == jnp.arange(plen, dtype=jnp.int32)[:, None]
    kv_cache = jnp.einsum(
        "rs,skd->rkd", placing.astype(jnp.bfloat16), keyval_heads, preferred_element_type=jnp.float32
    ).astype(jnp.bfloat16)
    seg_rows = step_rows(seg, rows)
    heads_out = attend(query_heads, keyval_heads, seg_rows, seg_rows, where_at, where_at)
    blocks = heads_out.reshape(owners, rows, -1)
    remote = gather_w_out(w_out)
    attention = jnp.dot(blocks[0], w_out, preferred_element_type=jnp.float32)
    for step in range(1, owners):
        got = shifted(blocks[step], -step)
        attention = attention + jnp.dot(
            got, remote[owners - step - 1], preferred_element_type=jnp.float32
        )
    resid = tokens.astype(jnp.float32) + attention
    normed2 = rms_scale(resid, norm_moe)
    packed = routing(normed2, expert_ids, w_router)
    experts = w_router.shape[1]
    moe = expert_mix(packed, 1, width, experts, w_gate, w_up, w_down, 1)[0]
    received = jnp.concatenate([shifted(packed, step) for step in range(1, owners)])
    pieces = expert_mix(received, owners - 1, width, experts, w_gate, w_up, w_down, 2)
    backs = []
    for piece in pieces:
        piece = piece.astype(jnp.bfloat16).reshape(owners - 1, rows, -1)
        back = sum(
            shifted(piece[step - 1], -step).astype(jnp.float32) for step in range(1, owners)
        )
        backs.append(back)
    moe = moe + jnp.concatenate(backs, axis=1)
    mixed = (resid + moe).astype(jnp.bfloat16)
    return (mixed, kv_cache)


def solution(mesh):
    placed = (
        P(("req", "exp"), None),
        P(),
        P(),
        P(),
        P(),
        P("exp", None),
        P(),
        P(),
        P("exp", None, None),
        P("exp", None, None),
        P("exp", None, None),
        P("req", None),
        P("req", None),
        P(("req", "exp"), None),
    )
    return jax.shard_map(
        shards,
        mesh=mesh,
        in_specs=placed,
        out_specs=(P(("req", "exp"), None), P("req", "exp", None)),
        check_vma=False,
    )
```

```python
import jax
import jax.numpy as jnp
from jax import lax
from jax.sharding import PartitionSpec as P

HD = 64
CAP = 64


def rms_scale(rows, gain):
    rows = rows.astype(jnp.float32)
    inverse = lax.rsqrt(jnp.mean(rows * rows, axis=-1, keepdims=True) + 1e-06)
    return (rows * inverse * gain.astype(jnp.float32)).astype(jnp.bfloat16)


def positions(seg):
    index = jnp.arange(seg.shape[0], dtype=jnp.int32)
    starts = jnp.concatenate([jnp.ones((1,), dtype=bool), seg[1:] != seg[:-1]])
    first = lax.cummax(jnp.where(starts, index, 0), axis=0)
    return index - first


def rotate(values, pos):
    half = values.shape[-1] // 2
    freq = 10000.0 ** (-jnp.arange(half, dtype=jnp.float32) / half)
    angle = pos.astype(jnp.float32)[:, None] * freq[None, :]
    cosine = jnp.cos(angle)[:, None, :]
    sine = jnp.sin(angle)[:, None, :]
    front = values[..., :half]
    back = values[..., half:]
    return jnp.concatenate([front * cosine - back * sine, back * cosine + front * sine], axis=-1)


def attend(query, keyval, query_seg, seg, query_at, where_at):
    plen, groups, width = query.shape
    half = width // 2
    queries = query.reshape(plen, groups, 2, half)
    keys = keyval[..., :half]
    values = keyval[..., half:]
    score = jnp.einsum("qkgd,tkd->kgqt", queries, keys, preferred_element_type=jnp.float32) * 0.125
    allowed = (query_seg[:, None] == seg[None, :]) & (where_at[None, :] <= query_at[:, None])
    score = jnp.where(allowed[None, None], score, -1e30)
    top = jnp.max(score, axis=-1, keepdims=True)
    expo = jnp.exp(score - top)
    probs = (expo / jnp.sum(expo, axis=-1, keepdims=True)).astype(jnp.bfloat16)
    out = jnp.einsum("kgqt,tkd->qkgd", probs, values, preferred_element_type=jnp.float32)
    return out.astype(jnp.bfloat16).reshape(plen, groups * width)


def routing(normed2, ids, w_router):
    experts = w_router.shape[1]
    logits = jnp.dot(normed2, w_router, preferred_element_type=jnp.float32)
    match = ids[:, :, None] == jnp.arange(experts, dtype=jnp.int32)
    chosen = jnp.sum(jnp.where(match, logits[:, None, :], 0.0), axis=2)
    weights = jax.nn.softmax(chosen, axis=-1)
    dense = jnp.sum(jnp.where(match, weights[:, :, None], 0.0), axis=1)
    high = dense.astype(jnp.bfloat16)
    low = (dense - high.astype(jnp.float32)).astype(jnp.bfloat16)
    named = jnp.any(match, axis=1).astype(jnp.bfloat16)
    pad = (-3 * experts) % 128
    fill = jnp.zeros((normed2.shape[0], pad), jnp.bfloat16)
    return jnp.concatenate([normed2, high, low, named, fill], axis=1)


def expert_mix(packed, sources, width, experts, w_gate, w_up, w_down, pieces):
    local = w_gate.shape[0]
    rows = packed.shape[0] // sources
    here = lax.axis_index("exp")
    rows_all = packed[:, :width].reshape(sources, rows, width)

    def columns(block):
        start = width + block * experts + here * local
        return lax.dynamic_slice_in_dim(packed, start, local, 1).reshape(sources, rows, local)

    high, low, named = columns(0), columns(1), columns(2)
    order = jnp.arange(rows, dtype=jnp.int32)
    before = (order[None, :] < order[:, None]).astype(jnp.bfloat16)
    slot = jnp.einsum("tu,bue->bet", before, named, preferred_element_type=jnp.float32)
    hits = jnp.transpose(named, (0, 2, 1)) > 0
    picks = hits[:, :, None, :] & (
        slot.astype(jnp.int32)[:, :, None, :] == jnp.arange(CAP, dtype=jnp.int32)[None, None, :, None]
    )
    received = jnp.einsum(
        "becr,brd->becd", picks.astype(jnp.bfloat16), rows_all, preferred_element_type=jnp.float32
    ).astype(jnp.bfloat16)
    gate = jnp.einsum("becd,edf->becf", received, w_gate, preferred_element_type=jnp.float32)
    upward = jnp.einsum("becd,edf->becf", received, w_up, preferred_element_type=jnp.float32)
    hidden = (jax.nn.silu(gate) * upward).astype(jnp.bfloat16)
    zero = jnp.zeros((), jnp.bfloat16)
    high = jnp.where(picks, jnp.transpose(high, (0, 2, 1))[:, :, None, :], zero)
    low = jnp.where(picks, jnp.transpose(low, (0, 2, 1))[:, :, None, :], zero)
    cut = w_down.shape[2] // pieces
    outs = []
    for piece in range(pieces):
        down = lax.slice_in_dim(w_down, piece * cut, (piece + 1) * cut, axis=2)
        result = jnp.einsum("becf,efd->becd", hidden, down, preferred_element_type=jnp.float32)
        result = result.astype(jnp.bfloat16)
        partial = jnp.einsum("becr,becd->brd", high, result, preferred_element_type=jnp.float32)
        partial = partial + jnp.einsum(
            "becr,becd->brd", low, result, preferred_element_type=jnp.float32
        )
        outs.append(partial)
    return outs


def shifted(x, step):
    count = lax.axis_size("exp")
    return lax.ppermute(x, "exp", [(j, (j + step) % count) for j in range(count)])


def exchange_sum(blocks):
    total = blocks[0].astype(jnp.float32)
    for step in range(1, blocks.shape[0]):
        total = total + shifted(blocks[step], -step).astype(jnp.float32)
    return total


def step_rows(x, rows):
    count = lax.axis_size("exp")
    here = lax.axis_index("exp")
    parts = [
        lax.dynamic_slice_in_dim(x, (here - step) % count * rows, rows) for step in range(count)
    ]
    return jnp.concatenate(parts)


def gather_w_out(w_out):
    count = lax.axis_size("exp")
    mates = lax.axis_size("req")
    part = lax.axis_index("req") % 2
    cut = w_out.shape[0] // 2
    mine = lax.dynamic_slice_in_dim(w_out, part * cut, cut, 0)
    got = jnp.stack([shifted(mine, step) for step in range(1, count)])
    other = lax.ppermute(got, "req", [(j, j ^ 1) for j in range(mates)])
    lower = jnp.where(part == 0, got, other)
    upper = jnp.where(part == 0, other, got)
    return jnp.concatenate([lower, upper], axis=1)


def shards(
    tokens,
    norm_attn,
    w_query,
    w_key,
    w_value,
    w_out,
    norm_moe,
    w_router,
    w_gate,
    w_up,
    w_down,
    segment_ids,
    page_order,
    expert_ids,
):
    rows, width = tokens.shape
    seg = segment_ids[0]
    groups = w_key.shape[1] // HD
    here = lax.axis_index("exp")
    pos = lax.dynamic_slice_in_dim(positions(seg), here * rows, rows)
    normed = rms_scale(tokens, norm_attn)
    query = jnp.dot(normed, w_query, preferred_element_type=jnp.float32).reshape(
        rows, 2 * groups, HD
    )
    query = rotate(query, pos).astype(jnp.bfloat16).reshape(rows, groups, 2 * HD)
    keys = jnp.dot(normed, w_key, preferred_element_type=jnp.float32).reshape(rows, groups, HD)
    keys = rotate(keys, pos).astype(jnp.bfloat16)
    values = (
        jnp.dot(normed, w_value, preferred_element_type=jnp.float32)
        .astype(jnp.bfloat16)
        .reshape(rows, groups, HD)
    )
    keyval = jnp.concatenate([keys, values], axis=-1)
    owners = lax.axis_size("exp")
    share = groups // owners
    both = jnp.concatenate([query, keyval], axis=-1)
    parts = [lax.dynamic_slice_in_dim(both, here * share, share, 1)]
    for step in range(1, owners):
        send = lax.dynamic_slice_in_dim(both, (here + step) % owners * share, share, 1)
        parts.append(shifted(send, step))
    both = jnp.concatenate(parts)
    query_heads, keyval_heads = both[..., : 2 * HD], both[..., 2 * HD :]
    plen = keyval_heads.shape[0]
    where_at = step_rows(jnp.arange(plen, dtype=jnp.int32), rows)
    placing = step_rows(page_order[0], rows)[None, :] == jnp.arange(plen, dtype=jnp.int32)[:, None]
    kv_cache = jnp.einsum(
        "rs,skd->rkd", placing.astype(jnp.bfloat16), keyval_heads, preferred_element_type=jnp.float32
    ).astype(jnp.bfloat16)
    seg_rows = step_rows(seg, rows)
    heads_out = attend(query_heads, keyval_heads, seg_rows, seg_rows, where_at, where_at)
    blocks = heads_out.reshape(owners, rows, -1)
    remote = gather_w_out(w_out)
    attention = jnp.dot(blocks[0], w_out, preferred_element_type=jnp.float32)
    for step in range(1, owners):
        got = shifted(blocks[step], -step)
        attention = attention + jnp.dot(
            got, remote[owners - step - 1], preferred_element_type=jnp.float32
        )
    resid = tokens.astype(jnp.float32) + attention
    normed2 = rms_scale(resid, norm_moe)
    packed = routing(normed2, expert_ids, w_router)
    experts = w_router.shape[1]
    moe = expert_mix(packed, 1, width, experts, w_gate, w_up, w_down, 1)[0][0]
    received = jnp.concatenate([shifted(packed, step) for step in range(1, owners)])
    pieces = expert_mix(received, owners - 1, width, experts, w_gate, w_up, w_down, 2)
    backs = []
    for piece in pieces:
        piece = piece.astype(jnp.bfloat16)
        back = sum(
            shifted(piece[step - 1], -step).astype(jnp.float32) for step in range(1, owners)
        )
        backs.append(back)
    moe = moe + jnp.concatenate(backs, axis=1)
    mixed = (resid + moe).astype(jnp.bfloat16)
    return (mixed, kv_cache)


def solution(mesh):
    placed = (
        P(("req", "exp"), None),
        P(),
        P(),
        P(),
        P(),
        P("exp", None),
        P(),
        P(),
        P("exp", None, None),
        P("exp", None, None),
        P("exp", None, None),
        P("req", None),
        P("req", None),
        P(("req", "exp"), None),
    )
    return jax.shard_map(
        shards,
        mesh=mesh,
        in_specs=placed,
        out_specs=(P(("req", "exp"), None), P("req", "exp", None)),
        check_vma=False,
    )
```

```python
import jax
import jax.numpy as jnp
from jax import lax
from jax.sharding import PartitionSpec as P

HD = 64
CAP = 64


def rms_scale(rows, gain):
    rows = rows.astype(jnp.float32)
    inverse = lax.rsqrt(jnp.mean(rows * rows, axis=-1, keepdims=True) + 1e-06)
    return (rows * inverse * gain.astype(jnp.float32)).astype(jnp.bfloat16)


def positions(seg):
    index = jnp.arange(seg.shape[0], dtype=jnp.int32)
    starts = jnp.concatenate([jnp.ones((1,), dtype=bool), seg[1:] != seg[:-1]])
    first = lax.cummax(jnp.where(starts, index, 0), axis=0)
    return index - first


def rotate(values, pos):
    half = values.shape[-1] // 2
    freq = 10000.0 ** (-jnp.arange(half, dtype=jnp.float32) / half)
    angle = pos.astype(jnp.float32)[:, None] * freq[None, :]
    cosine = jnp.cos(angle)[:, None, :]
    sine = jnp.sin(angle)[:, None, :]
    front = values[..., :half]
    back = values[..., half:]
    return jnp.concatenate([front * cosine - back * sine, back * cosine + front * sine], axis=-1)


def attend(query, keyval, query_seg, seg, query_at, where_at):
    plen, groups, width = query.shape
    half = width // 2
    queries = query.reshape(plen, groups, 2, half)
    keys = keyval[..., :half]
    values = keyval[..., half:]
    score = jnp.einsum("qkgd,tkd->kgqt", queries, keys, preferred_element_type=jnp.float32) * 0.125
    allowed = (query_seg[:, None] == seg[None, :]) & (where_at[None, :] <= query_at[:, None])
    score = jnp.where(allowed[None, None], score, -1e30)
    top = jnp.max(score, axis=-1, keepdims=True)
    expo = jnp.exp(score - top)
    probs = (expo / jnp.sum(expo, axis=-1, keepdims=True)).astype(jnp.bfloat16)
    out = jnp.einsum("kgqt,tkd->qkgd", probs, values, preferred_element_type=jnp.float32)
    return out.astype(jnp.bfloat16).reshape(plen, groups * width)


def routing(normed2, ids, w_router):
    experts = w_router.shape[1]
    logits = jnp.dot(normed2, w_router, preferred_element_type=jnp.float32)
    match = ids[:, :, None] == jnp.arange(experts, dtype=jnp.int32)
    chosen = jnp.sum(jnp.where(match, logits[:, None, :], 0.0), axis=2)
    weights = jax.nn.softmax(chosen, axis=-1)
    dense = jnp.sum(jnp.where(match, weights[:, :, None], 0.0), axis=1)
    high = dense.astype(jnp.bfloat16)
    low = (dense - high.astype(jnp.float32)).astype(jnp.bfloat16)
    named = jnp.any(match, axis=1).astype(jnp.bfloat16)
    pad = (-3 * experts) % 128
    fill = jnp.zeros((normed2.shape[0], pad), jnp.bfloat16)
    return jnp.concatenate([normed2, high, low, named, fill], axis=1)


def expert_mix(packed, sources, width, experts, w_gate, w_up, w_down, pieces):
    local = w_gate.shape[0]
    rows = packed.shape[0] // sources
    here = lax.axis_index("exp")
    rows_all = packed[:, :width].reshape(sources, rows, width)

    def columns(block):
        start = width + block * experts + here * local
        return lax.dynamic_slice_in_dim(packed, start, local, 1).reshape(sources, rows, local)

    high, low, named = columns(0), columns(1), columns(2)
    order = jnp.arange(rows, dtype=jnp.int32)
    before = (order[None, :] < order[:, None]).astype(jnp.bfloat16)
    slot = jnp.einsum("tu,bue->bet", before, named, preferred_element_type=jnp.float32)
    hits = jnp.transpose(named, (0, 2, 1)) > 0
    picks = hits[:, :, None, :] & (
        slot.astype(jnp.int32)[:, :, None, :] == jnp.arange(CAP, dtype=jnp.int32)[None, None, :, None]
    )
    received = jnp.einsum(
        "becr,brd->becd", picks.astype(jnp.bfloat16), rows_all, preferred_element_type=jnp.float32
    ).astype(jnp.bfloat16)
    gate = jnp.einsum("becd,edf->becf", received, w_gate, preferred_element_type=jnp.float32)
    upward = jnp.einsum("becd,edf->becf", received, w_up, preferred_element_type=jnp.float32)
    hidden = (jax.nn.silu(gate) * upward).astype(jnp.bfloat16)
    zero = jnp.zeros((), jnp.bfloat16)
    high = jnp.where(picks, jnp.transpose(high, (0, 2, 1))[:, :, None, :], zero)
    low = jnp.where(picks, jnp.transpose(low, (0, 2, 1))[:, :, None, :], zero)
    cut = w_down.shape[2] // pieces
    outs = []
    for piece in range(pieces):
        if outs:
            outs, hidden = lax.optimization_barrier((outs, hidden))
        down = lax.slice_in_dim(w_down, piece * cut, (piece + 1) * cut, axis=2)
        result = jnp.einsum("becf,efd->becd", hidden, down, preferred_element_type=jnp.float32)
        result = result.astype(jnp.bfloat16)
        partial = jnp.einsum("becr,becd->brd", high, result, preferred_element_type=jnp.float32)
        partial = partial + jnp.einsum(
            "becr,becd->brd", low, result, preferred_element_type=jnp.float32
        )
        outs.append(partial)
    return outs


def shifted(x, step):
    count = lax.axis_size("exp")
    return lax.ppermute(x, "exp", [(j, (j + step) % count) for j in range(count)])


def exchange_sum(blocks):
    total = blocks[0].astype(jnp.float32)
    for step in range(1, blocks.shape[0]):
        total = total + shifted(blocks[step], -step).astype(jnp.float32)
    return total


def step_rows(x, rows):
    count = lax.axis_size("exp")
    here = lax.axis_index("exp")
    parts = [
        lax.dynamic_slice_in_dim(x, (here - step) % count * rows, rows) for step in range(count)
    ]
    return jnp.concatenate(parts)


def gather_w_out(w_out):
    count = lax.axis_size("exp")
    mates = lax.axis_size("req")
    part = lax.axis_index("req") % 2
    cut = w_out.shape[0] // 2
    mine = lax.dynamic_slice_in_dim(w_out, part * cut, cut, 0)
    got = jnp.stack([shifted(mine, step) for step in range(1, count)])
    other = lax.ppermute(got, "req", [(j, j ^ 1) for j in range(mates)])
    lower = jnp.where(part == 0, got, other)
    upper = jnp.where(part == 0, other, got)
    return jnp.concatenate([lower, upper], axis=1)


def shards(
    tokens,
    norm_attn,
    w_query,
    w_key,
    w_value,
    w_out,
    norm_moe,
    w_router,
    w_gate,
    w_up,
    w_down,
    segment_ids,
    page_order,
    expert_ids,
):
    rows, width = tokens.shape
    seg = segment_ids[0]
    groups = w_key.shape[1] // HD
    here = lax.axis_index("exp")
    pos = lax.dynamic_slice_in_dim(positions(seg), here * rows, rows)
    normed = rms_scale(tokens, norm_attn)
    query = jnp.dot(normed, w_query, preferred_element_type=jnp.float32).reshape(
        rows, 2 * groups, HD
    )
    query = rotate(query, pos).astype(jnp.bfloat16).reshape(rows, groups, 2 * HD)
    keys = jnp.dot(normed, w_key, preferred_element_type=jnp.float32).reshape(rows, groups, HD)
    keys = rotate(keys, pos).astype(jnp.bfloat16)
    values = (
        jnp.dot(normed, w_value, preferred_element_type=jnp.float32)
        .astype(jnp.bfloat16)
        .reshape(rows, groups, HD)
    )
    keyval = jnp.concatenate([keys, values], axis=-1)
    owners = lax.axis_size("exp")
    share = groups // owners
    both = jnp.concatenate([query, keyval], axis=-1)
    parts = [lax.dynamic_slice_in_dim(both, here * share, share, 1)]
    for step in range(1, owners):
        send = lax.dynamic_slice_in_dim(both, (here + step) % owners * share, share, 1)
        parts.append(shifted(send, step))
    both = jnp.concatenate(parts)
    query_heads, keyval_heads = both[..., : 2 * HD], both[..., 2 * HD :]
    plen = keyval_heads.shape[0]
    where_at = step_rows(jnp.arange(plen, dtype=jnp.int32), rows)
    placing = step_rows(page_order[0], rows)[None, :] == jnp.arange(plen, dtype=jnp.int32)[:, None]
    kv_cache = jnp.einsum(
        "rs,skd->rkd", placing.astype(jnp.bfloat16), keyval_heads, preferred_element_type=jnp.float32
    ).astype(jnp.bfloat16)
    seg_rows = step_rows(seg, rows)
    heads_out = attend(query_heads, keyval_heads, seg_rows, seg_rows, where_at, where_at)
    blocks = heads_out.reshape(owners, rows, -1)
    remote = gather_w_out(w_out)
    attention = jnp.dot(blocks[0], w_out, preferred_element_type=jnp.float32)
    for step in range(1, owners):
        got = shifted(blocks[step], -step)
        attention = attention + jnp.dot(
            got, remote[owners - step - 1], preferred_element_type=jnp.float32
        )
    resid = tokens.astype(jnp.float32) + attention
    normed2 = rms_scale(resid, norm_moe)
    packed = routing(normed2, expert_ids, w_router)
    experts = w_router.shape[1]
    moe = expert_mix(packed, 1, width, experts, w_gate, w_up, w_down, 1)[0][0]
    received = jnp.concatenate([shifted(packed, step) for step in range(1, owners)])
    pieces = expert_mix(received, owners - 1, width, experts, w_gate, w_up, w_down, 2)
    backs = []
    for piece in pieces:
        piece = piece.astype(jnp.bfloat16)
        back = sum(
            shifted(piece[step - 1], -step).astype(jnp.float32) for step in range(1, owners)
        )
        backs.append(back)
    moe = moe + jnp.concatenate(backs, axis=1)
    mixed = (resid + moe).astype(jnp.bfloat16)
    return (mixed, kv_cache)


def solution(mesh):
    placed = (
        P(("req", "exp"), None),
        P(),
        P(),
        P(),
        P(),
        P("exp", None),
        P(),
        P(),
        P("exp", None, None),
        P("exp", None, None),
        P("exp", None, None),
        P("req", None),
        P("req", None),
        P(("req", "exp"), None),
    )
    return jax.shard_map(
        shards,
        mesh=mesh,
        in_specs=placed,
        out_specs=(P(("req", "exp"), None), P("req", "exp", None)),
        check_vma=False,
    )
```

```python
import jax
import jax.numpy as jnp
from jax import lax
from jax.sharding import PartitionSpec as P

HD = 64
CAP = 64


def rms_scale(rows, gain):
    rows = rows.astype(jnp.float32)
    inverse = lax.rsqrt(jnp.mean(rows * rows, axis=-1, keepdims=True) + 1e-06)
    return (rows * inverse * gain.astype(jnp.float32)).astype(jnp.bfloat16)


def positions(seg):
    index = jnp.arange(seg.shape[0], dtype=jnp.int32)
    starts = jnp.concatenate([jnp.ones((1,), dtype=bool), seg[1:] != seg[:-1]])
    first = lax.cummax(jnp.where(starts, index, 0), axis=0)
    return index - first


def rotate(values, pos):
    half = values.shape[-1] // 2
    freq = 10000.0 ** (-jnp.arange(half, dtype=jnp.float32) / half)
    angle = pos.astype(jnp.float32)[:, None] * freq[None, :]
    cosine = jnp.cos(angle)[:, None, :]
    sine = jnp.sin(angle)[:, None, :]
    front = values[..., :half]
    back = values[..., half:]
    return jnp.concatenate([front * cosine - back * sine, back * cosine + front * sine], axis=-1)


def attend(query, keyval, query_seg, seg, query_at, where_at):
    plen, groups, width = query.shape
    half = width // 2
    queries = query.reshape(plen, groups, 2, half)
    keys = keyval[..., :half]
    values = keyval[..., half:]
    score = jnp.einsum("qkgd,tkd->kgqt", queries, keys, preferred_element_type=jnp.float32) * 0.125
    allowed = (query_seg[:, None] == seg[None, :]) & (where_at[None, :] <= query_at[:, None])
    score = jnp.where(allowed[None, None], score, -1e30)
    top = jnp.max(score, axis=-1, keepdims=True)
    expo = jnp.exp(score - top)
    probs = (expo / jnp.sum(expo, axis=-1, keepdims=True)).astype(jnp.bfloat16)
    out = jnp.einsum("kgqt,tkd->qkgd", probs, values, preferred_element_type=jnp.float32)
    return out.astype(jnp.bfloat16).reshape(plen, groups * width)


def routing(normed2, ids, w_router):
    experts = w_router.shape[1]
    logits = jnp.dot(normed2, w_router, preferred_element_type=jnp.float32)
    match = ids[:, :, None] == jnp.arange(experts, dtype=jnp.int32)
    chosen = jnp.sum(jnp.where(match, logits[:, None, :], 0.0), axis=2)
    weights = jax.nn.softmax(chosen, axis=-1)
    dense = jnp.sum(jnp.where(match, weights[:, :, None], 0.0), axis=1)
    high = dense.astype(jnp.bfloat16)
    low = (dense - high.astype(jnp.float32)).astype(jnp.bfloat16)
    named = jnp.any(match, axis=1).astype(jnp.bfloat16)
    pad = (-3 * experts) % 128
    fill = jnp.zeros((normed2.shape[0], pad), jnp.bfloat16)
    return jnp.concatenate([normed2, high, low, named, fill], axis=1)


def expert_mix(packed, sources, width, experts, w_gate, w_up, w_down, pieces):
    local = w_gate.shape[0]
    rows = packed.shape[0] // sources
    here = lax.axis_index("exp")
    rows_all = packed[:, :width].reshape(sources, rows, width)

    def columns(block):
        start = width + block * experts + here * local
        return lax.dynamic_slice_in_dim(packed, start, local, 1).reshape(sources, rows, local)

    high, low, named = columns(0), columns(1), columns(2)
    order = jnp.arange(rows, dtype=jnp.int32)
    before = (order[None, :] < order[:, None]).astype(jnp.bfloat16)
    slot = jnp.einsum("tu,bue->bet", before, named, preferred_element_type=jnp.float32)
    hits = jnp.transpose(named, (0, 2, 1)) > 0
    picks = hits[:, :, None, :] & (
        slot.astype(jnp.int32)[:, :, None, :] == jnp.arange(CAP, dtype=jnp.int32)[None, None, :, None]
    )
    received = jnp.einsum(
        "becr,brd->becd", picks.astype(jnp.bfloat16), rows_all, preferred_element_type=jnp.float32
    ).astype(jnp.bfloat16)
    gate = jnp.einsum("becd,edf->becf", received, w_gate, preferred_element_type=jnp.float32)
    upward = jnp.einsum("becd,edf->becf", received, w_up, preferred_element_type=jnp.float32)
    hidden = (jax.nn.silu(gate) * upward).astype(jnp.bfloat16)
    zero = jnp.zeros((), jnp.bfloat16)
    high = jnp.where(picks, jnp.transpose(high, (0, 2, 1))[:, :, None, :], zero)
    low = jnp.where(picks, jnp.transpose(low, (0, 2, 1))[:, :, None, :], zero)
    cut = w_down.shape[2] // pieces
    outs = []
    for piece in range(pieces):
        down = lax.slice_in_dim(w_down, piece * cut, (piece + 1) * cut, axis=2)
        result = jnp.einsum("becf,efd->becd", hidden, down, preferred_element_type=jnp.float32)
        result = result.astype(jnp.bfloat16)
        partial = jnp.einsum("becr,becd->brd", high, result, preferred_element_type=jnp.float32)
        partial = partial + jnp.einsum(
            "becr,becd->brd", low, result, preferred_element_type=jnp.float32
        )
        outs.append(partial)
    return outs


def shifted(x, step):
    count = lax.axis_size("exp")
    return lax.ppermute(x, "exp", [(j, (j + step) % count) for j in range(count)])


def exchange_sum(blocks):
    total = blocks[0].astype(jnp.float32)
    for step in range(1, blocks.shape[0]):
        total = total + shifted(blocks[step], -step).astype(jnp.float32)
    return total


def step_rows(x, rows):
    count = lax.axis_size("exp")
    here = lax.axis_index("exp")
    parts = [
        lax.dynamic_slice_in_dim(x, (here - step) % count * rows, rows) for step in range(count)
    ]
    return jnp.concatenate(parts)


def gather_w_out(w_out):
    count = lax.axis_size("exp")
    mates = lax.axis_size("req")
    part = lax.axis_index("req") % 2
    cut = w_out.shape[0] // 2
    mine = lax.dynamic_slice_in_dim(w_out, part * cut, cut, 0)
    got = jnp.stack([shifted(mine, step) for step in range(1, count)])
    other = lax.ppermute(got, "req", [(j, j ^ 1) for j in range(mates)])
    lower = jnp.where(part == 0, got, other)
    upper = jnp.where(part == 0, other, got)
    return jnp.concatenate([lower, upper], axis=1)


def shards(
    tokens,
    norm_attn,
    w_query,
    w_key,
    w_value,
    w_out,
    norm_moe,
    w_router,
    w_gate,
    w_up,
    w_down,
    segment_ids,
    page_order,
    expert_ids,
):
    rows, width = tokens.shape
    seg = segment_ids[0]
    groups = w_key.shape[1] // HD
    here = lax.axis_index("exp")
    pos = lax.dynamic_slice_in_dim(positions(seg), here * rows, rows)
    normed = rms_scale(tokens, norm_attn)
    query = jnp.dot(normed, w_query, preferred_element_type=jnp.float32).reshape(
        rows, 2 * groups, HD
    )
    query = rotate(query, pos).astype(jnp.bfloat16).reshape(rows, groups, 2 * HD)
    keys = jnp.dot(normed, w_key, preferred_element_type=jnp.float32).reshape(rows, groups, HD)
    keys = rotate(keys, pos).astype(jnp.bfloat16)
    values = (
        jnp.dot(normed, w_value, preferred_element_type=jnp.float32)
        .astype(jnp.bfloat16)
        .reshape(rows, groups, HD)
    )
    keyval = jnp.concatenate([keys, values], axis=-1)
    owners = lax.axis_size("exp")
    share = groups // owners
    plen = seg.shape[0]
    reach = min(owners - 1, -(-(plen // 2 - 1) // rows))
    remote = gather_w_out(w_out)
    parts = [lax.dynamic_slice_in_dim(keyval, here * share, share, 1)]
    for step in range(1, owners):
        send = lax.dynamic_slice_in_dim(keyval, (here + step) % owners * share, share, 1)
        parts.append(shifted(send, step))
    cache_rows = jnp.concatenate(parts)
    placing = step_rows(page_order[0], rows)[None, :] == jnp.arange(plen, dtype=jnp.int32)[:, None]
    kv_cache = jnp.einsum(
        "rs,skd->rkd", placing.astype(jnp.bfloat16), cache_rows, preferred_element_type=jnp.float32
    ).astype(jnp.bfloat16)
    index = jnp.arange(rows, dtype=jnp.int32)
    windows, key_at, key_seg = [keyval], [here * rows + index], [lax.dynamic_slice_in_dim(seg, here * rows, rows)]
    for back in range(1, reach + 1):
        pairs = [(j, j + back) for j in range(owners - back)]
        windows.append(lax.ppermute(keyval, "exp", pairs))
        start = (here - back) * rows
        key_at.append(jnp.where(here >= back, start + index, 4 * plen))
        key_seg.append(lax.dynamic_slice_in_dim(seg, jnp.maximum(start, 0), rows))
    heads_out = attend(
        query,
        jnp.concatenate(windows),
        key_seg[0],
        jnp.concatenate(key_seg),
        key_at[0],
        jnp.concatenate(key_at),
    )
    cols = heads_out.shape[1] // owners
    attention = jnp.dot(
        lax.dynamic_slice_in_dim(heads_out, here * cols, cols, 1),
        w_out,
        preferred_element_type=jnp.float32,
    )
    for step in range(1, owners):
        block = lax.dynamic_slice_in_dim(heads_out, (here - step) % owners * cols, cols, 1)
        attention = attention + jnp.dot(block, remote[step - 1], preferred_element_type=jnp.float32)
    resid = tokens.astype(jnp.float32) + attention
    normed2 = rms_scale(resid, norm_moe)
    packed = routing(normed2, expert_ids, w_router)
    experts = w_router.shape[1]
    moe = expert_mix(packed, 1, width, experts, w_gate, w_up, w_down, 1)[0][0]
    received = jnp.concatenate([shifted(packed, step) for step in range(1, owners)])
    pieces = expert_mix(received, owners - 1, width, experts, w_gate, w_up, w_down, 2)
    backs = []
    for piece in pieces:
        piece = piece.astype(jnp.bfloat16)
        back = sum(
            shifted(piece[step - 1], -step).astype(jnp.float32) for step in range(1, owners)
        )
        backs.append(back)
    moe = moe + jnp.concatenate(backs, axis=1)
    mixed = (resid + moe).astype(jnp.bfloat16)
    return (mixed, kv_cache)


def solution(mesh):
    placed = (
        P(("req", "exp"), None),
        P(),
        P(),
        P(),
        P(),
        P("exp", None),
        P(),
        P(),
        P("exp", None, None),
        P("exp", None, None),
        P("exp", None, None),
        P("req", None),
        P("req", None),
        P(("req", "exp"), None),
    )
    return jax.shard_map(
        shards,
        mesh=mesh,
        in_specs=placed,
        out_specs=(P(("req", "exp"), None), P("req", "exp", None)),
        check_vma=False,
    )
```

```python
import jax
import jax.numpy as jnp
from jax import lax
from jax.sharding import PartitionSpec as P

HD = 64
CAP = 64


def rms_scale(rows, gain):
    rows = rows.astype(jnp.float32)
    inverse = lax.rsqrt(jnp.mean(rows * rows, axis=-1, keepdims=True) + 1e-06)
    return (rows * inverse * gain.astype(jnp.float32)).astype(jnp.bfloat16)


def positions(seg):
    index = jnp.arange(seg.shape[0], dtype=jnp.int32)
    starts = jnp.concatenate([jnp.ones((1,), dtype=bool), seg[1:] != seg[:-1]])
    first = lax.cummax(jnp.where(starts, index, 0), axis=0)
    return index - first


def rotate(values, pos):
    half = values.shape[-1] // 2
    freq = 10000.0 ** (-jnp.arange(half, dtype=jnp.float32) / half)
    angle = pos.astype(jnp.float32)[:, None] * freq[None, :]
    cosine = jnp.cos(angle)[:, None, :]
    sine = jnp.sin(angle)[:, None, :]
    front = values[..., :half]
    back = values[..., half:]
    return jnp.concatenate([front * cosine - back * sine, back * cosine + front * sine], axis=-1)


def attend(query, keyval, query_seg, seg, query_at, where_at):
    plen, groups, width = query.shape
    half = width // 2
    queries = query.reshape(plen, groups, 2, half)
    keys = keyval[..., :half]
    values = keyval[..., half:]
    score = jnp.einsum("qkgd,tkd->kgqt", queries, keys, preferred_element_type=jnp.float32) * 0.125
    allowed = (query_seg[:, None] == seg[None, :]) & (where_at[None, :] <= query_at[:, None])
    score = jnp.where(allowed[None, None], score, -1e30)
    top = jnp.max(score, axis=-1, keepdims=True)
    expo = jnp.exp(score - top)
    probs = (expo / jnp.sum(expo, axis=-1, keepdims=True)).astype(jnp.bfloat16)
    out = jnp.einsum("kgqt,tkd->qkgd", probs, values, preferred_element_type=jnp.float32)
    return out.astype(jnp.bfloat16).reshape(plen, groups * width)


def routing(normed2, ids, w_router):
    experts = w_router.shape[1]
    logits = jnp.dot(normed2, w_router, preferred_element_type=jnp.float32)
    match = ids[:, :, None] == jnp.arange(experts, dtype=jnp.int32)
    chosen = jnp.sum(jnp.where(match, logits[:, None, :], 0.0), axis=2)
    weights = jax.nn.softmax(chosen, axis=-1)
    dense = jnp.sum(jnp.where(match, weights[:, :, None], 0.0), axis=1)
    high = dense.astype(jnp.bfloat16)
    low = (dense - high.astype(jnp.float32)).astype(jnp.bfloat16)
    named = jnp.any(match, axis=1).astype(jnp.bfloat16)
    pad = (-3 * experts) % 128
    fill = jnp.zeros((normed2.shape[0], pad), jnp.bfloat16)
    return jnp.concatenate([normed2, high, low, named, fill], axis=1)


def expert_mix(packed, sources, width, experts, w_gate, w_up, w_down, pieces):
    local = w_gate.shape[0]
    rows = packed.shape[0] // sources
    here = lax.axis_index("exp")
    rows_all = packed[:, :width].reshape(sources, rows, width)

    def columns(block):
        start = width + block * experts + here * local
        return lax.dynamic_slice_in_dim(packed, start, local, 1).reshape(sources, rows, local)

    high, low, named = columns(0), columns(1), columns(2)
    order = jnp.arange(rows, dtype=jnp.int32)
    before = (order[None, :] < order[:, None]).astype(jnp.bfloat16)
    slot = jnp.einsum("tu,bue->bet", before, named, preferred_element_type=jnp.float32)
    hits = jnp.transpose(named, (0, 2, 1)) > 0
    picks = hits[:, :, None, :] & (
        slot.astype(jnp.int32)[:, :, None, :] == jnp.arange(CAP, dtype=jnp.int32)[None, None, :, None]
    )
    received = jnp.einsum(
        "becr,brd->becd", picks.astype(jnp.bfloat16), rows_all, preferred_element_type=jnp.float32
    ).astype(jnp.bfloat16)
    gate = jnp.einsum("becd,edf->becf", received, w_gate, preferred_element_type=jnp.float32)
    upward = jnp.einsum("becd,edf->becf", received, w_up, preferred_element_type=jnp.float32)
    hidden = (jax.nn.silu(gate) * upward).astype(jnp.bfloat16)
    zero = jnp.zeros((), jnp.bfloat16)
    high = jnp.where(picks, jnp.transpose(high, (0, 2, 1))[:, :, None, :], zero)
    low = jnp.where(picks, jnp.transpose(low, (0, 2, 1))[:, :, None, :], zero)
    cut = w_down.shape[2] // pieces
    outs = []
    for piece in range(pieces):
        down = lax.slice_in_dim(w_down, piece * cut, (piece + 1) * cut, axis=2)
        result = jnp.einsum("becf,efd->becd", hidden, down, preferred_element_type=jnp.float32)
        result = result.astype(jnp.bfloat16)
        partial = jnp.einsum("becr,becd->brd", high, result, preferred_element_type=jnp.float32)
        partial = partial + jnp.einsum(
            "becr,becd->brd", low, result, preferred_element_type=jnp.float32
        )
        outs.append(partial)
    return outs


def shifted(x, step):
    count = lax.axis_size("exp")
    return lax.ppermute(x, "exp", [(j, (j + step) % count) for j in range(count)])


def exchange_sum(blocks):
    total = blocks[0].astype(jnp.float32)
    for step in range(1, blocks.shape[0]):
        total = total + shifted(blocks[step], -step).astype(jnp.float32)
    return total


def step_rows(x, rows):
    count = lax.axis_size("exp")
    here = lax.axis_index("exp")
    parts = [
        lax.dynamic_slice_in_dim(x, (here - step) % count * rows, rows) for step in range(count)
    ]
    return jnp.concatenate(parts)


def gather_w_out(w_out):
    count = lax.axis_size("exp")
    mates = lax.axis_size("req")
    part = lax.axis_index("req") % 2
    cut = w_out.shape[0] // 2
    mine = lax.dynamic_slice_in_dim(w_out, part * cut, cut, 0)
    got = jnp.stack([shifted(mine, step) for step in range(1, count)])
    other = lax.ppermute(got, "req", [(j, j ^ 1) for j in range(mates)])
    lower = jnp.where(part == 0, got, other)
    upper = jnp.where(part == 0, other, got)
    return jnp.concatenate([lower, upper], axis=1)


def shards(
    tokens,
    norm_attn,
    w_query,
    w_key,
    w_value,
    w_out,
    norm_moe,
    w_router,
    w_gate,
    w_up,
    w_down,
    segment_ids,
    page_order,
    expert_ids,
):
    rows, width = tokens.shape
    seg = segment_ids[0]
    groups = w_key.shape[1] // HD
    here = lax.axis_index("exp")
    pos = lax.dynamic_slice_in_dim(positions(seg), here * rows, rows)
    normed = rms_scale(tokens, norm_attn)
    query = jnp.dot(normed, w_query, preferred_element_type=jnp.float32).reshape(
        rows, 2 * groups, HD
    )
    query = rotate(query, pos).astype(jnp.bfloat16).reshape(rows, groups, 2 * HD)
    keys = jnp.dot(normed, w_key, preferred_element_type=jnp.float32).reshape(rows, groups, HD)
    keys = rotate(keys, pos).astype(jnp.bfloat16)
    values = (
        jnp.dot(normed, w_value, preferred_element_type=jnp.float32)
        .astype(jnp.bfloat16)
        .reshape(rows, groups, HD)
    )
    keyval = jnp.concatenate([keys, values], axis=-1)
    owners = lax.axis_size("exp")
    share = groups // owners
    both = jnp.concatenate([query, keyval], axis=-1)
    parts = [lax.dynamic_slice_in_dim(both, here * share, share, 1)]
    for step in range(1, owners):
        send = lax.dynamic_slice_in_dim(both, (here + step) % owners * share, share, 1)
        parts.append(shifted(send, step))
    both = jnp.concatenate(parts)
    query_heads, keyval_heads = both[..., : 2 * HD], both[..., 2 * HD :]
    plen = keyval_heads.shape[0]
    where_at = step_rows(jnp.arange(plen, dtype=jnp.int32), rows)
    placing = step_rows(page_order[0], rows)[None, :] == jnp.arange(plen, dtype=jnp.int32)[:, None]
    kv_cache = jnp.einsum(
        "rs,skd->rkd", placing.astype(jnp.bfloat16), keyval_heads, preferred_element_type=jnp.float32
    ).astype(jnp.bfloat16)
    seg_rows = step_rows(seg, rows)
    heads_out = attend(query_heads, keyval_heads, seg_rows, seg_rows, where_at, where_at)
    blocks = heads_out.reshape(owners, rows, -1)
    remote = gather_w_out(w_out)
    attention = jnp.dot(blocks[0], w_out, preferred_element_type=jnp.float32)
    for step in range(1, owners):
        got = shifted(blocks[step], -step)
        attention = attention + jnp.dot(
            got, remote[owners - step - 1], preferred_element_type=jnp.float32
        )
    resid = tokens.astype(jnp.float32) + attention
    normed2 = rms_scale(resid, norm_moe)
    packed = routing(normed2, expert_ids, w_router)
    experts = w_router.shape[1]
    moe = jnp.concatenate(expert_mix(packed, 1, width, experts, w_gate, w_up, w_down, 2), axis=2)[0]
    received = jnp.concatenate([shifted(packed, step) for step in range(1, owners)])
    pieces = expert_mix(received, owners - 1, width, experts, w_gate, w_up, w_down, 2)
    backs = []
    for piece in pieces:
        piece = piece.astype(jnp.bfloat16)
        back = sum(
            shifted(piece[step - 1], -step).astype(jnp.float32) for step in range(1, owners)
        )
        backs.append(back)
    moe = moe + jnp.concatenate(backs, axis=1)
    mixed = (resid + moe).astype(jnp.bfloat16)
    return (mixed, kv_cache)


def solution(mesh):
    placed = (
        P(("req", "exp"), None),
        P(),
        P(),
        P(),
        P(),
        P("exp", None),
        P(),
        P(),
        P("exp", None, None),
        P("exp", None, None),
        P("exp", None, None),
        P("req", None),
        P("req", None),
        P(("req", "exp"), None),
    )
    return jax.shard_map(
        shards,
        mesh=mesh,
        in_specs=placed,
        out_specs=(P(("req", "exp"), None), P("req", "exp", None)),
        check_vma=False,
    )
```

```python
import jax
import jax.numpy as jnp
from jax import lax
from jax.sharding import PartitionSpec as P

HD = 64
CAP = 64


def rms_scale(rows, gain):
    rows = rows.astype(jnp.float32)
    inverse = lax.rsqrt(jnp.mean(rows * rows, axis=-1, keepdims=True) + 1e-06)
    return (rows * inverse * gain.astype(jnp.float32)).astype(jnp.bfloat16)


def positions(seg):
    index = jnp.arange(seg.shape[0], dtype=jnp.int32)
    starts = jnp.concatenate([jnp.ones((1,), dtype=bool), seg[1:] != seg[:-1]])
    first = lax.cummax(jnp.where(starts, index, 0), axis=0)
    return index - first


def rotate(values, pos):
    half = values.shape[-1] // 2
    freq = 10000.0 ** (-jnp.arange(half, dtype=jnp.float32) / half)
    angle = pos.astype(jnp.float32)[:, None] * freq[None, :]
    cosine = jnp.cos(angle)[:, None, :]
    sine = jnp.sin(angle)[:, None, :]
    front = values[..., :half]
    back = values[..., half:]
    return jnp.concatenate([front * cosine - back * sine, back * cosine + front * sine], axis=-1)


def attend(query, keyval, query_seg, seg, query_at, where_at):
    plen, groups, width = query.shape
    half = width // 2
    queries = query.reshape(plen, groups, 2, half)
    keys = keyval[..., :half]
    values = keyval[..., half:]
    score = jnp.einsum("qkgd,tkd->kgqt", queries, keys, preferred_element_type=jnp.float32) * 0.125
    allowed = (query_seg[:, None] == seg[None, :]) & (where_at[None, :] <= query_at[:, None])
    score = jnp.where(allowed[None, None], score, -1e30)
    top = jnp.max(score, axis=-1, keepdims=True)
    expo = jnp.exp(score - top)
    probs = (expo / jnp.sum(expo, axis=-1, keepdims=True)).astype(jnp.bfloat16)
    out = jnp.einsum("kgqt,tkd->qkgd", probs, values, preferred_element_type=jnp.float32)
    return out.astype(jnp.bfloat16).reshape(plen, groups * width)


def routing(normed2, ids, w_router):
    experts = w_router.shape[1]
    logits = jnp.dot(normed2, w_router, preferred_element_type=jnp.float32)
    match = ids[:, :, None] == jnp.arange(experts, dtype=jnp.int32)
    chosen = jnp.sum(jnp.where(match, logits[:, None, :], 0.0), axis=2)
    weights = jax.nn.softmax(chosen, axis=-1)
    dense = jnp.sum(jnp.where(match, weights[:, :, None], 0.0), axis=1)
    high = dense.astype(jnp.bfloat16)
    low = (dense - high.astype(jnp.float32)).astype(jnp.bfloat16)
    named = jnp.any(match, axis=1).astype(jnp.bfloat16)
    pad = (-3 * experts) % 128
    fill = jnp.zeros((normed2.shape[0], pad), jnp.bfloat16)
    return jnp.concatenate([normed2, high, low, named, fill], axis=1)


def expert_mix(chunks, width, experts, w_gate, w_up, w_down, pieces):
    local = w_gate.shape[0]
    rows = chunks[0].shape[0]
    here = lax.axis_index("exp")
    rows_all = jnp.stack([chunk[:, :width] for chunk in chunks])

    def columns(block):
        start = width + block * experts + here * local
        return jnp.stack([lax.dynamic_slice_in_dim(chunk, start, local, 1) for chunk in chunks])

    high, low, named = columns(0), columns(1), columns(2)
    order = jnp.arange(rows, dtype=jnp.int32)
    before = (order[None, :] < order[:, None]).astype(jnp.bfloat16)
    slot = jnp.einsum("tu,bue->bet", before, named, preferred_element_type=jnp.float32)
    hits = jnp.transpose(named, (0, 2, 1)) > 0
    picks = hits[:, :, None, :] & (
        slot.astype(jnp.int32)[:, :, None, :] == jnp.arange(CAP, dtype=jnp.int32)[None, None, :, None]
    )
    received = jnp.einsum(
        "becr,brd->becd", picks.astype(jnp.bfloat16), rows_all, preferred_element_type=jnp.float32
    ).astype(jnp.bfloat16)
    gate = jnp.einsum("becd,edf->becf", received, w_gate, preferred_element_type=jnp.float32)
    upward = jnp.einsum("becd,edf->becf", received, w_up, preferred_element_type=jnp.float32)
    hidden = (jax.nn.silu(gate) * upward).astype(jnp.bfloat16)
    zero = jnp.zeros((), jnp.bfloat16)
    high = jnp.where(picks, jnp.transpose(high, (0, 2, 1))[:, :, None, :], zero)
    low = jnp.where(picks, jnp.transpose(low, (0, 2, 1))[:, :, None, :], zero)
    cut = w_down.shape[2] // pieces
    outs = []
    for piece in range(pieces):
        down = lax.slice_in_dim(w_down, piece * cut, (piece + 1) * cut, axis=2)
        result = jnp.einsum("becf,efd->becd", hidden, down, preferred_element_type=jnp.float32)
        result = result.astype(jnp.bfloat16)
        partial = jnp.einsum("becr,becd->brd", high, result, preferred_element_type=jnp.float32)
        partial = partial + jnp.einsum(
            "becr,becd->brd", low, result, preferred_element_type=jnp.float32
        )
        outs.append(partial)
    return outs


def shifted(x, step):
    count = lax.axis_size("exp")
    return lax.ppermute(x, "exp", [(j, (j + step) % count) for j in range(count)])


def exchange_sum(blocks):
    total = blocks[0].astype(jnp.float32)
    for step in range(1, blocks.shape[0]):
        total = total + shifted(blocks[step], -step).astype(jnp.float32)
    return total


def step_rows(x, rows):
    count = lax.axis_size("exp")
    here = lax.axis_index("exp")
    parts = [
        lax.dynamic_slice_in_dim(x, (here - step) % count * rows, rows) for step in range(count)
    ]
    return jnp.concatenate(parts)


def gather_w_out(w_out):
    count = lax.axis_size("exp")
    mates = lax.axis_size("req")
    part = lax.axis_index("req") % 2
    cut = w_out.shape[0] // 2
    mine = lax.dynamic_slice_in_dim(w_out, part * cut, cut, 0)
    got = jnp.stack([shifted(mine, step) for step in range(1, count)])
    other = lax.ppermute(got, "req", [(j, j ^ 1) for j in range(mates)])
    lower = jnp.where(part == 0, got, other)
    upper = jnp.where(part == 0, other, got)
    return jnp.concatenate([lower, upper], axis=1)


def shards(
    tokens,
    norm_attn,
    w_query,
    w_key,
    w_value,
    w_out,
    norm_moe,
    w_router,
    w_gate,
    w_up,
    w_down,
    segment_ids,
    page_order,
    expert_ids,
):
    rows, width = tokens.shape
    seg = segment_ids[0]
    groups = w_key.shape[1] // HD
    here = lax.axis_index("exp")
    pos = lax.dynamic_slice_in_dim(positions(seg), here * rows, rows)
    normed = rms_scale(tokens, norm_attn)
    query = jnp.dot(normed, w_query, preferred_element_type=jnp.float32).reshape(
        rows, 2 * groups, HD
    )
    query = rotate(query, pos).astype(jnp.bfloat16).reshape(rows, groups, 2 * HD)
    keys = jnp.dot(normed, w_key, preferred_element_type=jnp.float32).reshape(rows, groups, HD)
    keys = rotate(keys, pos).astype(jnp.bfloat16)
    values = (
        jnp.dot(normed, w_value, preferred_element_type=jnp.float32)
        .astype(jnp.bfloat16)
        .reshape(rows, groups, HD)
    )
    keyval = jnp.concatenate([keys, values], axis=-1)
    owners = lax.axis_size("exp")
    share = groups // owners
    both = jnp.concatenate([query, keyval], axis=-1)
    parts = [lax.dynamic_slice_in_dim(both, here * share, share, 1)]
    for step in range(1, owners):
        send = lax.dynamic_slice_in_dim(both, (here + step) % owners * share, share, 1)
        parts.append(shifted(send, step))
    both = jnp.concatenate(parts)
    query_heads, keyval_heads = both[..., : 2 * HD], both[..., 2 * HD :]
    plen = keyval_heads.shape[0]
    where_at = step_rows(jnp.arange(plen, dtype=jnp.int32), rows)
    placing = step_rows(page_order[0], rows)[None, :] == jnp.arange(plen, dtype=jnp.int32)[:, None]
    kv_cache = jnp.einsum(
        "rs,skd->rkd", placing.astype(jnp.bfloat16), keyval_heads, preferred_element_type=jnp.float32
    ).astype(jnp.bfloat16)
    seg_rows = step_rows(seg, rows)
    heads_out = attend(query_heads, keyval_heads, seg_rows, seg_rows, where_at, where_at)
    blocks = heads_out.reshape(owners, rows, -1)
    remote = gather_w_out(w_out)
    attention = jnp.dot(blocks[0], w_out, preferred_element_type=jnp.float32)
    for step in range(1, owners):
        got = shifted(blocks[step], -step)
        attention = attention + jnp.dot(
            got, remote[owners - step - 1], preferred_element_type=jnp.float32
        )
    resid = tokens.astype(jnp.float32) + attention
    normed2 = rms_scale(resid, norm_moe)
    packed = routing(normed2, expert_ids, w_router)
    experts = w_router.shape[1]
    moe = expert_mix([packed], width, experts, w_gate, w_up, w_down, 1)[0][0]
    received = [shifted(packed, step) for step in range(1, owners)]
    pieces = expert_mix(received, width, experts, w_gate, w_up, w_down, 2)
    backs = []
    for piece in pieces:
        piece = piece.astype(jnp.bfloat16)
        back = sum(
            shifted(piece[step - 1], -step).astype(jnp.float32) for step in range(1, owners)
        )
        backs.append(back)
    moe = moe + jnp.concatenate(backs, axis=1)
    mixed = (resid + moe).astype(jnp.bfloat16)
    return (mixed, kv_cache)


def solution(mesh):
    placed = (
        P(("req", "exp"), None),
        P(),
        P(),
        P(),
        P(),
        P("exp", None),
        P(),
        P(),
        P("exp", None, None),
        P("exp", None, None),
        P("exp", None, None),
        P("req", None),
        P("req", None),
        P(("req", "exp"), None),
    )
    return jax.shard_map(
        shards,
        mesh=mesh,
        in_specs=placed,
        out_specs=(P(("req", "exp"), None), P("req", "exp", None)),
        check_vma=False,
    )
```

```python
import jax
import jax.numpy as jnp
from jax import lax
from jax.sharding import PartitionSpec as P

HD = 64
CAP = 64


def rms_scale(rows, gain):
    rows = rows.astype(jnp.float32)
    inverse = lax.rsqrt(jnp.mean(rows * rows, axis=-1, keepdims=True) + 1e-06)
    return (rows * inverse * gain.astype(jnp.float32)).astype(jnp.bfloat16)


def positions(seg):
    index = jnp.arange(seg.shape[0], dtype=jnp.int32)
    starts = jnp.concatenate([jnp.ones((1,), dtype=bool), seg[1:] != seg[:-1]])
    first = lax.cummax(jnp.where(starts, index, 0), axis=0)
    return index - first


def rotate(values, pos):
    half = values.shape[-1] // 2
    freq = 10000.0 ** (-jnp.arange(half, dtype=jnp.float32) / half)
    angle = pos.astype(jnp.float32)[:, None] * freq[None, :]
    cosine = jnp.cos(angle)[:, None, :]
    sine = jnp.sin(angle)[:, None, :]
    front = values[..., :half]
    back = values[..., half:]
    return jnp.concatenate([front * cosine - back * sine, back * cosine + front * sine], axis=-1)


def attend(query, keyval, query_seg, seg, query_at, where_at):
    plen, groups, width = query.shape
    half = width // 2
    queries = query.reshape(plen, groups, 2, half)
    keys = keyval[..., :half]
    values = keyval[..., half:]
    score = jnp.einsum("qkgd,tkd->kgqt", queries, keys, preferred_element_type=jnp.float32) * 0.125
    allowed = (query_seg[:, None] == seg[None, :]) & (where_at[None, :] <= query_at[:, None])
    score = jnp.where(allowed[None, None], score, -1e30)
    top = jnp.max(score, axis=-1, keepdims=True)
    expo = jnp.exp(score - top)
    probs = (expo / jnp.sum(expo, axis=-1, keepdims=True)).astype(jnp.bfloat16)
    out = jnp.einsum("kgqt,tkd->qkgd", probs, values, preferred_element_type=jnp.float32)
    return out.astype(jnp.bfloat16).reshape(plen, groups * width)


def routing(normed2, ids, w_router):
    experts = w_router.shape[1]
    logits = jnp.dot(normed2, w_router, preferred_element_type=jnp.float32)
    match = ids[:, :, None] == jnp.arange(experts, dtype=jnp.int32)
    chosen = jnp.sum(jnp.where(match, logits[:, None, :], 0.0), axis=2)
    weights = jax.nn.softmax(chosen, axis=-1)
    dense = jnp.sum(jnp.where(match, weights[:, :, None], 0.0), axis=1)
    high = dense.astype(jnp.bfloat16)
    low = (dense - high.astype(jnp.float32)).astype(jnp.bfloat16)
    named = jnp.any(match, axis=1).astype(jnp.bfloat16)
    pad = (-3 * experts) % 128
    fill = jnp.zeros((normed2.shape[0], pad), jnp.bfloat16)
    return jnp.concatenate([normed2, high, low, named, fill], axis=1)


def expert_mix(packed, sources, width, experts, w_gate, w_up, w_down, pieces):
    local = w_gate.shape[0]
    rows = packed.shape[0] // sources
    here = lax.axis_index("exp")
    rows_all = packed[:, :width].reshape(sources, rows, width)

    def columns(block):
        start = width + block * experts + here * local
        return lax.dynamic_slice_in_dim(packed, start, local, 1).reshape(sources, rows, local)

    high, low, named = columns(0), columns(1), columns(2)
    order = jnp.arange(rows, dtype=jnp.int32)
    before = (order[None, :] < order[:, None]).astype(jnp.bfloat16)
    slot = jnp.einsum("tu,bue->bet", before, named, preferred_element_type=jnp.float32)
    hits = jnp.transpose(named, (0, 2, 1)) > 0
    picks = hits[:, :, None, :] & (
        slot.astype(jnp.int32)[:, :, None, :] == jnp.arange(CAP, dtype=jnp.int32)[None, None, :, None]
    )
    received = jnp.einsum(
        "becr,brd->becd", picks.astype(jnp.bfloat16), rows_all, preferred_element_type=jnp.float32
    ).astype(jnp.bfloat16)
    gate = jnp.einsum("becd,edf->becf", received, w_gate, preferred_element_type=jnp.float32)
    upward = jnp.einsum("becd,edf->becf", received, w_up, preferred_element_type=jnp.float32)
    hidden = (jax.nn.silu(gate) * upward).astype(jnp.bfloat16)
    zero = jnp.zeros((), jnp.bfloat16)
    high = jnp.where(picks, jnp.transpose(high, (0, 2, 1))[:, :, None, :], zero)
    low = jnp.where(picks, jnp.transpose(low, (0, 2, 1))[:, :, None, :], zero)
    cut = w_down.shape[2] // pieces
    outs = []
    for piece in range(pieces):
        down = lax.slice_in_dim(w_down, piece * cut, (piece + 1) * cut, axis=2)
        result = jnp.einsum("becf,efd->becd", hidden, down, preferred_element_type=jnp.float32)
        result = result.astype(jnp.bfloat16)
        partial = jnp.einsum("becr,becd->brd", high, result, preferred_element_type=jnp.float32)
        partial = partial + jnp.einsum(
            "becr,becd->brd", low, result, preferred_element_type=jnp.float32
        )
        outs.append(partial)
    return outs


def shifted(x, step):
    count = lax.axis_size("exp")
    return lax.ppermute(x, "exp", [(j, (j + step) % count) for j in range(count)])


def exchange_sum(blocks):
    total = blocks[0].astype(jnp.float32)
    for step in range(1, blocks.shape[0]):
        total = total + shifted(blocks[step], -step).astype(jnp.float32)
    return total


def step_rows(x, rows):
    count = lax.axis_size("exp")
    here = lax.axis_index("exp")
    parts = [
        lax.dynamic_slice_in_dim(x, (here - step) % count * rows, rows) for step in range(count)
    ]
    return jnp.concatenate(parts)


def gather_w_out(w_out, extra):
    count = lax.axis_size("exp")
    mates = lax.axis_size("req")
    part = lax.axis_index("req") % 2
    cut = w_out.shape[0] // 2
    mine = jnp.concatenate([lax.dynamic_slice_in_dim(w_out, part * cut, cut, 0), extra])
    got = jnp.stack([shifted(mine, step) for step in range(1, count)])
    names, got = got[:, cut:], got[:, :cut]
    other = lax.ppermute(got, "req", [(j, j ^ 1) for j in range(mates)])
    lower = jnp.where(part == 0, got, other)
    upper = jnp.where(part == 0, other, got)
    return jnp.concatenate([lower, upper], axis=1), names


def shards(
    tokens,
    norm_attn,
    w_query,
    w_key,
    w_value,
    w_out,
    norm_moe,
    w_router,
    w_gate,
    w_up,
    w_down,
    segment_ids,
    page_order,
    expert_ids,
):
    rows, width = tokens.shape
    seg = segment_ids[0]
    groups = w_key.shape[1] // HD
    here = lax.axis_index("exp")
    pos = lax.dynamic_slice_in_dim(positions(seg), here * rows, rows)
    normed = rms_scale(tokens, norm_attn)
    query = jnp.dot(normed, w_query, preferred_element_type=jnp.float32).reshape(
        rows, 2 * groups, HD
    )
    query = rotate(query, pos).astype(jnp.bfloat16).reshape(rows, groups, 2 * HD)
    keys = jnp.dot(normed, w_key, preferred_element_type=jnp.float32).reshape(rows, groups, HD)
    keys = rotate(keys, pos).astype(jnp.bfloat16)
    values = (
        jnp.dot(normed, w_value, preferred_element_type=jnp.float32)
        .astype(jnp.bfloat16)
        .reshape(rows, groups, HD)
    )
    keyval = jnp.concatenate([keys, values], axis=-1)
    owners = lax.axis_size("exp")
    share = groups // owners
    both = jnp.concatenate([query, keyval], axis=-1)
    parts = [lax.dynamic_slice_in_dim(both, here * share, share, 1)]
    for step in range(1, owners):
        send = lax.dynamic_slice_in_dim(both, (here + step) % owners * share, share, 1)
        parts.append(shifted(send, step))
    both = jnp.concatenate(parts)
    query_heads, keyval_heads = both[..., : 2 * HD], both[..., 2 * HD :]
    plen = keyval_heads.shape[0]
    where_at = step_rows(jnp.arange(plen, dtype=jnp.int32), rows)
    placing = step_rows(page_order[0], rows)[None, :] == jnp.arange(plen, dtype=jnp.int32)[:, None]
    kv_cache = jnp.einsum(
        "rs,skd->rkd", placing.astype(jnp.bfloat16), keyval_heads, preferred_element_type=jnp.float32
    ).astype(jnp.bfloat16)
    seg_rows = step_rows(seg, rows)
    heads_out = attend(query_heads, keyval_heads, seg_rows, seg_rows, where_at, where_at)
    blocks = heads_out.reshape(owners, rows, -1)
    topk = expert_ids.shape[1]
    flat = expert_ids.T.reshape(-1).astype(jnp.bfloat16)
    flat = jnp.pad(flat, (0, (-flat.shape[0]) % width)).reshape(-1, width)
    remote, names = gather_w_out(w_out, flat)
    attention = jnp.dot(blocks[0], w_out, preferred_element_type=jnp.float32)
    for step in range(1, owners):
        got = shifted(blocks[step], -step)
        attention = attention + jnp.dot(
            got, remote[owners - step - 1], preferred_element_type=jnp.float32
        )
    resid = tokens.astype(jnp.float32) + attention
    normed2 = rms_scale(resid, norm_moe)
    packed = routing(normed2, expert_ids, w_router)
    experts = w_router.shape[1]
    moe = expert_mix(packed, 1, width, experts, w_gate, w_up, w_down, 1)[0][0]
    received = []
    for step in range(1, owners):
        ids = names[step - 1].reshape(-1)[: topk * rows].reshape(topk, rows).T.astype(jnp.int32)
        received.append(routing(shifted(normed2, step), ids, w_router))
    received = jnp.concatenate(received)
    pieces = expert_mix(received, owners - 1, width, experts, w_gate, w_up, w_down, 2)
    backs = []
    for piece in pieces:
        piece = piece.astype(jnp.bfloat16)
        back = sum(
            shifted(piece[step - 1], -step).astype(jnp.float32) for step in range(1, owners)
        )
        backs.append(back)
    moe = moe + jnp.concatenate(backs, axis=1)
    mixed = (resid + moe).astype(jnp.bfloat16)
    return (mixed, kv_cache)


def solution(mesh):
    placed = (
        P(("req", "exp"), None),
        P(),
        P(),
        P(),
        P(),
        P("exp", None),
        P(),
        P(),
        P("exp", None, None),
        P("exp", None, None),
        P("exp", None, None),
        P("req", None),
        P("req", None),
        P(("req", "exp"), None),
    )
    return jax.shard_map(
        shards,
        mesh=mesh,
        in_specs=placed,
        out_specs=(P(("req", "exp"), None), P("req", "exp", None)),
        check_vma=False,
    )
```

```python
import jax
import jax.numpy as jnp
from jax import lax
from jax.sharding import PartitionSpec as P

HD = 64
CAP = 64


def rms_scale(rows, gain):
    rows = rows.astype(jnp.float32)
    inverse = lax.rsqrt(jnp.mean(rows * rows, axis=-1, keepdims=True) + 1e-06)
    return (rows * inverse * gain.astype(jnp.float32)).astype(jnp.bfloat16)


def positions(seg):
    index = jnp.arange(seg.shape[0], dtype=jnp.int32)
    starts = jnp.concatenate([jnp.ones((1,), dtype=bool), seg[1:] != seg[:-1]])
    first = lax.cummax(jnp.where(starts, index, 0), axis=0)
    return index - first


def rotate(values, pos):
    half = values.shape[-1] // 2
    freq = 10000.0 ** (-jnp.arange(half, dtype=jnp.float32) / half)
    angle = pos.astype(jnp.float32)[:, None] * freq[None, :]
    cosine = jnp.cos(angle)[:, None, :]
    sine = jnp.sin(angle)[:, None, :]
    front = values[..., :half]
    back = values[..., half:]
    return jnp.concatenate([front * cosine - back * sine, back * cosine + front * sine], axis=-1)


def attend(query, keyval, query_seg, seg, query_at, where_at):
    plen, groups, width = query.shape
    half = width // 2
    queries = query.reshape(plen, groups, 2, half)
    keys = keyval[..., :half]
    values = keyval[..., half:]
    score = jnp.einsum("qkgd,tkd->kgqt", queries, keys, preferred_element_type=jnp.float32) * 0.125
    allowed = (query_seg[:, None] == seg[None, :]) & (where_at[None, :] <= query_at[:, None])
    score = jnp.where(allowed[None, None], score, -1e30)
    top = jnp.max(score, axis=-1, keepdims=True)
    expo = jnp.exp(score - top)
    probs = (expo / jnp.sum(expo, axis=-1, keepdims=True)).astype(jnp.bfloat16)
    out = jnp.einsum("kgqt,tkd->qkgd", probs, values, preferred_element_type=jnp.float32)
    return out.astype(jnp.bfloat16).reshape(plen, groups * width)


def routing(normed2, ids, w_router):
    experts = w_router.shape[1]
    logits = jnp.dot(normed2, w_router, preferred_element_type=jnp.float32)
    match = ids[:, :, None] == jnp.arange(experts, dtype=jnp.int32)
    chosen = jnp.sum(jnp.where(match, logits[:, None, :], 0.0), axis=2)
    weights = jax.nn.softmax(chosen, axis=-1)
    dense = jnp.sum(jnp.where(match, weights[:, :, None], 0.0), axis=1)
    high = dense.astype(jnp.bfloat16)
    low = (dense - high.astype(jnp.float32)).astype(jnp.bfloat16)
    named = jnp.any(match, axis=1).astype(jnp.bfloat16)
    pad = (-3 * experts) % 128
    fill = jnp.zeros((normed2.shape[0], pad), jnp.bfloat16)
    return jnp.concatenate([normed2, high, low, named, fill], axis=1)


def expert_mix(packed, sources, width, experts, w_gate, w_up, w_down, pieces):
    local = w_gate.shape[0]
    rows = packed.shape[0] // sources
    here = lax.axis_index("exp")
    rows_all = packed[:, :width].reshape(sources, rows, width)

    def columns(block):
        start = width + block * experts + here * local
        return lax.dynamic_slice_in_dim(packed, start, local, 1).reshape(sources, rows, local)

    high, low, named = columns(0), columns(1), columns(2)
    order = jnp.arange(rows, dtype=jnp.int32)
    before = (order[None, :] < order[:, None]).astype(jnp.bfloat16)
    slot = jnp.einsum("tu,bue->bet", before, named, preferred_element_type=jnp.float32)
    hits = jnp.transpose(named, (0, 2, 1)) > 0
    picks = hits[:, :, None, :] & (
        slot.astype(jnp.int32)[:, :, None, :] == jnp.arange(CAP, dtype=jnp.int32)[None, None, :, None]
    )
    received = jnp.einsum(
        "becr,brd->becd", picks.astype(jnp.bfloat16), rows_all, preferred_element_type=jnp.float32
    ).astype(jnp.bfloat16)
    gate = jnp.einsum("becd,edf->becf", received, w_gate, preferred_element_type=jnp.float32)
    upward = jnp.einsum("becd,edf->becf", received, w_up, preferred_element_type=jnp.float32)
    hidden = (jax.nn.silu(gate) * upward).astype(jnp.bfloat16)
    zero = jnp.zeros((), jnp.bfloat16)
    high = jnp.where(picks, jnp.transpose(high, (0, 2, 1))[:, :, None, :], zero)
    low = jnp.where(picks, jnp.transpose(low, (0, 2, 1))[:, :, None, :], zero)
    cut = w_down.shape[2] // pieces
    outs = []
    for piece in range(pieces):
        down = lax.slice_in_dim(w_down, piece * cut, (piece + 1) * cut, axis=2)
        result = jnp.einsum("becf,efd->becd", hidden, down, preferred_element_type=jnp.float32)
        result = result.astype(jnp.bfloat16)
        partial = jnp.einsum("becr,becd->brd", high, result, preferred_element_type=jnp.float32)
        partial = partial + jnp.einsum(
            "becr,becd->brd", low, result, preferred_element_type=jnp.float32
        )
        outs.append(partial)
    return outs


def shifted(x, step):
    count = lax.axis_size("exp")
    return lax.ppermute(x, "exp", [(j, (j + step) % count) for j in range(count)])


def exchange_sum(blocks):
    total = blocks[0].astype(jnp.float32)
    for step in range(1, blocks.shape[0]):
        total = total + shifted(blocks[step], -step).astype(jnp.float32)
    return total


def step_rows(x, rows):
    count = lax.axis_size("exp")
    here = lax.axis_index("exp")
    parts = [
        lax.dynamic_slice_in_dim(x, (here - step) % count * rows, rows) for step in range(count)
    ]
    return jnp.concatenate(parts)


def gather_w_out(w_out):
    count = lax.axis_size("exp")
    mates = lax.axis_size("req")
    part = lax.axis_index("req") % 2
    cut = w_out.shape[0] // 2
    mine = lax.dynamic_slice_in_dim(w_out, part * cut, cut, 0)
    got = jnp.stack([shifted(mine, step) for step in range(1, count)])
    other = lax.ppermute(got, "req", [(j, j ^ 1) for j in range(mates)])
    return got, other


def shards(
    tokens,
    norm_attn,
    w_query,
    w_key,
    w_value,
    w_out,
    norm_moe,
    w_router,
    w_gate,
    w_up,
    w_down,
    segment_ids,
    page_order,
    expert_ids,
):
    rows, width = tokens.shape
    seg = segment_ids[0]
    groups = w_key.shape[1] // HD
    here = lax.axis_index("exp")
    pos = lax.dynamic_slice_in_dim(positions(seg), here * rows, rows)
    normed = rms_scale(tokens, norm_attn)
    query = jnp.dot(normed, w_query, preferred_element_type=jnp.float32).reshape(
        rows, 2 * groups, HD
    )
    query = rotate(query, pos).astype(jnp.bfloat16).reshape(rows, groups, 2 * HD)
    keys = jnp.dot(normed, w_key, preferred_element_type=jnp.float32).reshape(rows, groups, HD)
    keys = rotate(keys, pos).astype(jnp.bfloat16)
    values = (
        jnp.dot(normed, w_value, preferred_element_type=jnp.float32)
        .astype(jnp.bfloat16)
        .reshape(rows, groups, HD)
    )
    keyval = jnp.concatenate([keys, values], axis=-1)
    owners = lax.axis_size("exp")
    share = groups // owners
    both = jnp.concatenate([query, keyval], axis=-1)
    parts = [lax.dynamic_slice_in_dim(both, here * share, share, 1)]
    for step in range(1, owners):
        send = lax.dynamic_slice_in_dim(both, (here + step) % owners * share, share, 1)
        parts.append(shifted(send, step))
    both = jnp.concatenate(parts)
    query_heads, keyval_heads = both[..., : 2 * HD], both[..., 2 * HD :]
    plen = keyval_heads.shape[0]
    where_at = step_rows(jnp.arange(plen, dtype=jnp.int32), rows)
    placing = step_rows(page_order[0], rows)[None, :] == jnp.arange(plen, dtype=jnp.int32)[:, None]
    kv_cache = jnp.einsum(
        "rs,skd->rkd", placing.astype(jnp.bfloat16), keyval_heads, preferred_element_type=jnp.float32
    ).astype(jnp.bfloat16)
    seg_rows = step_rows(seg, rows)
    heads_out = attend(query_heads, keyval_heads, seg_rows, seg_rows, where_at, where_at)
    blocks = heads_out.reshape(owners, rows, -1)
    remote = gather_w_out(w_out)
    attention = jnp.dot(blocks[0], w_out, preferred_element_type=jnp.float32)
    mine, other = remote
    part = lax.axis_index("req") % 2
    cut = mine.shape[1]
    for step in range(1, owners):
        got = shifted(blocks[step], -step)
        attention = attention + jnp.dot(
            lax.dynamic_slice_in_dim(got, part * cut, cut, 1),
            mine[owners - step - 1],
            preferred_element_type=jnp.float32,
        )
        attention = attention + jnp.dot(
            lax.dynamic_slice_in_dim(got, (1 - part) * cut, cut, 1),
            other[owners - step - 1],
            preferred_element_type=jnp.float32,
        )
    resid = tokens.astype(jnp.float32) + attention
    normed2 = rms_scale(resid, norm_moe)
    packed = routing(normed2, expert_ids, w_router)
    experts = w_router.shape[1]
    moe = expert_mix(packed, 1, width, experts, w_gate, w_up, w_down, 1)[0][0]
    received = jnp.concatenate([shifted(packed, step) for step in range(1, owners)])
    pieces = expert_mix(received, owners - 1, width, experts, w_gate, w_up, w_down, 2)
    backs = []
    for piece in pieces:
        piece = piece.astype(jnp.bfloat16)
        back = sum(
            shifted(piece[step - 1], -step).astype(jnp.float32) for step in range(1, owners)
        )
        backs.append(back)
    moe = moe + jnp.concatenate(backs, axis=1)
    mixed = (resid + moe).astype(jnp.bfloat16)
    return (mixed, kv_cache)


def solution(mesh):
    placed = (
        P(("req", "exp"), None),
        P(),
        P(),
        P(),
        P(),
        P("exp", None),
        P(),
        P(),
        P("exp", None, None),
        P("exp", None, None),
        P("exp", None, None),
        P("req", None),
        P("req", None),
        P(("req", "exp"), None),
    )
    return jax.shard_map(
        shards,
        mesh=mesh,
        in_specs=placed,
        out_specs=(P(("req", "exp"), None), P("req", "exp", None)),
        check_vma=False,
    )
```

```python
import jax
import jax.numpy as jnp
from jax import lax
from jax.sharding import PartitionSpec as P

HD = 64
CAP = 64


def rms_scale(rows, gain):
    rows = rows.astype(jnp.float32)
    inverse = lax.rsqrt(jnp.mean(rows * rows, axis=-1, keepdims=True) + 1e-06)
    return (rows * inverse * gain.astype(jnp.float32)).astype(jnp.bfloat16)


def positions(seg):
    index = jnp.arange(seg.shape[0], dtype=jnp.int32)
    starts = jnp.concatenate([jnp.ones((1,), dtype=bool), seg[1:] != seg[:-1]])
    first = lax.cummax(jnp.where(starts, index, 0), axis=0)
    return index - first


def rotate(values, pos):
    half = values.shape[-1] // 2
    freq = 10000.0 ** (-jnp.arange(half, dtype=jnp.float32) / half)
    angle = pos.astype(jnp.float32)[:, None] * freq[None, :]
    cosine = jnp.cos(angle)[:, None, :]
    sine = jnp.sin(angle)[:, None, :]
    front = values[..., :half]
    back = values[..., half:]
    return jnp.concatenate([front * cosine - back * sine, back * cosine + front * sine], axis=-1)


def attend(query, keyval, query_seg, seg, query_at, where_at):
    plen, groups, width = query.shape
    half = width // 2
    queries = query.reshape(plen, groups, 2, half)
    keys = keyval[..., :half]
    values = keyval[..., half:]
    score = jnp.einsum("qkgd,tkd->kgqt", queries, keys, preferred_element_type=jnp.float32) * 0.125
    allowed = (query_seg[:, None] == seg[None, :]) & (where_at[None, :] <= query_at[:, None])
    score = jnp.where(allowed[None, None], score, -1e30)
    top = jnp.max(score, axis=-1, keepdims=True)
    expo = jnp.exp(score - top)
    probs = (expo / jnp.sum(expo, axis=-1, keepdims=True)).astype(jnp.bfloat16)
    out = jnp.einsum("kgqt,tkd->qkgd", probs, values, preferred_element_type=jnp.float32)
    return out.astype(jnp.bfloat16).reshape(plen, groups * width)


def routing(normed2, ids, w_router):
    experts = w_router.shape[1]
    logits = jnp.dot(normed2, w_router, preferred_element_type=jnp.float32)
    match = ids[:, :, None] == jnp.arange(experts, dtype=jnp.int32)
    chosen = jnp.sum(jnp.where(match, logits[:, None, :], 0.0), axis=2)
    weights = jax.nn.softmax(chosen, axis=-1)
    dense = jnp.sum(jnp.where(match, weights[:, :, None], 0.0), axis=1)
    high = dense.astype(jnp.bfloat16)
    low = (dense - high.astype(jnp.float32)).astype(jnp.bfloat16)
    named = jnp.any(match, axis=1).astype(jnp.bfloat16)
    pad = (-3 * experts) % 128
    fill = jnp.zeros((normed2.shape[0], pad), jnp.bfloat16)
    return jnp.concatenate([normed2, high, low, named, fill], axis=1)


def expert_mix(packed, sources, width, experts, w_gate, w_up, w_down, pieces):
    local = w_gate.shape[0]
    rows = packed.shape[0] // sources
    here = lax.axis_index("exp")
    rows_all = packed[:, :width].reshape(sources, rows, width)

    def columns(block):
        start = width + block * experts + here * local
        return lax.dynamic_slice_in_dim(packed, start, local, 1).reshape(sources, rows, local)

    high, low, named = columns(0), columns(1), columns(2)
    order = jnp.arange(rows, dtype=jnp.int32)
    before = (order[None, :] < order[:, None]).astype(jnp.bfloat16)
    slot = jnp.einsum("tu,bue->bet", before, named, preferred_element_type=jnp.float32)
    hits = jnp.transpose(named, (0, 2, 1)) > 0
    picks = hits[:, :, None, :] & (
        slot.astype(jnp.int32)[:, :, None, :] == jnp.arange(CAP, dtype=jnp.int32)[None, None, :, None]
    )
    received = jnp.einsum(
        "becr,brd->becd", picks.astype(jnp.bfloat16), rows_all, preferred_element_type=jnp.float32
    ).astype(jnp.bfloat16)
    gate = jnp.einsum("becd,edf->becf", received, w_gate, preferred_element_type=jnp.float32)
    upward = jnp.einsum("becd,edf->becf", received, w_up, preferred_element_type=jnp.float32)
    hidden = (jax.nn.silu(gate) * upward).astype(jnp.bfloat16)
    zero = jnp.zeros((), jnp.bfloat16)
    high = jnp.where(picks, jnp.transpose(high, (0, 2, 1))[:, :, None, :], zero)
    low = jnp.where(picks, jnp.transpose(low, (0, 2, 1))[:, :, None, :], zero)
    cut = w_down.shape[2] // pieces
    outs = []
    for piece in range(pieces):
        down = lax.slice_in_dim(w_down, piece * cut, (piece + 1) * cut, axis=2)
        result = jnp.einsum("becf,efd->becd", hidden, down, preferred_element_type=jnp.float32)
        result = result.astype(jnp.bfloat16)
        partial = jnp.einsum(
            "becr,becd->brd",
            jnp.concatenate([high, low], axis=2),
            jnp.concatenate([result, result], axis=2),
            preferred_element_type=jnp.float32,
        )
        outs.append(partial)
    return outs


def shifted(x, step):
    count = lax.axis_size("exp")
    return lax.ppermute(x, "exp", [(j, (j + step) % count) for j in range(count)])


def exchange_sum(blocks):
    total = blocks[0].astype(jnp.float32)
    for step in range(1, blocks.shape[0]):
        total = total + shifted(blocks[step], -step).astype(jnp.float32)
    return total


def step_rows(x, rows):
    count = lax.axis_size("exp")
    here = lax.axis_index("exp")
    parts = [
        lax.dynamic_slice_in_dim(x, (here - step) % count * rows, rows) for step in range(count)
    ]
    return jnp.concatenate(parts)


def gather_w_out(w_out):
    count = lax.axis_size("exp")
    mates = lax.axis_size("req")
    part = lax.axis_index("req") % 2
    cut = w_out.shape[0] // 2
    mine = lax.dynamic_slice_in_dim(w_out, part * cut, cut, 0)
    got = jnp.stack([shifted(mine, step) for step in range(1, count)])
    other = lax.ppermute(got, "req", [(j, j ^ 1) for j in range(mates)])
    lower = jnp.where(part == 0, got, other)
    upper = jnp.where(part == 0, other, got)
    return jnp.concatenate([lower, upper], axis=1)


def shards(
    tokens,
    norm_attn,
    w_query,
    w_key,
    w_value,
    w_out,
    norm_moe,
    w_router,
    w_gate,
    w_up,
    w_down,
    segment_ids,
    page_order,
    expert_ids,
):
    rows, width = tokens.shape
    seg = segment_ids[0]
    groups = w_key.shape[1] // HD
    here = lax.axis_index("exp")
    pos = lax.dynamic_slice_in_dim(positions(seg), here * rows, rows)
    normed = rms_scale(tokens, norm_attn)
    query = jnp.dot(normed, w_query, preferred_element_type=jnp.float32).reshape(
        rows, 2 * groups, HD
    )
    query = rotate(query, pos).astype(jnp.bfloat16).reshape(rows, groups, 2 * HD)
    keys = jnp.dot(normed, w_key, preferred_element_type=jnp.float32).reshape(rows, groups, HD)
    keys = rotate(keys, pos).astype(jnp.bfloat16)
    values = (
        jnp.dot(normed, w_value, preferred_element_type=jnp.float32)
        .astype(jnp.bfloat16)
        .reshape(rows, groups, HD)
    )
    keyval = jnp.concatenate([keys, values], axis=-1)
    owners = lax.axis_size("exp")
    share = groups // owners
    both = jnp.concatenate([query, keyval], axis=-1)
    parts = [lax.dynamic_slice_in_dim(both, here * share, share, 1)]
    for step in range(1, owners):
        send = lax.dynamic_slice_in_dim(both, (here + step) % owners * share, share, 1)
        parts.append(shifted(send, step))
    both = jnp.concatenate(parts)
    query_heads, keyval_heads = both[..., : 2 * HD], both[..., 2 * HD :]
    plen = keyval_heads.shape[0]
    where_at = step_rows(jnp.arange(plen, dtype=jnp.int32), rows)
    placing = step_rows(page_order[0], rows)[None, :] == jnp.arange(plen, dtype=jnp.int32)[:, None]
    kv_cache = jnp.einsum(
        "rs,skd->rkd", placing.astype(jnp.bfloat16), keyval_heads, preferred_element_type=jnp.float32
    ).astype(jnp.bfloat16)
    seg_rows = step_rows(seg, rows)
    heads_out = attend(query_heads, keyval_heads, seg_rows, seg_rows, where_at, where_at)
    blocks = heads_out.reshape(owners, rows, -1)
    remote = gather_w_out(w_out)
    attention = jnp.dot(blocks[0], w_out, preferred_element_type=jnp.float32)
    for step in range(1, owners):
        got = shifted(blocks[step], -step)
        attention = attention + jnp.dot(
            got, remote[owners - step - 1], preferred_element_type=jnp.float32
        )
    resid = tokens.astype(jnp.float32) + attention
    normed2 = rms_scale(resid, norm_moe)
    packed = routing(normed2, expert_ids, w_router)
    experts = w_router.shape[1]
    moe = expert_mix(packed, 1, width, experts, w_gate, w_up, w_down, 1)[0][0]
    received = jnp.concatenate([shifted(packed, step) for step in range(1, owners)])
    pieces = expert_mix(received, owners - 1, width, experts, w_gate, w_up, w_down, 2)
    backs = []
    for piece in pieces:
        piece = piece.astype(jnp.bfloat16)
        back = sum(
            shifted(piece[step - 1], -step).astype(jnp.float32) for step in range(1, owners)
        )
        backs.append(back)
    moe = moe + jnp.concatenate(backs, axis=1)
    mixed = (resid + moe).astype(jnp.bfloat16)
    return (mixed, kv_cache)


def solution(mesh):
    placed = (
        P(("req", "exp"), None),
        P(),
        P(),
        P(),
        P(),
        P("exp", None),
        P(),
        P(),
        P("exp", None, None),
        P("exp", None, None),
        P("exp", None, None),
        P("req", None),
        P("req", None),
        P(("req", "exp"), None),
    )
    return jax.shard_map(
        shards,
        mesh=mesh,
        in_specs=placed,
        out_specs=(P(("req", "exp"), None), P("req", "exp", None)),
        check_vma=False,
    )
```

```python
import jax
import jax.numpy as jnp
from jax import lax
from jax.sharding import PartitionSpec as P

HD = 64
CAP = 64


def rms_scale(rows, gain):
    rows = rows.astype(jnp.float32)
    inverse = lax.rsqrt(jnp.mean(rows * rows, axis=-1, keepdims=True) + 1e-06)
    return (rows * inverse * gain.astype(jnp.float32)).astype(jnp.bfloat16)


def positions(seg):
    index = jnp.arange(seg.shape[0], dtype=jnp.int32)
    starts = jnp.concatenate([jnp.ones((1,), dtype=bool), seg[1:] != seg[:-1]])
    first = lax.cummax(jnp.where(starts, index, 0), axis=0)
    return index - first


def rotate(values, pos):
    half = values.shape[-1] // 2
    freq = 10000.0 ** (-jnp.arange(half, dtype=jnp.float32) / half)
    angle = pos.astype(jnp.float32)[:, None] * freq[None, :]
    cosine = jnp.cos(angle)[:, None, :]
    sine = jnp.sin(angle)[:, None, :]
    front = values[..., :half]
    back = values[..., half:]
    return jnp.concatenate([front * cosine - back * sine, back * cosine + front * sine], axis=-1)


def attend(query, keyval, query_seg, seg, query_at, where_at):
    plen, groups, width = query.shape
    half = width // 2
    queries = query.reshape(plen, groups, 2, half)
    keys = keyval[..., :half]
    values = keyval[..., half:]
    score = jnp.einsum("qkgd,tkd->kgqt", queries, keys, preferred_element_type=jnp.float32) * 0.125
    allowed = (query_seg[:, None] == seg[None, :]) & (where_at[None, :] <= query_at[:, None])
    score = jnp.where(allowed[None, None], score, -1e30)
    top = jnp.max(score, axis=-1, keepdims=True)
    expo = jnp.exp(score - top)
    probs = (expo / jnp.sum(expo, axis=-1, keepdims=True)).astype(jnp.bfloat16)
    out = jnp.einsum("kgqt,tkd->qkgd", probs, values, preferred_element_type=jnp.float32)
    return out.astype(jnp.bfloat16).reshape(plen, groups * width)


def routing(normed2, ids, w_router):
    experts = w_router.shape[1]
    logits = jnp.dot(normed2, w_router, preferred_element_type=jnp.float32)
    match = ids[:, :, None] == jnp.arange(experts, dtype=jnp.int32)
    chosen = jnp.sum(jnp.where(match, logits[:, None, :], 0.0), axis=2)
    weights = jax.nn.softmax(chosen, axis=-1)
    dense = jnp.sum(jnp.where(match, weights[:, :, None], 0.0), axis=1)
    high = dense.astype(jnp.bfloat16)
    low = (dense - high.astype(jnp.float32)).astype(jnp.bfloat16)
    named = jnp.any(match, axis=1).astype(jnp.bfloat16)
    pad = (-3 * experts) % 128
    fill = jnp.zeros((normed2.shape[0], pad), jnp.bfloat16)
    return jnp.concatenate([normed2, high, low, named, fill], axis=1)


def expert_mix(packed, sources, width, experts, w_gate, w_up, w_down, pieces):
    local = w_gate.shape[0]
    rows = packed.shape[0] // sources
    here = lax.axis_index("exp")
    rows_all = packed[:, :width].reshape(sources, rows, width)

    def columns(block):
        start = width + block * experts + here * local
        return lax.dynamic_slice_in_dim(packed, start, local, 1).reshape(sources, rows, local)

    high, low, named = columns(0), columns(1), columns(2)
    order = jnp.arange(rows, dtype=jnp.int32)
    before = (order[None, :] < order[:, None]).astype(jnp.bfloat16)
    slot = jnp.einsum("tu,bue->bet", before, named, preferred_element_type=jnp.float32)
    hits = jnp.transpose(named, (0, 2, 1)) > 0
    picks = hits[:, :, None, :] & (
        slot.astype(jnp.int32)[:, :, None, :] == jnp.arange(CAP, dtype=jnp.int32)[None, None, :, None]
    )
    received = jnp.einsum(
        "becr,brd->becd", picks.astype(jnp.bfloat16), rows_all, preferred_element_type=jnp.float32
    ).astype(jnp.bfloat16)
    gate = jnp.einsum("becd,edf->becf", received, w_gate, preferred_element_type=jnp.float32)
    upward = jnp.einsum("becd,edf->becf", received, w_up, preferred_element_type=jnp.float32)
    hidden = (jax.nn.silu(gate) * upward).astype(jnp.bfloat16)
    zero = jnp.zeros((), jnp.bfloat16)
    high = jnp.where(picks, jnp.transpose(high, (0, 2, 1))[:, :, None, :], zero)
    low = jnp.where(picks, jnp.transpose(low, (0, 2, 1))[:, :, None, :], zero)
    cut = w_down.shape[2] // pieces
    outs = []
    for piece in range(pieces):
        down = lax.slice_in_dim(w_down, piece * cut, (piece + 1) * cut, axis=2)
        result = jnp.einsum("becf,efd->becd", hidden, down, preferred_element_type=jnp.float32)
        result = result.astype(jnp.bfloat16)
        partial = jnp.einsum("becr,becd->brd", high, result, preferred_element_type=jnp.float32)
        partial = partial + jnp.einsum(
            "becr,becd->brd", low, result, preferred_element_type=jnp.float32
        )
        outs.append(partial)
    return outs


def shifted(x, step):
    count = lax.axis_size("exp")
    return lax.ppermute(x, "exp", [(j, (j + step) % count) for j in range(count)])


def exchange_sum(blocks):
    total = blocks[0].astype(jnp.float32)
    for step in range(1, blocks.shape[0]):
        total = total + shifted(blocks[step], -step).astype(jnp.float32)
    return total


def step_rows(x, rows):
    count = lax.axis_size("exp")
    here = lax.axis_index("exp")
    parts = [
        lax.dynamic_slice_in_dim(x, (here - step) % count * rows, rows) for step in range(count)
    ]
    return jnp.concatenate(parts)


def gather_w_out(w_out):
    count = lax.axis_size("exp")
    mates = lax.axis_size("req")
    part = lax.axis_index("req") % 2
    cut = w_out.shape[0] // 2
    mine = lax.dynamic_slice_in_dim(w_out, part * cut, cut, 0)
    got = jnp.stack([shifted(mine, step) for step in range(1, count)])
    other = lax.ppermute(got, "req", [(j, j ^ 1) for j in range(mates)])
    lower = jnp.where(part == 0, got, other)
    upper = jnp.where(part == 0, other, got)
    return jnp.concatenate([lower, upper], axis=1)


def shards(
    tokens,
    norm_attn,
    w_query,
    w_key,
    w_value,
    w_out,
    norm_moe,
    w_router,
    w_gate,
    w_up,
    w_down,
    segment_ids,
    page_order,
    expert_ids,
):
    rows, width = tokens.shape
    seg = segment_ids[0]
    groups = w_key.shape[1] // HD
    here = lax.axis_index("exp")
    pos = lax.dynamic_slice_in_dim(positions(seg), here * rows, rows)
    normed = rms_scale(tokens, norm_attn)
    query = jnp.dot(normed, w_query, preferred_element_type=jnp.float32).reshape(
        rows, 2 * groups, HD
    )
    query = rotate(query, pos).astype(jnp.bfloat16).reshape(rows, groups, 2 * HD)
    keys = jnp.dot(normed, w_key, preferred_element_type=jnp.float32).reshape(rows, groups, HD)
    keys = rotate(keys, pos).astype(jnp.bfloat16)
    values = (
        jnp.dot(normed, w_value, preferred_element_type=jnp.float32)
        .astype(jnp.bfloat16)
        .reshape(rows, groups, HD)
    )
    keyval = jnp.concatenate([keys, values], axis=-1)
    owners = lax.axis_size("exp")
    share = groups // owners
    both = jnp.concatenate([query, keyval], axis=-1)
    parts = [lax.dynamic_slice_in_dim(both, here * share, share, 1)]
    for step in range(1, owners):
        send = lax.dynamic_slice_in_dim(both, (here + step) % owners * share, share, 1)
        parts.append(shifted(send, step))
    both = jnp.concatenate(parts)
    query_heads, keyval_heads = both[..., : 2 * HD], both[..., 2 * HD :]
    plen = keyval_heads.shape[0]
    where_at = step_rows(jnp.arange(plen, dtype=jnp.int32), rows)
    placing = step_rows(page_order[0], rows)[None, :] == jnp.arange(plen, dtype=jnp.int32)[:, None]
    kv_cache = jnp.einsum(
        "rs,skd->rkd", placing.astype(jnp.bfloat16), keyval_heads, preferred_element_type=jnp.float32
    ).astype(jnp.bfloat16)
    seg_rows = step_rows(seg, rows)
    heads_out = attend(query_heads, keyval_heads, seg_rows, seg_rows, where_at, where_at)
    blocks = heads_out.reshape(owners, rows, -1)
    remote = gather_w_out(w_out)
    attention = jnp.dot(blocks[0], w_out, preferred_element_type=jnp.float32)
    for step in range(1, owners):
        got = shifted(blocks[step], -step)
        attention = attention + jnp.dot(
            got, remote[owners - step - 1], preferred_element_type=jnp.float32
        )
    resid = tokens.astype(jnp.float32) + attention
    normed2 = rms_scale(resid, norm_moe)
    packed = routing(normed2, expert_ids, w_router)
    experts = w_router.shape[1]
    moe = expert_mix(packed, 1, width, experts, w_gate, w_up, w_down, 1)[0][0]
    received = jnp.concatenate([shifted(packed, step) for step in range(1, owners)])
    pieces = expert_mix(received, owners - 1, width, experts, w_gate, w_up, w_down, 4)
    backs = []
    for piece in pieces:
        piece = piece.astype(jnp.bfloat16)
        back = sum(
            shifted(piece[step - 1], -step).astype(jnp.float32) for step in range(1, owners)
        )
        backs.append(back)
    moe = moe + jnp.concatenate(backs, axis=1)
    mixed = (resid + moe).astype(jnp.bfloat16)
    return (mixed, kv_cache)


def solution(mesh):
    placed = (
        P(("req", "exp"), None),
        P(),
        P(),
        P(),
        P(),
        P("exp", None),
        P(),
        P(),
        P("exp", None, None),
        P("exp", None, None),
        P("exp", None, None),
        P("req", None),
        P("req", None),
        P(("req", "exp"), None),
    )
    return jax.shard_map(
        shards,
        mesh=mesh,
        in_specs=placed,
        out_specs=(P(("req", "exp"), None), P("req", "exp", None)),
        check_vma=False,
    )
```

```python
import jax
import jax.numpy as jnp
from jax import lax
from jax.sharding import PartitionSpec as P

HD = 64
CAP = 64


def rms_scale(rows, gain):
    rows = rows.astype(jnp.float32)
    inverse = lax.rsqrt(jnp.mean(rows * rows, axis=-1, keepdims=True) + 1e-06)
    return (rows * inverse * gain.astype(jnp.float32)).astype(jnp.bfloat16)


def positions(seg):
    index = jnp.arange(seg.shape[0], dtype=jnp.int32)
    starts = jnp.concatenate([jnp.ones((1,), dtype=bool), seg[1:] != seg[:-1]])
    first = lax.cummax(jnp.where(starts, index, 0), axis=0)
    return index - first


def rotate(values, pos):
    half = values.shape[-1] // 2
    freq = 10000.0 ** (-jnp.arange(half, dtype=jnp.float32) / half)
    angle = pos.astype(jnp.float32)[:, None] * freq[None, :]
    cosine = jnp.cos(angle)[:, None, :]
    sine = jnp.sin(angle)[:, None, :]
    front = values[..., :half]
    back = values[..., half:]
    return jnp.concatenate([front * cosine - back * sine, back * cosine + front * sine], axis=-1)


def attend(query, keyval, query_seg, seg, query_at, where_at):
    plen, groups, width = query.shape
    half = width // 2
    queries = query.reshape(plen, groups, 2, half)
    keys = keyval[..., :half]
    values = keyval[..., half:]
    score = jnp.einsum("qkgd,tkd->kgqt", queries, keys, preferred_element_type=jnp.float32) * 0.125
    allowed = (query_seg[:, None] == seg[None, :]) & (where_at[None, :] <= query_at[:, None])
    score = jnp.where(allowed[None, None], score, -1e30)
    top = jnp.max(score, axis=-1, keepdims=True)
    expo = jnp.exp(score - top)
    probs = (expo / jnp.sum(expo, axis=-1, keepdims=True)).astype(jnp.bfloat16)
    out = jnp.einsum("kgqt,tkd->qkgd", probs, values, preferred_element_type=jnp.float32)
    return out.astype(jnp.bfloat16).reshape(plen, groups * width)


def routing(normed2, ids, w_router):
    experts = w_router.shape[1]
    logits = jnp.dot(normed2, w_router, preferred_element_type=jnp.float32)
    match = ids[:, :, None] == jnp.arange(experts, dtype=jnp.int32)
    chosen = jnp.sum(jnp.where(match, logits[:, None, :], 0.0), axis=2)
    weights = jax.nn.softmax(chosen, axis=-1)
    dense = jnp.sum(jnp.where(match, weights[:, :, None], 0.0), axis=1)
    high = dense.astype(jnp.bfloat16)
    low = (dense - high.astype(jnp.float32)).astype(jnp.bfloat16)
    named = jnp.any(match, axis=1).astype(jnp.bfloat16)
    pad = (-3 * experts) % 128
    fill = jnp.zeros((normed2.shape[0], pad), jnp.bfloat16)
    return jnp.concatenate([normed2, high, low, named, fill], axis=1)


def expert_mix(packed, sources, width, experts, w_gate, w_up, w_down, pieces):
    local = w_gate.shape[0]
    rows = packed.shape[0] // sources
    here = lax.axis_index("exp")
    rows_all = packed[:, :width].reshape(sources, rows, width)

    def columns(block):
        start = width + block * experts + here * local
        return lax.dynamic_slice_in_dim(packed, start, local, 1).reshape(sources, rows, local)

    high, low, named = columns(0), columns(1), columns(2)
    order = jnp.arange(rows, dtype=jnp.int32)
    before = (order[None, :] < order[:, None]).astype(jnp.bfloat16)
    slot = jnp.einsum("tu,bue->bet", before, named, preferred_element_type=jnp.float32)
    hits = jnp.transpose(named, (0, 2, 1)) > 0
    picks = hits[:, :, None, :] & (
        slot.astype(jnp.int32)[:, :, None, :] == jnp.arange(CAP, dtype=jnp.int32)[None, None, :, None]
    )
    received = jnp.einsum(
        "becr,brd->becd", picks.astype(jnp.bfloat16), rows_all, preferred_element_type=jnp.float32
    ).astype(jnp.bfloat16)
    gate = jnp.einsum("becd,edf->becf", received, w_gate, preferred_element_type=jnp.float32)
    upward = jnp.einsum("becd,edf->becf", received, w_up, preferred_element_type=jnp.float32)
    hidden = (jax.nn.silu(gate) * upward).astype(jnp.bfloat16)
    zero = jnp.zeros((), jnp.bfloat16)
    high = jnp.where(picks, jnp.transpose(high, (0, 2, 1))[:, :, None, :], zero)
    low = jnp.where(picks, jnp.transpose(low, (0, 2, 1))[:, :, None, :], zero)
    cut = w_down.shape[2] // pieces
    outs = []
    for piece in range(pieces):
        down = lax.slice_in_dim(w_down, piece * cut, (piece + 1) * cut, axis=2)
        result = jnp.einsum("becf,efd->becd", hidden, down, preferred_element_type=jnp.float32)
        result = result.astype(jnp.bfloat16)
        partial = jnp.einsum("becr,becd->brd", high, result, preferred_element_type=jnp.float32)
        if pieces == 1:
            partial = partial + jnp.einsum(
                "becr,becd->brd", low, result, preferred_element_type=jnp.float32
            )
        outs.append(partial)
    return outs


def shifted(x, step):
    count = lax.axis_size("exp")
    return lax.ppermute(x, "exp", [(j, (j + step) % count) for j in range(count)])


def exchange_sum(blocks):
    total = blocks[0].astype(jnp.float32)
    for step in range(1, blocks.shape[0]):
        total = total + shifted(blocks[step], -step).astype(jnp.float32)
    return total


def step_rows(x, rows):
    count = lax.axis_size("exp")
    here = lax.axis_index("exp")
    parts = [
        lax.dynamic_slice_in_dim(x, (here - step) % count * rows, rows) for step in range(count)
    ]
    return jnp.concatenate(parts)


def gather_w_out(w_out):
    count = lax.axis_size("exp")
    mates = lax.axis_size("req")
    part = lax.axis_index("req") % 2
    cut = w_out.shape[0] // 2
    mine = lax.dynamic_slice_in_dim(w_out, part * cut, cut, 0)
    got = jnp.stack([shifted(mine, step) for step in range(1, count)])
    other = lax.ppermute(got, "req", [(j, j ^ 1) for j in range(mates)])
    lower = jnp.where(part == 0, got, other)
    upper = jnp.where(part == 0, other, got)
    return jnp.concatenate([lower, upper], axis=1)


def shards(
    tokens,
    norm_attn,
    w_query,
    w_key,
    w_value,
    w_out,
    norm_moe,
    w_router,
    w_gate,
    w_up,
    w_down,
    segment_ids,
    page_order,
    expert_ids,
):
    rows, width = tokens.shape
    seg = segment_ids[0]
    groups = w_key.shape[1] // HD
    here = lax.axis_index("exp")
    pos = lax.dynamic_slice_in_dim(positions(seg), here * rows, rows)
    normed = rms_scale(tokens, norm_attn)
    query = jnp.dot(normed, w_query, preferred_element_type=jnp.float32).reshape(
        rows, 2 * groups, HD
    )
    query = rotate(query, pos).astype(jnp.bfloat16).reshape(rows, groups, 2 * HD)
    keys = jnp.dot(normed, w_key, preferred_element_type=jnp.float32).reshape(rows, groups, HD)
    keys = rotate(keys, pos).astype(jnp.bfloat16)
    values = (
        jnp.dot(normed, w_value, preferred_element_type=jnp.float32)
        .astype(jnp.bfloat16)
        .reshape(rows, groups, HD)
    )
    keyval = jnp.concatenate([keys, values], axis=-1)
    owners = lax.axis_size("exp")
    share = groups // owners
    both = jnp.concatenate([query, keyval], axis=-1)
    parts = [lax.dynamic_slice_in_dim(both, here * share, share, 1)]
    for step in range(1, owners):
        send = lax.dynamic_slice_in_dim(both, (here + step) % owners * share, share, 1)
        parts.append(shifted(send, step))
    both = jnp.concatenate(parts)
    query_heads, keyval_heads = both[..., : 2 * HD], both[..., 2 * HD :]
    plen = keyval_heads.shape[0]
    where_at = step_rows(jnp.arange(plen, dtype=jnp.int32), rows)
    placing = step_rows(page_order[0], rows)[None, :] == jnp.arange(plen, dtype=jnp.int32)[:, None]
    kv_cache = jnp.einsum(
        "rs,skd->rkd", placing.astype(jnp.bfloat16), keyval_heads, preferred_element_type=jnp.float32
    ).astype(jnp.bfloat16)
    seg_rows = step_rows(seg, rows)
    heads_out = attend(query_heads, keyval_heads, seg_rows, seg_rows, where_at, where_at)
    blocks = heads_out.reshape(owners, rows, -1)
    remote = gather_w_out(w_out)
    attention = jnp.dot(blocks[0], w_out, preferred_element_type=jnp.float32)
    for step in range(1, owners):
        got = shifted(blocks[step], -step)
        attention = attention + jnp.dot(
            got, remote[owners - step - 1], preferred_element_type=jnp.float32
        )
    resid = tokens.astype(jnp.float32) + attention
    normed2 = rms_scale(resid, norm_moe)
    packed = routing(normed2, expert_ids, w_router)
    experts = w_router.shape[1]
    moe = expert_mix(packed, 1, width, experts, w_gate, w_up, w_down, 1)[0][0]
    received = jnp.concatenate([shifted(packed, step) for step in range(1, owners)])
    pieces = expert_mix(received, owners - 1, width, experts, w_gate, w_up, w_down, 2)
    backs = []
    for piece in pieces:
        piece = piece.astype(jnp.bfloat16)
        back = sum(
            shifted(piece[step - 1], -step).astype(jnp.float32) for step in range(1, owners)
        )
        backs.append(back)
    moe = moe + jnp.concatenate(backs, axis=1)
    mixed = (resid + moe).astype(jnp.bfloat16)
    return (mixed, kv_cache)


def solution(mesh):
    placed = (
        P(("req", "exp"), None),
        P(),
        P(),
        P(),
        P(),
        P("exp", None),
        P(),
        P(),
        P("exp", None, None),
        P("exp", None, None),
        P("exp", None, None),
        P("req", None),
        P("req", None),
        P(("req", "exp"), None),
    )
    return jax.shard_map(
        shards,
        mesh=mesh,
        in_specs=placed,
        out_specs=(P(("req", "exp"), None), P("req", "exp", None)),
        check_vma=False,
    )
```
